32 devices in a mesh: groups: 2 (over y), dp: 4 (over x, core), head: 4 (over z).
Axes of the slice: x: 2, y: 2, z: 4, core: 2. Of those that a mesh axis runs over, the one named last changes fastest.
Arguments:
- activations: bfloat16 [64, 4, 2048], P(('groups', 'head'), None, 'dp'), parts along dimension 0, may hold values from -6 to 6
- w_qk: bfloat16 [2048, 4096], P('dp', 'head'), may hold values from -0.125 to 0.125
- w_vz: bfloat16 [2048, 8192], P('dp', 'head'), may hold values from -0.125 to 0.125
- w_ba: bfloat16 [2048, 64], P('dp', 'head'), may hold values from -0.125 to 0.125
- conv_qk: bfloat16 [4, 4096], P(None, 'head'), may hold values from -3 to 3
- conv_v: bfloat16 [4, 4096], P(None, 'head'), may hold values from -3 to 3
- a_log: float32 [32], P('head'), may hold values from -1.5 to 1.5
- dt_bias: float32 [32], P('head'), may hold values from -2 to 1
- norm_gain: float32 [128], replicated, may hold values from 0.1 to 1.9
- w_out: bfloat16 [4096, 2048], P('head', 'dp'), may hold values from -0.09375 to 0.09375
- conv_state_qk: bfloat16 [64, 3, 4096], P(('groups', 'dp'), None, 'head'), parts along dimension 0, may hold values from -6 to 6
- conv_state_v: bfloat16 [64, 3, 4096], P(('groups', 'dp'), None, 'head'), parts along dimension 0, may hold values from -6 to 6
- memory_state: float32 [64, 32, 128, 128], P(('groups', 'dp'), 'head'), parts along dimension 0, may hold values from -4 to 4
Outputs:
- layer_out: bfloat16 [64, 4, 2048], P(('groups', 'head'), None, 'dp'), parts along dimension 0
- new_state: float32 [64, 32, 128, 128], P(('groups', 'dp'), 'head'), parts along dimension 0
The draws below stay inside these ranges and needn't reach their ends.
There are 2 independent parts, one for each index of `groups`. The reference program is written for one: setup_inputs(seed, part) draws one part's arguments, and reference() takes and returns one part's arrays. A program takes and returns all parts, laid end to end along the dimension named above; an argument that names none is the same for every part. Nothing has to cross between parts.
All inputs are finite; a program needn't handle non-finite values.
Results may differ from the reference program's by a relative error of at most 0.0069.
Values may be sent and summed in bfloat16 or wider, within the bound.
No kernel may reach another device: no remote copies, remote signals or barrier semaphores. Data moves between devices by JAX's collectives and lax.ppermute only.
A program may use at most 64 MiB of HBM per device.

```python
import jax
import jax.numpy as jnp
from jax import lax

D = 2048
HK = 16
HV = 32
DK = 128
DV = 128
KERNEL = 4
STEPS = 4
ROWS = 32
QK = 4096
VZ = 8192
BA = 64


def steps_of(stream_key, shape, shards, smallest, high):
    gain, own = 1.0, jax.random.fold_in(stream_key, 6)
    for dim, parts in shards:
        draws = jnp.exp(jax.random.uniform(jax.random.fold_in(own, dim), (parts,), jnp.float32, smallest / len(shards), high / len(shards)))
        gain = gain * jnp.repeat(draws, shape[dim] // parts).reshape([-1 if axis == dim else 1 for axis in range(len(shape))])
    return gain


def bell_draw(key, shape, width, most, cuts=(), dtype=jnp.bfloat16):
    gain = steps_of(key, shape, cuts, -0.22, 0.18) if cuts else 1.0
    entries = jax.random.normal(key, shape, jnp.float32) * width * gain
    return jnp.minimum(jnp.maximum(entries, -most), most).astype(dtype)


def setup_inputs(seed: int = 0, part: int = 0) -> dict:
    key_of = jax.random.split(jax.random.key(seed), 14)
    own_keys = jax.random.split(jax.random.fold_in(key_of[13], part), 14)
    activations = bell_draw(own_keys[0], (ROWS, STEPS, D), 1.0, 6.0, ((0, 4), (2, 4)))
    w_qk = bell_draw(key_of[1], (D, QK), D ** -0.5, 0.125, ((0, 4), (1, 4)))
    w_vz = bell_draw(key_of[2], (D, VZ), D ** -0.5, 0.125, ((0, 4), (1, 4)))
    w_ba = bell_draw(key_of[3], (D, BA), D ** -0.5, 0.125, ((0, 4), (1, 4)))
    conv_qk = bell_draw(key_of[4], (KERNEL, QK), 0.5, 3.0, ((1, 4),))
    conv_v = bell_draw(key_of[5], (KERNEL, HV * DV), 0.5, 3.0, ((1, 4),))
    a_log = jnp.clip(jax.random.uniform(key_of[6], (HV,), jnp.float32, -1.5, 1.5) * steps_of(key_of[6], (HV,), ((0, 4),), -0.4, 0.0), -1.5, 1.5)
    dt_bias = jnp.clip(-2.0 + 3.0 * jax.random.uniform(key_of[7], (HV,), jnp.float32) ** steps_of(key_of[7], (HV,), ((0, 4),), -0.2, 0.2), -2.0, 1.0)
    norm_gain = jnp.clip(1.0 + 0.18 * jax.random.normal(key_of[8], (DV,), jnp.float32), 0.1, 1.9)
    w_out = bell_draw(key_of[9], (HV * DV, D), (HV * DV) ** -0.5, 0.09375, ((0, 4), (1, 4)))
    conv_state_qk = bell_draw(own_keys[10], (ROWS, KERNEL - 1, QK), 1.0, 6.0, ((0, 4), (2, 4)))
    conv_state_v = bell_draw(own_keys[11], (ROWS, KERNEL - 1, HV * DV), 1.0, 6.0, ((0, 4), (2, 4)))
    memory_state = bell_draw(own_keys[12], (ROWS, HV, DK, DV), 0.5, 4.0, ((0, 4), (1, 4)), jnp.float32)
    return dict(activations=activations, w_qk=w_qk, w_vz=w_vz, w_ba=w_ba, conv_qk=conv_qk, conv_v=conv_v, a_log=a_log, dt_bias=dt_bias, norm_gain=norm_gain, w_out=w_out, conv_state_qk=conv_state_qk, conv_state_v=conv_state_v, memory_state=memory_state)


def conv_apply(window, taps):
    mixed = lax.optimization_barrier(jnp.sum(window.astype(jnp.float32) * taps.astype(jnp.float32)[None], axis=1))
    return jax.nn.silu(mixed)

def normalize(vectors):
    return vectors * lax.rsqrt(lax.optimization_barrier(jnp.sum(vectors * vectors, axis=-1, keepdims=True)) + 1e-06)

def prepare(qk_proj, vz_proj, ba_proj, conv_qk, conv_v, a_log, dt_bias, conv_state_qk, conv_state_v, head_ratio):
    row_count = qk_proj.shape[0]
    window_qk = jnp.concatenate([conv_state_qk, qk_proj[:, None, :]], axis=1)
    split_vz = vz_proj.reshape(row_count, -1, 2, DV)
    values_now = split_vz[:, :, 0, :].reshape(row_count, -1)
    gate_z = split_vz[:, :, 1, :].astype(jnp.float32)
    window_v = jnp.concatenate([conv_state_v, values_now[:, None, :]], axis=1)
    qk_conv = conv_apply(window_qk, conv_qk).reshape(row_count, -1, 2, DK)
    v_conv = conv_apply(window_v, conv_v).reshape(row_count, -1, DV)
    queries = normalize(qk_conv[:, :, 0, :]) * DK ** (-0.5)
    key_vec = normalize(qk_conv[:, :, 1, :])
    queries = jnp.repeat(queries, head_ratio, axis=1)
    key_vec = jnp.repeat(key_vec, head_ratio, axis=1)
    split_ba = ba_proj.reshape(row_count, -1, 2).astype(jnp.float32)
    beta_gate = jax.nn.sigmoid(split_ba[:, :, 0])
    log_decay = -jnp.exp(a_log)[None, :] * jax.nn.softplus(split_ba[:, :, 1] + dt_bias[None, :])
    return (queries, key_vec, v_conv, gate_z, beta_gate, log_decay, window_qk[:, 1:], window_v[:, 1:])

def recurrent(queries, key_vec, values, beta_gate, log_decay, memory_state):
    memory_state = memory_state * jnp.exp(log_decay)[:, :, None, None]
    recalled = lax.optimization_barrier(jnp.sum(key_vec[:, :, :, None] * memory_state, axis=2))
    correction = (values - recalled) * beta_gate[:, :, None]
    memory_state = memory_state + key_vec[:, :, :, None] * correction[:, :, None, :]
    readout = lax.optimization_barrier(jnp.sum(queries[:, :, :, None] * memory_state, axis=2))
    return (memory_state, readout)

def finish(readout, gate_z, norm_gain):
    scale = lax.rsqrt(lax.optimization_barrier(jnp.mean(readout * readout, axis=-1, keepdims=True)) + 1e-06)
    normed = readout * scale * norm_gain[None, None, :] * jax.nn.silu(gate_z)
    return normed.reshape(readout.shape[0], -1).astype(jnp.bfloat16)

def reference(activations, w_qk, w_vz, w_ba, conv_qk, conv_v, a_log, dt_bias, norm_gain, w_out, conv_state_qk, conv_state_v, memory_state):
    head_ratio = HV // HK
    outputs = []
    for step_index in range(STEPS):
        step_input = activations[:, step_index, :]
        qk_proj = jnp.dot(step_input, w_qk, preferred_element_type=jnp.float32).astype(jnp.bfloat16)
        vz_proj = jnp.dot(step_input, w_vz, preferred_element_type=jnp.float32).astype(jnp.bfloat16)
        ba_proj = jnp.dot(step_input, w_ba, preferred_element_type=jnp.float32).astype(jnp.bfloat16)
        queries, key_vec, values, gate_z, beta_gate, log_decay, conv_state_qk, conv_state_v = prepare(qk_proj, vz_proj, ba_proj, conv_qk, conv_v, a_log, dt_bias, conv_state_qk, conv_state_v, head_ratio)
        memory_state, readout = recurrent(queries, key_vec, values, beta_gate, log_decay, memory_state)
        normed = finish(readout, gate_z, norm_gain)
        outputs.append(jnp.dot(normed, w_out, preferred_element_type=jnp.float32).astype(jnp.bfloat16))
    return (jnp.stack(outputs, axis=1), memory_state)
```

```python
import functools

import jax
import jax.numpy as jnp
from jax import lax
from jax.experimental import pallas as pl
from jax.experimental.pallas import tpu as pltpu
from jax.sharding import PartitionSpec as P

HK = 16
HV = 32
DK = 128
DV = 128


def normalize(vectors):
    return vectors * lax.rsqrt(jnp.sum(vectors * vectors, axis=-1, keepdims=True) + 1e-06)


def conv_steps(state, proj, taps):
    seq = jnp.concatenate([state, proj], axis=1).astype(jnp.float32)
    taps = taps.astype(jnp.float32)
    kernel = taps.shape[0]
    steps = proj.shape[1]
    mixed = sum(seq[:, k : k + steps, :] * taps[k][None, None, :] for k in range(kernel))
    return jax.nn.silu(mixed)


def recurrence_kernel(decay_ref, beta_ref, qt_ref, kt_ref, v_ref, s_ref, s_out, o_ref, *, heads, steps):
    r = pl.program_id(0)
    for h in range(heads):
        state = s_ref[0, h]
        for t in range(steps):
            c = t * heads + h
            key_col = kt_ref[0, :, c : c + 1]
            query_col = qt_ref[0, :, c : c + 1]
            state = state * decay_ref[r, c]
            recalled = jnp.sum(key_col * state, axis=0, keepdims=True)
            correction = (v_ref[0, c : c + 1, :] - recalled) * beta_ref[r, c]
            state = state + key_col * correction
            o_ref[0, c : c + 1, :] = jnp.sum(query_col * state, axis=0, keepdims=True)
        s_out[0, h] = state


def recurrence(decay, beta, qt, kt, values, memory_state):
    rows, heads = memory_state.shape[0], memory_state.shape[1]
    cols = decay.shape[1]
    steps = cols // heads
    kern = functools.partial(recurrence_kernel, heads=heads, steps=steps)
    return pl.pallas_call(
        kern,
        grid=(rows,),
        in_specs=[
            pl.BlockSpec(memory_space=pltpu.SMEM),
            pl.BlockSpec(memory_space=pltpu.SMEM),
            pl.BlockSpec((1, DK, cols), lambda r: (r, 0, 0)),
            pl.BlockSpec((1, DK, cols), lambda r: (r, 0, 0)),
            pl.BlockSpec((1, cols, DV), lambda r: (r, 0, 0)),
            pl.BlockSpec((1, heads, DK, DV), lambda r: (r, 0, 0, 0)),
        ],
        out_specs=[
            pl.BlockSpec((1, heads, DK, DV), lambda r: (r, 0, 0, 0)),
            pl.BlockSpec((1, cols, DV), lambda r: (r, 0, 0)),
        ],
        out_shape=[
            jax.ShapeDtypeStruct(memory_state.shape, jnp.float32),
            jax.ShapeDtypeStruct((rows, cols, DV), jnp.float32),
        ],
        cost_estimate=pl.CostEstimate(
            flops=8 * rows * cols * DK * DV,
            bytes_accessed=2 * memory_state.size * 4,
            transcendentals=0,
        ),
    )(decay, beta, qt, kt, values, memory_state)


def shards(
    activations,
    w_qk,
    w_vz,
    w_ba,
    conv_qk,
    conv_v,
    a_log,
    dt_bias,
    norm_gain,
    w_out,
    conv_state_qk,
    conv_state_v,
    memory_state,
):
    head_ratio = HV // HK
    step_count = activations.shape[1]
    rows_mem = memory_state.shape[0]
    heads = memory_state.shape[1]
    width_qk = w_qk.shape[1]
    width_vz = w_vz.shape[1]

    step_rows = lax.all_gather(activations, "head", axis=0, tiled=True)
    flat_rows = step_rows.reshape(-1, step_rows.shape[-1])
    partial_qk = jnp.dot(flat_rows, w_qk, preferred_element_type=jnp.float32)
    partial_vz = jnp.dot(flat_rows, w_vz, preferred_element_type=jnp.float32)
    partial_ba = jnp.dot(flat_rows, w_ba, preferred_element_type=jnp.float32)
    summed = lax.psum_scatter(
        jnp.concatenate([partial_qk, partial_vz, partial_ba], axis=1),
        "dp",
        scatter_dimension=0,
        tiled=True,
    )
    summed_qk = summed[:, :width_qk]
    summed_vz = summed[:, width_qk : width_qk + width_vz]
    summed_ba = summed[:, width_qk + width_vz :]
    qk_proj = summed_qk.astype(jnp.bfloat16).reshape(rows_mem, step_count, width_qk)
    vz_proj = summed_vz.astype(jnp.bfloat16).reshape(rows_mem, step_count, width_vz)
    ba_proj = summed_ba.astype(jnp.bfloat16).reshape(rows_mem, step_count, -1)

    split_vz = vz_proj.reshape(rows_mem, step_count, heads, 2, DV)
    values_now = split_vz[:, :, :, 0, :].reshape(rows_mem, step_count, heads * DV)
    gate_z = split_vz[:, :, :, 1, :].astype(jnp.float32)

    qk_conv = conv_steps(conv_state_qk, qk_proj, conv_qk).reshape(rows_mem, step_count, -1, 2, DK)
    v_conv = conv_steps(conv_state_v, values_now, conv_v).reshape(rows_mem, step_count * heads, DV)
    queries = normalize(qk_conv[:, :, :, 0, :]) * DK ** (-0.5)
    key_vec = normalize(qk_conv[:, :, :, 1, :])
    queries = jnp.repeat(queries, head_ratio, axis=2)
    key_vec = jnp.repeat(key_vec, head_ratio, axis=2)
    qt = queries.transpose(0, 3, 1, 2).reshape(rows_mem, DK, step_count * heads)
    kt = key_vec.transpose(0, 3, 1, 2).reshape(rows_mem, DK, step_count * heads)

    split_ba = ba_proj.reshape(rows_mem, step_count, heads, 2).astype(jnp.float32)
    beta_gate = jax.nn.sigmoid(split_ba[..., 0])
    log_decay = -jnp.exp(a_log)[None, None, :] * jax.nn.softplus(split_ba[..., 1] + dt_bias[None, None, :])
    decay = jnp.exp(log_decay).reshape(rows_mem, step_count * heads)
    beta_gate = beta_gate.reshape(rows_mem, step_count * heads)

    new_state, readout = recurrence(decay, beta_gate, qt, kt, v_conv, memory_state)
    readout = readout.reshape(rows_mem, step_count, heads, DV)

    scale = lax.rsqrt(jnp.mean(readout * readout, axis=-1, keepdims=True) + 1e-06)
    normed = readout * scale * norm_gain[None, None, None, :] * jax.nn.silu(gate_z)
    normed = normed.reshape(rows_mem, step_count, heads * DV).astype(jnp.bfloat16)

    all_normed = lax.all_gather(normed, "dp", axis=0, tiled=True)
    partials = jnp.dot(
        all_normed.reshape(-1, all_normed.shape[-1]), w_out, preferred_element_type=jnp.float32
    )
    layer_out = lax.psum_scatter(partials, "head", scatter_dimension=0, tiled=True)
    layer_out = layer_out.astype(jnp.bfloat16).reshape(-1, step_count, w_out.shape[1])
    return (layer_out, new_state)


def solution(mesh):
    in_specs = (
        P(("groups", "head"), None, "dp"),
        P("dp", "head"),
        P("dp", "head"),
        P("dp", "head"),
        P(None, "head"),
        P(None, "head"),
        P("head"),
        P("head"),
        P(),
        P("head", "dp"),
        P(("groups", "dp"), None, "head"),
        P(("groups", "dp"), None, "head"),
        P(("groups", "dp"), "head", None, None),
    )
    out_specs = (P(("groups", "head"), None, "dp"), P(("groups", "dp"), "head", None, None))
    return jax.shard_map(shards, mesh=mesh, in_specs=in_specs, out_specs=out_specs, check_vma=False)
```

```python
import functools

import jax
import jax.numpy as jnp
from jax import lax
from jax.experimental import pallas as pl
from jax.experimental.pallas import tpu as pltpu
from jax.sharding import PartitionSpec as P

HK = 16
HV = 32
DK = 128
DV = 128


def normalize(vectors):
    return vectors * lax.rsqrt(jnp.sum(vectors * vectors, axis=-1, keepdims=True) + 1e-06)


def conv_steps(state, proj, taps):
    seq = jnp.concatenate([state, proj], axis=1).astype(jnp.float32)
    taps = taps.astype(jnp.float32)
    kernel = taps.shape[0]
    steps = proj.shape[1]
    mixed = sum(seq[:, k : k + steps, :] * taps[k][None, None, :] for k in range(kernel))
    return jax.nn.silu(mixed)


def gather_rows(x, axis):
    n = lax.axis_size(axis)
    me = lax.axis_index(axis)
    pieces = [x]
    for s in range(1, n):
        pieces.append(lax.ppermute(x, axis, [(i, (i + s) % n) for i in range(n)]))
    stacked = jnp.stack(pieces)
    source = (me - jnp.arange(n)) % n
    order = jnp.argsort(source)
    return jnp.take(stacked, order, axis=0).reshape(n * x.shape[0], *x.shape[1:])


def scatter_sum_rows(x, axis):
    n = lax.axis_size(axis)
    me = lax.axis_index(axis)
    chunks = x.reshape(n, x.shape[0] // n, *x.shape[1:])
    acc = jnp.take(chunks, me, axis=0)
    for s in range(1, n):
        send = jnp.take(chunks, (me + s) % n, axis=0)
        acc = acc + lax.ppermute(send, axis, [(i, (i + s) % n) for i in range(n)])
    return acc


def scatter_sum_rows_paired(x, axis):
    n = lax.axis_size(axis)
    m = n // 2
    me = lax.axis_index(axis)
    core = me % 2
    chip = me // 2
    chunks = x.reshape(m, 2, x.shape[0] // n, *x.shape[1:])
    keep = jnp.take(chunks, core, axis=1)
    send = jnp.take(chunks, 1 - core, axis=1)
    part = keep + lax.ppermute(send, axis, [(i, i ^ 1) for i in range(n)])
    acc = jnp.take(part, chip, axis=0)
    for s in range(1, m):
        send = jnp.take(part, (chip + s) % m, axis=0)
        perm = [(i, ((i // 2 + s) % m) * 2 + i % 2) for i in range(n)]
        acc = acc + lax.ppermute(send, axis, perm)
    return acc


def recurrence_kernel(decay_ref, beta_ref, qt_ref, kt_ref, v_ref, s_ref, s_out, o_ref, *, heads, steps):
    r = pl.program_id(0)
    for h in range(heads):
        state = s_ref[0, h]
        for t in range(steps):
            c = t * heads + h
            key_col = kt_ref[0, :, c : c + 1]
            query_col = qt_ref[0, :, c : c + 1]
            state = state * decay_ref[r, c]
            recalled = jnp.sum(key_col * state, axis=0, keepdims=True)
            correction = (v_ref[0, c : c + 1, :] - recalled) * beta_ref[r, c]
            state = state + key_col * correction
            o_ref[0, c : c + 1, :] = jnp.sum(query_col * state, axis=0, keepdims=True)
        s_out[0, h] = state


def recurrence(decay, beta, qt, kt, values, memory_state):
    rows, heads = memory_state.shape[0], memory_state.shape[1]
    cols = decay.shape[1]
    steps = cols // heads
    kern = functools.partial(recurrence_kernel, heads=heads, steps=steps)
    return pl.pallas_call(
        kern,
        grid=(rows,),
        in_specs=[
            pl.BlockSpec(memory_space=pltpu.SMEM),
            pl.BlockSpec(memory_space=pltpu.SMEM),
            pl.BlockSpec((1, DK, cols), lambda r: (r, 0, 0)),
            pl.BlockSpec((1, DK, cols), lambda r: (r, 0, 0)),
            pl.BlockSpec((1, cols, DV), lambda r: (r, 0, 0)),
            pl.BlockSpec((1, heads, DK, DV), lambda r: (r, 0, 0, 0)),
        ],
        out_specs=[
            pl.BlockSpec((1, heads, DK, DV), lambda r: (r, 0, 0, 0)),
            pl.BlockSpec((1, cols, DV), lambda r: (r, 0, 0)),
        ],
        out_shape=[
            jax.ShapeDtypeStruct(memory_state.shape, jnp.float32),
            jax.ShapeDtypeStruct((rows, cols, DV), jnp.float32),
        ],
        cost_estimate=pl.CostEstimate(
            flops=8 * rows * cols * DK * DV,
            bytes_accessed=2 * memory_state.size * 4,
            transcendentals=0,
        ),
    )(decay, beta, qt, kt, values, memory_state)


def shards(
    activations,
    w_qk,
    w_vz,
    w_ba,
    conv_qk,
    conv_v,
    a_log,
    dt_bias,
    norm_gain,
    w_out,
    conv_state_qk,
    conv_state_v,
    memory_state,
):
    head_ratio = HV // HK
    step_count = activations.shape[1]
    rows_mem = memory_state.shape[0]
    heads = memory_state.shape[1]
    width_qk = w_qk.shape[1]
    width_vz = w_vz.shape[1]

    step_rows = gather_rows(activations, "head")
    flat_rows = step_rows.reshape(-1, step_rows.shape[-1])
    partial_qk = jnp.dot(flat_rows, w_qk, preferred_element_type=jnp.float32)
    partial_vz = jnp.dot(flat_rows, w_vz, preferred_element_type=jnp.float32)
    partial_ba = jnp.dot(flat_rows, w_ba, preferred_element_type=jnp.float32)
    summed = scatter_sum_rows_paired(
        jnp.concatenate([partial_qk, partial_vz, partial_ba], axis=1), "dp"
    )
    summed_qk = summed[:, :width_qk]
    summed_vz = summed[:, width_qk : width_qk + width_vz]
    summed_ba = summed[:, width_qk + width_vz :]
    qk_proj = summed_qk.astype(jnp.bfloat16).reshape(rows_mem, step_count, width_qk)
    vz_proj = summed_vz.astype(jnp.bfloat16).reshape(rows_mem, step_count, width_vz)
    ba_proj = summed_ba.astype(jnp.bfloat16).reshape(rows_mem, step_count, -1)

    split_vz = vz_proj.reshape(rows_mem, step_count, heads, 2, DV)
    values_now = split_vz[:, :, :, 0, :].reshape(rows_mem, step_count, heads * DV)
    gate_z = split_vz[:, :, :, 1, :].astype(jnp.float32)

    qk_conv = conv_steps(conv_state_qk, qk_proj, conv_qk).reshape(rows_mem, step_count, -1, 2, DK)
    v_conv = conv_steps(conv_state_v, values_now, conv_v).reshape(rows_mem, step_count * heads, DV)
    queries = normalize(qk_conv[:, :, :, 0, :]) * DK ** (-0.5)
    key_vec = normalize(qk_conv[:, :, :, 1, :])
    queries = jnp.repeat(queries, head_ratio, axis=2)
    key_vec = jnp.repeat(key_vec, head_ratio, axis=2)
    qt = queries.transpose(0, 3, 1, 2).reshape(rows_mem, DK, step_count * heads)
    kt = key_vec.transpose(0, 3, 1, 2).reshape(rows_mem, DK, step_count * heads)

    split_ba = ba_proj.reshape(rows_mem, step_count, heads, 2).astype(jnp.float32)
    beta_gate = jax.nn.sigmoid(split_ba[..., 0])
    log_decay = -jnp.exp(a_log)[None, None, :] * jax.nn.softplus(split_ba[..., 1] + dt_bias[None, None, :])
    decay = jnp.exp(log_decay).reshape(rows_mem, step_count * heads)
    beta_gate = beta_gate.reshape(rows_mem, step_count * heads)

    new_state, readout = recurrence(decay, beta_gate, qt, kt, v_conv, memory_state)
    readout = readout.reshape(rows_mem, step_count, heads, DV)

    scale = lax.rsqrt(jnp.mean(readout * readout, axis=-1, keepdims=True) + 1e-06)
    normed = readout * scale * norm_gain[None, None, None, :] * jax.nn.silu(gate_z)
    normed = normed.reshape(rows_mem, step_count, heads * DV).astype(jnp.bfloat16)

    all_normed = gather_rows(normed, "dp")
    partials = jnp.dot(
        all_normed.reshape(-1, all_normed.shape[-1]), w_out, preferred_element_type=jnp.float32
    )
    layer_out = scatter_sum_rows(partials, "head")
    layer_out = layer_out.astype(jnp.bfloat16).reshape(-1, step_count, w_out.shape[1])
    return (layer_out, new_state)


def solution(mesh):
    in_specs = (
        P(("groups", "head"), None, "dp"),
        P("dp", "head"),
        P("dp", "head"),
        P("dp", "head"),
        P(None, "head"),
        P(None, "head"),
        P("head"),
        P("head"),
        P(),
        P("head", "dp"),
        P(("groups", "dp"), None, "head"),
        P(("groups", "dp"), None, "head"),
        P(("groups", "dp"), "head", None, None),
    )
    out_specs = (P(("groups", "head"), None, "dp"), P(("groups", "dp"), "head", None, None))
    return jax.shard_map(shards, mesh=mesh, in_specs=in_specs, out_specs=out_specs, check_vma=False)
```

```python
import functools

import jax
import jax.numpy as jnp
from jax import lax
from jax.experimental import pallas as pl
from jax.experimental.pallas import tpu as pltpu
from jax.sharding import PartitionSpec as P

HK = 16
HV = 32
DK = 128
DV = 128


def normalize(vectors):
    return vectors * lax.rsqrt(jnp.sum(vectors * vectors, axis=-1, keepdims=True) + 1e-06)


def conv_steps(state, proj, taps):
    seq = jnp.concatenate([state, proj], axis=1).astype(jnp.float32)
    taps = taps.astype(jnp.float32)
    kernel = taps.shape[0]
    steps = proj.shape[1]
    mixed = sum(seq[:, k : k + steps, :] * taps[k][None, None, :] for k in range(kernel))
    return jax.nn.silu(mixed)


def gather_rows(x, axis):
    n = lax.axis_size(axis)
    me = lax.axis_index(axis)
    pieces = [x]
    for s in range(1, n):
        pieces.append(lax.ppermute(x, axis, [(i, (i + s) % n) for i in range(n)]))
    stacked = jnp.stack(pieces)
    order = (me - jnp.arange(n)) % n
    return jnp.take(stacked, order, axis=0).reshape(n * x.shape[0], *x.shape[1:])


def scatter_sum_rows(x, axis):
    n = lax.axis_size(axis)
    me = lax.axis_index(axis)
    chunks = x.reshape(n, x.shape[0] // n, *x.shape[1:])
    acc = jnp.take(chunks, me, axis=0)
    for s in range(1, n):
        send = jnp.take(chunks, (me + s) % n, axis=0)
        acc = acc + lax.ppermute(send, axis, [(i, (i + s) % n) for i in range(n)])
    return acc


def scatter_sum_rows_paired(x, axis):
    n = lax.axis_size(axis)
    m = n // 2
    me = lax.axis_index(axis)
    core = me % 2
    chip = me // 2
    chunks = x.reshape(m, 2, x.shape[0] // n, *x.shape[1:])
    keep = jnp.take(chunks, core, axis=1)
    send = jnp.take(chunks, 1 - core, axis=1)
    part = keep + lax.ppermute(send, axis, [(i, i ^ 1) for i in range(n)])
    acc = jnp.take(part, chip, axis=0)
    for s in range(1, m):
        send = jnp.take(part, (chip + s) % m, axis=0)
        perm = [(i, ((i // 2 + s) % m) * 2 + i % 2) for i in range(n)]
        acc = acc + lax.ppermute(send, axis, perm)
    return acc


def gather_pieces(x, axis):
    n = lax.axis_size(axis)
    pieces = [x]
    for s in range(1, n):
        pieces.append(lax.ppermute(x, axis, [(i, (i + s) % n) for i in range(n)]))
    return jnp.stack(pieces)


def projection_kernel(x_ref, wqk_ref, wvz_ref, wba_ref, *outs):
    x = x_ref[...]
    section = outs[0].shape[0]
    offset = 0
    for w_ref in (wqk_ref, wvz_ref, wba_ref):
        width = w_ref.shape[1]
        y = jnp.dot(x, w_ref[...], preferred_element_type=jnp.float32)
        for i, o_ref in enumerate(outs):
            o_ref[:, offset : offset + width] = y[i * section : (i + 1) * section]
        offset += width


def projection(x, w_qk, w_vz, w_ba, sections):
    rows = x.shape[0] // sections
    cols = w_qk.shape[1] + w_vz.shape[1] + w_ba.shape[1]
    return pl.pallas_call(
        projection_kernel,
        out_shape=[jax.ShapeDtypeStruct((rows, cols), jnp.float32)] * sections,
        cost_estimate=pl.CostEstimate(
            flops=2 * x.shape[0] * x.shape[1] * cols,
            bytes_accessed=2 * x.shape[1] * cols + 2 * x.size + 4 * x.shape[0] * cols,
            transcendentals=0,
        ),
    )(x, w_qk, w_vz, w_ba)


def recurrence_kernel(decay_ref, beta_ref, qt_ref, kt_ref, v_ref, s_ref, s_out, o_ref, *, heads, steps):
    r = pl.program_id(0)
    for h in range(heads):
        state = s_ref[0, h]
        for t in range(steps):
            c = t * heads + h
            key_col = kt_ref[0, :, c : c + 1]
            query_col = qt_ref[0, :, c : c + 1]
            state = state * decay_ref[r, c]
            recalled = jnp.sum(key_col * state, axis=0, keepdims=True)
            correction = (v_ref[0, c : c + 1, :] - recalled) * beta_ref[r, c]
            state = state + key_col * correction
            o_ref[0, c : c + 1, :] = jnp.sum(query_col * state, axis=0, keepdims=True)
        s_out[0, h] = state


def recurrence(decay, beta, qt, kt, values, memory_state):
    rows, heads = memory_state.shape[0], memory_state.shape[1]
    cols = decay.shape[1]
    steps = cols // heads
    kern = functools.partial(recurrence_kernel, heads=heads, steps=steps)
    return pl.pallas_call(
        kern,
        grid=(rows,),
        in_specs=[
            pl.BlockSpec(memory_space=pltpu.SMEM),
            pl.BlockSpec(memory_space=pltpu.SMEM),
            pl.BlockSpec((1, DK, cols), lambda r: (r, 0, 0)),
            pl.BlockSpec((1, DK, cols), lambda r: (r, 0, 0)),
            pl.BlockSpec((1, cols, DV), lambda r: (r, 0, 0)),
            pl.BlockSpec((1, heads, DK, DV), lambda r: (r, 0, 0, 0)),
        ],
        out_specs=[
            pl.BlockSpec((1, heads, DK, DV), lambda r: (r, 0, 0, 0)),
            pl.BlockSpec((1, cols, DV), lambda r: (r, 0, 0)),
        ],
        out_shape=[
            jax.ShapeDtypeStruct(memory_state.shape, jnp.float32),
            jax.ShapeDtypeStruct((rows, cols, DV), jnp.float32),
        ],
        cost_estimate=pl.CostEstimate(
            flops=8 * rows * cols * DK * DV,
            bytes_accessed=2 * memory_state.size * 4,
            transcendentals=0,
        ),
    )(decay, beta, qt, kt, values, memory_state)


def shards(
    activations,
    w_qk,
    w_vz,
    w_ba,
    conv_qk,
    conv_v,
    a_log,
    dt_bias,
    norm_gain,
    w_out,
    conv_state_qk,
    conv_state_v,
    memory_state,
):
    head_ratio = HV // HK
    step_count = activations.shape[1]
    rows_mem = memory_state.shape[0]
    heads = memory_state.shape[1]
    width_qk = w_qk.shape[1]
    width_vz = w_vz.shape[1]

    pieces = gather_pieces(activations, "head")
    n_head, rows_head = pieces.shape[0], pieces.shape[1]
    flat_pieces = pieces.reshape(-1, pieces.shape[-1])
    me_head = lax.axis_index("head")
    n_dp = lax.axis_size("dp")
    chips = n_dp // 2
    me_dp = lax.axis_index("dp")
    core, chip = me_dp % 2, me_dp // 2
    local_rows = jnp.arange(rows_mem)
    steps = jnp.arange(step_count)
    index_blocks = []
    for which in (1 - core, core):
        for s in range(chips):
            block = ((chip + s) % chips) * 2 + which
            rows = block * rows_mem + local_rows
            source = (me_head - rows // rows_head) % n_head
            flat = (source * rows_head + rows % rows_head)[:, None] * step_count + steps[None, :]
            index_blocks.append(flat.reshape(-1))
    flat_rows = jnp.take(flat_pieces, jnp.concatenate(index_blocks), axis=0)
    outs = projection(flat_rows, w_qk, w_vz, w_ba, 2 * chips)
    pair = [(i, i ^ 1) for i in range(n_dp)]
    part = [keep + lax.ppermute(send, "dp", pair) for send, keep in zip(outs[:chips], outs[chips:])]
    summed = part[0]
    for s in range(1, chips):
        perm = [(i, ((i // 2 + s) % chips) * 2 + i % 2) for i in range(n_dp)]
        summed = summed + lax.ppermute(part[s], "dp", perm)
    summed_qk = summed[:, :width_qk]
    summed_vz = summed[:, width_qk : width_qk + width_vz]
    summed_ba = summed[:, width_qk + width_vz :]
    qk_proj = summed_qk.astype(jnp.bfloat16).reshape(rows_mem, step_count, width_qk)
    vz_proj = summed_vz.astype(jnp.bfloat16).reshape(rows_mem, step_count, width_vz)
    ba_proj = summed_ba.astype(jnp.bfloat16).reshape(rows_mem, step_count, -1)

    split_vz = vz_proj.reshape(rows_mem, step_count, heads, 2, DV)
    values_now = split_vz[:, :, :, 0, :].reshape(rows_mem, step_count, heads * DV)
    gate_z = split_vz[:, :, :, 1, :].astype(jnp.float32)

    qk_conv = conv_steps(conv_state_qk, qk_proj, conv_qk).reshape(rows_mem, step_count, -1, 2, DK)
    v_conv = conv_steps(conv_state_v, values_now, conv_v).reshape(rows_mem, step_count * heads, DV)
    queries = normalize(qk_conv[:, :, :, 0, :]) * DK ** (-0.5)
    key_vec = normalize(qk_conv[:, :, :, 1, :])
    queries = jnp.repeat(queries, head_ratio, axis=2)
    key_vec = jnp.repeat(key_vec, head_ratio, axis=2)
    qt = queries.transpose(0, 3, 1, 2).reshape(rows_mem, DK, step_count * heads)
    kt = key_vec.transpose(0, 3, 1, 2).reshape(rows_mem, DK, step_count * heads)

    split_ba = ba_proj.reshape(rows_mem, step_count, heads, 2).astype(jnp.float32)
    beta_gate = jax.nn.sigmoid(split_ba[..., 0])
    log_decay = -jnp.exp(a_log)[None, None, :] * jax.nn.softplus(split_ba[..., 1] + dt_bias[None, None, :])
    decay = jnp.exp(log_decay).reshape(rows_mem, step_count * heads)
    beta_gate = beta_gate.reshape(rows_mem, step_count * heads)

    new_state, readout = recurrence(decay, beta_gate, qt, kt, v_conv, memory_state)
    readout = readout.reshape(rows_mem, step_count, heads, DV)

    scale = lax.rsqrt(jnp.mean(readout * readout, axis=-1, keepdims=True) + 1e-06)
    normed = readout * scale * norm_gain[None, None, None, :] * jax.nn.silu(gate_z)
    normed = normed.reshape(rows_mem, step_count, heads * DV).astype(jnp.bfloat16)

    all_normed = gather_rows(normed, "dp")
    partials = jnp.dot(
        all_normed.reshape(-1, all_normed.shape[-1]), w_out, preferred_element_type=jnp.float32
    )
    layer_out = scatter_sum_rows(partials, "head")
    layer_out = layer_out.astype(jnp.bfloat16).reshape(-1, step_count, w_out.shape[1])
    return (layer_out, new_state)


def solution(mesh):
    in_specs = (
        P(("groups", "head"), None, "dp"),
        P("dp", "head"),
        P("dp", "head"),
        P("dp", "head"),
        P(None, "head"),
        P(None, "head"),
        P("head"),
        P("head"),
        P(),
        P("head", "dp"),
        P(("groups", "dp"), None, "head"),
        P(("groups", "dp"), None, "head"),
        P(("groups", "dp"), "head", None, None),
    )
    out_specs = (P(("groups", "head"), None, "dp"), P(("groups", "dp"), "head", None, None))
    return jax.shard_map(shards, mesh=mesh, in_specs=in_specs, out_specs=out_specs, check_vma=False)
```

```python
import functools

import jax
import jax.numpy as jnp
from jax import lax
from jax.experimental import pallas as pl
from jax.experimental.pallas import tpu as pltpu
from jax.sharding import PartitionSpec as P

HK = 16
HV = 32
DK = 128
DV = 128


def normalize(vectors):
    return vectors * lax.rsqrt(jnp.sum(vectors * vectors, axis=-1, keepdims=True) + 1e-06)


def conv_steps(state, proj, taps):
    seq = jnp.concatenate([state, proj], axis=1).astype(jnp.float32)
    taps = taps.astype(jnp.float32)
    kernel = taps.shape[0]
    steps = proj.shape[1]
    mixed = sum(seq[:, k : k + steps, :] * taps[k][None, None, :] for k in range(kernel))
    return jax.nn.silu(mixed)


def gather_rows(x, axis):
    n = lax.axis_size(axis)
    me = lax.axis_index(axis)
    pieces = [x]
    for s in range(1, n):
        pieces.append(lax.ppermute(x, axis, [(i, (i + s) % n) for i in range(n)]))
    stacked = jnp.stack(pieces)
    order = (me - jnp.arange(n)) % n
    return jnp.take(stacked, order, axis=0).reshape(n * x.shape[0], *x.shape[1:])


def scatter_sum_rows(x, axis):
    n = lax.axis_size(axis)
    me = lax.axis_index(axis)
    chunks = x.reshape(n, x.shape[0] // n, *x.shape[1:])
    acc = jnp.take(chunks, me, axis=0)
    for s in range(1, n):
        send = jnp.take(chunks, (me + s) % n, axis=0)
        acc = acc + lax.ppermute(send, axis, [(i, (i + s) % n) for i in range(n)])
    return acc


def scatter_sum_rows_paired(x, axis):
    n = lax.axis_size(axis)
    m = n // 2
    me = lax.axis_index(axis)
    core = me % 2
    chip = me // 2
    chunks = x.reshape(m, 2, x.shape[0] // n, *x.shape[1:])
    keep = jnp.take(chunks, core, axis=1)
    send = jnp.take(chunks, 1 - core, axis=1)
    part = keep + lax.ppermute(send, axis, [(i, i ^ 1) for i in range(n)])
    acc = jnp.take(part, chip, axis=0)
    for s in range(1, m):
        send = jnp.take(part, (chip + s) % m, axis=0)
        perm = [(i, ((i // 2 + s) % m) * 2 + i % 2) for i in range(n)]
        acc = acc + lax.ppermute(send, axis, perm)
    return acc


def gather_pieces(x, axis):
    n = lax.axis_size(axis)
    pieces = [x]
    for s in range(1, n):
        pieces.append(lax.ppermute(x, axis, [(i, (i + s) % n) for i in range(n)]))
    return jnp.stack(pieces)


def projection_kernel(x_ref, wqk_ref, wvz_ref, wba_ref, *outs):
    x = x_ref[...]
    section = outs[0].shape[0]
    offset = 0
    for w_ref in (wqk_ref, wvz_ref, wba_ref):
        width = w_ref.shape[1]
        y = jnp.dot(x, w_ref[...], preferred_element_type=jnp.float32)
        for i, o_ref in enumerate(outs):
            o_ref[:, offset : offset + width] = y[i * section : (i + 1) * section]
        offset += width


def projection(x, w_qk, w_vz, w_ba, sections):
    rows = x.shape[0] // sections
    cols = w_qk.shape[1] + w_vz.shape[1] + w_ba.shape[1]
    return pl.pallas_call(
        projection_kernel,
        out_shape=[jax.ShapeDtypeStruct((rows, cols), jnp.float32)] * sections,
        cost_estimate=pl.CostEstimate(
            flops=2 * x.shape[0] * x.shape[1] * cols,
            bytes_accessed=2 * x.shape[1] * cols + 2 * x.size + 4 * x.shape[0] * cols,
            transcendentals=0,
        ),
    )(x, w_qk, w_vz, w_ba)


def recurrence_kernel(decay_ref, beta_ref, qt_ref, kt_ref, v_ref, s_ref, s_out, o_ref, *, heads, steps):
    r = pl.program_id(0)
    for h in range(heads):
        state = s_ref[0, h]
        for t in range(steps):
            c = t * heads + h
            key_col = kt_ref[0, :, c : c + 1]
            query_col = qt_ref[0, :, c : c + 1]
            state = state * decay_ref[r, c]
            recalled = jnp.sum(key_col * state, axis=0, keepdims=True)
            correction = (v_ref[0, c : c + 1, :] - recalled) * beta_ref[r, c]
            state = state + key_col * correction
            o_ref[0, c : c + 1, :] = jnp.sum(query_col * state, axis=0, keepdims=True)
        s_out[0, h] = state


def recurrence(decay, beta, qt, kt, values, memory_state):
    rows, heads = memory_state.shape[0], memory_state.shape[1]
    cols = decay.shape[1]
    steps = cols // heads
    kern = functools.partial(recurrence_kernel, heads=heads, steps=steps)
    return pl.pallas_call(
        kern,
        grid=(rows,),
        in_specs=[
            pl.BlockSpec(memory_space=pltpu.SMEM),
            pl.BlockSpec(memory_space=pltpu.SMEM),
            pl.BlockSpec((1, DK, cols), lambda r: (r, 0, 0)),
            pl.BlockSpec((1, DK, cols), lambda r: (r, 0, 0)),
            pl.BlockSpec((1, cols, DV), lambda r: (r, 0, 0)),
            pl.BlockSpec((1, heads, DK, DV), lambda r: (r, 0, 0, 0)),
        ],
        out_specs=[
            pl.BlockSpec((1, heads, DK, DV), lambda r: (r, 0, 0, 0)),
            pl.BlockSpec((1, cols, DV), lambda r: (r, 0, 0)),
        ],
        out_shape=[
            jax.ShapeDtypeStruct(memory_state.shape, jnp.float32),
            jax.ShapeDtypeStruct((rows, cols, DV), jnp.float32),
        ],
        cost_estimate=pl.CostEstimate(
            flops=8 * rows * cols * DK * DV,
            bytes_accessed=2 * memory_state.size * 4,
            transcendentals=0,
        ),
    )(decay, beta, qt, kt, values, memory_state)


def shards(
    activations,
    w_qk,
    w_vz,
    w_ba,
    conv_qk,
    conv_v,
    a_log,
    dt_bias,
    norm_gain,
    w_out,
    conv_state_qk,
    conv_state_v,
    memory_state,
):
    head_ratio = HV // HK
    step_count = activations.shape[1]
    rows_mem = memory_state.shape[0]
    heads = memory_state.shape[1]
    width_qk = w_qk.shape[1]
    width_vz = w_vz.shape[1]

    pieces = gather_pieces(activations, "head")
    n_head, rows_head = pieces.shape[0], pieces.shape[1]
    flat_pieces = pieces.reshape(-1, pieces.shape[-1])
    me_head = lax.axis_index("head")
    n_dp = lax.axis_size("dp")
    chips = n_dp // 2
    me_dp = lax.axis_index("dp")
    core, chip = me_dp % 2, me_dp // 2
    local_rows = jnp.arange(rows_mem)
    steps = jnp.arange(step_count)
    index_blocks = []
    for which in (1 - core, core):
        for s in range(chips):
            block = ((chip + s) % chips) * 2 + which
            rows = block * rows_mem + local_rows
            source = (me_head - rows // rows_head) % n_head
            flat = (source * rows_head + rows % rows_head)[:, None] * step_count + steps[None, :]
            index_blocks.append(flat.reshape(-1))
    flat_rows = jnp.take(flat_pieces, jnp.concatenate(index_blocks), axis=0)
    outs = projection(flat_rows, w_qk, w_vz, w_ba, 2 * chips)
    pair = [(i, i ^ 1) for i in range(n_dp)]
    part = [keep + lax.ppermute(send, "dp", pair) for send, keep in zip(outs[:chips], outs[chips:])]
    summed = part[0]
    for s in range(1, chips):
        perm = [(i, ((i // 2 + s) % chips) * 2 + i % 2) for i in range(n_dp)]
        sent = lax.ppermute(part[s].astype(jnp.bfloat16), "dp", perm)
        summed = summed + sent.astype(jnp.float32)
    summed_qk = summed[:, :width_qk]
    summed_vz = summed[:, width_qk : width_qk + width_vz]
    summed_ba = summed[:, width_qk + width_vz :]
    qk_proj = summed_qk.astype(jnp.bfloat16).reshape(rows_mem, step_count, width_qk)
    vz_proj = summed_vz.astype(jnp.bfloat16).reshape(rows_mem, step_count, width_vz)
    ba_proj = summed_ba.astype(jnp.bfloat16).reshape(rows_mem, step_count, -1)

    split_vz = vz_proj.reshape(rows_mem, step_count, heads, 2, DV)
    values_now = split_vz[:, :, :, 0, :].reshape(rows_mem, step_count, heads * DV)
    gate_z = split_vz[:, :, :, 1, :].astype(jnp.float32)

    qk_conv = conv_steps(conv_state_qk, qk_proj, conv_qk).reshape(rows_mem, step_count, -1, 2, DK)
    v_conv = conv_steps(conv_state_v, values_now, conv_v).reshape(rows_mem, step_count * heads, DV)
    queries = normalize(qk_conv[:, :, :, 0, :]) * DK ** (-0.5)
    key_vec = normalize(qk_conv[:, :, :, 1, :])
    queries = jnp.repeat(queries, head_ratio, axis=2)
    key_vec = jnp.repeat(key_vec, head_ratio, axis=2)
    qt = queries.transpose(0, 3, 1, 2).reshape(rows_mem, DK, step_count * heads)
    kt = key_vec.transpose(0, 3, 1, 2).reshape(rows_mem, DK, step_count * heads)

    split_ba = ba_proj.reshape(rows_mem, step_count, heads, 2).astype(jnp.float32)
    beta_gate = jax.nn.sigmoid(split_ba[..., 0])
    log_decay = -jnp.exp(a_log)[None, None, :] * jax.nn.softplus(split_ba[..., 1] + dt_bias[None, None, :])
    decay = jnp.exp(log_decay).reshape(rows_mem, step_count * heads)
    beta_gate = beta_gate.reshape(rows_mem, step_count * heads)

    new_state, readout = recurrence(decay, beta_gate, qt, kt, v_conv, memory_state)
    readout = readout.reshape(rows_mem, step_count, heads, DV)

    scale = lax.rsqrt(jnp.mean(readout * readout, axis=-1, keepdims=True) + 1e-06)
    normed = readout * scale * norm_gain[None, None, None, :] * jax.nn.silu(gate_z)
    normed = normed.reshape(rows_mem, step_count, heads * DV).astype(jnp.bfloat16)

    all_normed = gather_rows(normed, "dp")
    partials = jnp.dot(
        all_normed.reshape(-1, all_normed.shape[-1]), w_out, preferred_element_type=jnp.float32
    )
    layer_out = scatter_sum_rows(partials, "head")
    layer_out = layer_out.astype(jnp.bfloat16).reshape(-1, step_count, w_out.shape[1])
    return (layer_out, new_state)


def solution(mesh):
    in_specs = (
        P(("groups", "head"), None, "dp"),
        P("dp", "head"),
        P("dp", "head"),
        P("dp", "head"),
        P(None, "head"),
        P(None, "head"),
        P("head"),
        P("head"),
        P(),
        P("head", "dp"),
        P(("groups", "dp"), None, "head"),
        P(("groups", "dp"), None, "head"),
        P(("groups", "dp"), "head", None, None),
    )
    out_specs = (P(("groups", "head"), None, "dp"), P(("groups", "dp"), "head", None, None))
    return jax.shard_map(shards, mesh=mesh, in_specs=in_specs, out_specs=out_specs, check_vma=False)
```

```python
import functools

import jax
import jax.numpy as jnp
from jax import lax
from jax.experimental import pallas as pl
from jax.experimental.pallas import tpu as pltpu
from jax.sharding import PartitionSpec as P

HK = 16
HV = 32
DK = 128
DV = 128


def normalize(vectors):
    return vectors * lax.rsqrt(jnp.sum(vectors * vectors, axis=-1, keepdims=True) + 1e-06)


def conv_steps(state, proj, taps):
    seq = jnp.concatenate([state, proj], axis=1).astype(jnp.float32)
    taps = taps.astype(jnp.float32)
    kernel = taps.shape[0]
    steps = proj.shape[1]
    mixed = sum(seq[:, k : k + steps, :] * taps[k][None, None, :] for k in range(kernel))
    return jax.nn.silu(mixed)


def gather_rows(x, axis):
    n = lax.axis_size(axis)
    me = lax.axis_index(axis)
    pieces = [x]
    for s in range(1, n):
        pieces.append(lax.ppermute(x, axis, [(i, (i + s) % n) for i in range(n)]))
    stacked = jnp.stack(pieces)
    order = (me - jnp.arange(n)) % n
    return jnp.take(stacked, order, axis=0).reshape(n * x.shape[0], *x.shape[1:])


def scatter_sum_rows(x, axis):
    n = lax.axis_size(axis)
    me = lax.axis_index(axis)
    chunks = x.reshape(n, x.shape[0] // n, *x.shape[1:])
    acc = jnp.take(chunks, me, axis=0)
    for s in range(1, n):
        send = jnp.take(chunks, (me + s) % n, axis=0)
        acc = acc + lax.ppermute(send, axis, [(i, (i + s) % n) for i in range(n)])
    return acc


def scatter_sum_rows_paired(x, axis):
    n = lax.axis_size(axis)
    m = n // 2
    me = lax.axis_index(axis)
    core = me % 2
    chip = me // 2
    chunks = x.reshape(m, 2, x.shape[0] // n, *x.shape[1:])
    keep = jnp.take(chunks, core, axis=1)
    send = jnp.take(chunks, 1 - core, axis=1)
    part = keep + lax.ppermute(send, axis, [(i, i ^ 1) for i in range(n)])
    acc = jnp.take(part, chip, axis=0)
    for s in range(1, m):
        send = jnp.take(part, (chip + s) % m, axis=0)
        perm = [(i, ((i // 2 + s) % m) * 2 + i % 2) for i in range(n)]
        acc = acc + lax.ppermute(send, axis, perm)
    return acc


def gather_pieces(x, axis):
    n = lax.axis_size(axis)
    pieces = [x]
    for s in range(1, n):
        pieces.append(lax.ppermute(x, axis, [(i, (i + s) % n) for i in range(n)]))
    return jnp.stack(pieces)


def projection_kernel(x_ref, wqk_ref, wvz_ref, wba_ref, *outs):
    x = x_ref[...]
    section = outs[0].shape[0]
    offset = 0
    for w_ref in (wqk_ref, wvz_ref, wba_ref):
        width = w_ref.shape[1]
        y = jnp.dot(x, w_ref[...], preferred_element_type=jnp.float32)
        for i, o_ref in enumerate(outs):
            o_ref[:, offset : offset + width] = y[i * section : (i + 1) * section]
        offset += width


def projection(x, w_qk, w_vz, w_ba, sections):
    rows = x.shape[0] // sections
    cols = w_qk.shape[1] + w_vz.shape[1] + w_ba.shape[1]
    return pl.pallas_call(
        projection_kernel,
        out_shape=[jax.ShapeDtypeStruct((rows, cols), jnp.float32)] * sections,
        cost_estimate=pl.CostEstimate(
            flops=2 * x.shape[0] * x.shape[1] * cols,
            bytes_accessed=2 * x.shape[1] * cols + 2 * x.size + 4 * x.shape[0] * cols,
            transcendentals=0,
        ),
    )(x, w_qk, w_vz, w_ba)


def recurrence_kernel(decay_ref, beta_ref, qt_ref, kt_ref, sel_ref, v_ref, s_ref, s_out, o_ref, *, heads, steps):
    r = pl.program_id(0)
    select = sel_ref[...]
    key_all = jnp.dot(kt_ref[0], select, preferred_element_type=jnp.float32)
    query_all = jnp.dot(qt_ref[0], select, preferred_element_type=jnp.float32)
    for h in range(heads):
        state = s_ref[0, h]
        for t in range(steps):
            c = t * heads + h
            key_b = key_all[:, c * DV : (c + 1) * DV]
            query_b = query_all[:, c * DV : (c + 1) * DV]
            state = state * decay_ref[r, c]
            recalled = jnp.sum(key_b * state, axis=0, keepdims=True)
            correction = (v_ref[0, c : c + 1, :] - recalled) * beta_ref[r, c]
            state = state + key_b * correction
            o_ref[0, c : c + 1, :] = jnp.sum(query_b * state, axis=0, keepdims=True)
        s_out[0, h] = state


def split_three(x, width):
    hi = lax.reduce_precision(x, exponent_bits=8, mantissa_bits=7)
    rest = x - hi
    mid = lax.reduce_precision(rest, exponent_bits=8, mantissa_bits=7)
    lo = rest - mid
    parts = jnp.concatenate([hi, mid, lo], axis=-1)
    parts = jnp.pad(parts, ((0, 0), (0, 0), (0, width - parts.shape[-1])))
    return parts.astype(jnp.bfloat16)


def selector(cols, width):
    rows = jnp.arange(width)[:, None]
    lanes = jnp.arange(cols * DV)[None, :]
    return ((rows % cols == lanes // DV) & (rows < 3 * cols)).astype(jnp.bfloat16)


def recurrence(decay, beta, qt, kt, values, memory_state):
    rows, heads = memory_state.shape[0], memory_state.shape[1]
    cols = decay.shape[1]
    steps = cols // heads
    width = -(-3 * cols // 128) * 128
    qt3 = split_three(qt, width)
    kt3 = split_three(kt, width)
    select = selector(cols, width)
    kern = functools.partial(recurrence_kernel, heads=heads, steps=steps)
    return pl.pallas_call(
        kern,
        grid=(rows,),
        in_specs=[
            pl.BlockSpec(memory_space=pltpu.SMEM),
            pl.BlockSpec(memory_space=pltpu.SMEM),
            pl.BlockSpec((1, DK, width), lambda r: (r, 0, 0)),
            pl.BlockSpec((1, DK, width), lambda r: (r, 0, 0)),
            pl.BlockSpec((width, cols * DV), lambda r: (0, 0)),
            pl.BlockSpec((1, cols, DV), lambda r: (r, 0, 0)),
            pl.BlockSpec((1, heads, DK, DV), lambda r: (r, 0, 0, 0)),
        ],
        out_specs=[
            pl.BlockSpec((1, heads, DK, DV), lambda r: (r, 0, 0, 0)),
            pl.BlockSpec((1, cols, DV), lambda r: (r, 0, 0)),
        ],
        out_shape=[
            jax.ShapeDtypeStruct(memory_state.shape, jnp.float32),
            jax.ShapeDtypeStruct((rows, cols, DV), jnp.float32),
        ],
        cost_estimate=pl.CostEstimate(
            flops=8 * rows * cols * DK * DV + 4 * rows * width * cols * DV * DK,
            bytes_accessed=2 * memory_state.size * 4,
            transcendentals=0,
        ),
    )(decay, beta, qt3, kt3, select, values, memory_state)


def shards(
    activations,
    w_qk,
    w_vz,
    w_ba,
    conv_qk,
    conv_v,
    a_log,
    dt_bias,
    norm_gain,
    w_out,
    conv_state_qk,
    conv_state_v,
    memory_state,
):
    head_ratio = HV // HK
    step_count = activations.shape[1]
    rows_mem = memory_state.shape[0]
    heads = memory_state.shape[1]
    width_qk = w_qk.shape[1]
    width_vz = w_vz.shape[1]

    pieces = gather_pieces(activations, "head")
    n_head, rows_head = pieces.shape[0], pieces.shape[1]
    flat_pieces = pieces.reshape(-1, pieces.shape[-1])
    me_head = lax.axis_index("head")
    n_dp = lax.axis_size("dp")
    chips = n_dp // 2
    me_dp = lax.axis_index("dp")
    core, chip = me_dp % 2, me_dp // 2
    local_rows = jnp.arange(rows_mem)
    steps = jnp.arange(step_count)
    index_blocks = []
    for which in (1 - core, core):
        for s in range(chips):
            block = ((chip + s) % chips) * 2 + which
            rows = block * rows_mem + local_rows
            source = (me_head - rows // rows_head) % n_head
            flat = (source * rows_head + rows % rows_head)[:, None] * step_count + steps[None, :]
            index_blocks.append(flat.reshape(-1))
    flat_rows = jnp.take(flat_pieces, jnp.concatenate(index_blocks), axis=0)
    outs = projection(flat_rows, w_qk, w_vz, w_ba, 2 * chips)
    pair = [(i, i ^ 1) for i in range(n_dp)]
    part = [keep + lax.ppermute(send, "dp", pair) for send, keep in zip(outs[:chips], outs[chips:])]
    summed = part[0]
    for s in range(1, chips):
        perm = [(i, ((i // 2 + s) % chips) * 2 + i % 2) for i in range(n_dp)]
        summed = summed + lax.ppermute(part[s], "dp", perm)
    summed_qk = summed[:, :width_qk]
    summed_vz = summed[:, width_qk : width_qk + width_vz]
    summed_ba = summed[:, width_qk + width_vz :]
    qk_proj = summed_qk.astype(jnp.bfloat16).reshape(rows_mem, step_count, width_qk)
    vz_proj = summed_vz.astype(jnp.bfloat16).reshape(rows_mem, step_count, width_vz)
    ba_proj = summed_ba.astype(jnp.bfloat16).reshape(rows_mem, step_count, -1)

    split_vz = vz_proj.reshape(rows_mem, step_count, heads, 2, DV)
    values_now = split_vz[:, :, :, 0, :].reshape(rows_mem, step_count, heads * DV)
    gate_z = split_vz[:, :, :, 1, :].astype(jnp.float32)

    qk_conv = conv_steps(conv_state_qk, qk_proj, conv_qk).reshape(rows_mem, step_count, -1, 2, DK)
    v_conv = conv_steps(conv_state_v, values_now, conv_v).reshape(rows_mem, step_count * heads, DV)
    queries = normalize(qk_conv[:, :, :, 0, :]) * DK ** (-0.5)
    key_vec = normalize(qk_conv[:, :, :, 1, :])
    queries = jnp.repeat(queries, head_ratio, axis=2)
    key_vec = jnp.repeat(key_vec, head_ratio, axis=2)
    qt = queries.transpose(0, 3, 1, 2).reshape(rows_mem, DK, step_count * heads)
    kt = key_vec.transpose(0, 3, 1, 2).reshape(rows_mem, DK, step_count * heads)

    split_ba = ba_proj.reshape(rows_mem, step_count, heads, 2).astype(jnp.float32)
    beta_gate = jax.nn.sigmoid(split_ba[..., 0])
    log_decay = -jnp.exp(a_log)[None, None, :] * jax.nn.softplus(split_ba[..., 1] + dt_bias[None, None, :])
    decay = jnp.exp(log_decay).reshape(rows_mem, step_count * heads)
    beta_gate = beta_gate.reshape(rows_mem, step_count * heads)

    new_state, readout = recurrence(decay, beta_gate, qt, kt, v_conv, memory_state)
    readout = readout.reshape(rows_mem, step_count, heads, DV)

    scale = lax.rsqrt(jnp.mean(readout * readout, axis=-1, keepdims=True) + 1e-06)
    normed = readout * scale * norm_gain[None, None, None, :] * jax.nn.silu(gate_z)
    normed = normed.reshape(rows_mem, step_count, heads * DV).astype(jnp.bfloat16)

    all_normed = gather_rows(normed, "dp")
    partials = jnp.dot(
        all_normed.reshape(-1, all_normed.shape[-1]), w_out, preferred_element_type=jnp.float32
    )
    layer_out = scatter_sum_rows(partials, "head")
    layer_out = layer_out.astype(jnp.bfloat16).reshape(-1, step_count, w_out.shape[1])
    return (layer_out, new_state)


def solution(mesh):
    in_specs = (
        P(("groups", "head"), None, "dp"),
        P("dp", "head"),
        P("dp", "head"),
        P("dp", "head"),
        P(None, "head"),
        P(None, "head"),
        P("head"),
        P("head"),
        P(),
        P("head", "dp"),
        P(("groups", "dp"), None, "head"),
        P(("groups", "dp"), None, "head"),
        P(("groups", "dp"), "head", None, None),
    )
    out_specs = (P(("groups", "head"), None, "dp"), P(("groups", "dp"), "head", None, None))
    return jax.shard_map(shards, mesh=mesh, in_specs=in_specs, out_specs=out_specs, check_vma=False)
```

```python
import functools

import jax
import jax.numpy as jnp
from jax import lax
from jax.experimental import pallas as pl
from jax.experimental.pallas import tpu as pltpu
from jax.sharding import PartitionSpec as P

HK = 16
HV = 32
DK = 128
DV = 128


def normalize(vectors):
    return vectors * lax.rsqrt(jnp.sum(vectors * vectors, axis=-1, keepdims=True) + 1e-06)


def conv_steps(state, proj, taps):
    seq = jnp.concatenate([state, proj], axis=1).astype(jnp.float32)
    taps = taps.astype(jnp.float32)
    kernel = taps.shape[0]
    steps = proj.shape[1]
    mixed = sum(seq[:, k : k + steps, :] * taps[k][None, None, :] for k in range(kernel))
    return jax.nn.silu(mixed)


def gather_rows(x, axis):
    n = lax.axis_size(axis)
    me = lax.axis_index(axis)
    pieces = [x]
    for s in range(1, n):
        pieces.append(lax.ppermute(x, axis, [(i, (i + s) % n) for i in range(n)]))
    stacked = jnp.stack(pieces)
    order = (me - jnp.arange(n)) % n
    return jnp.take(stacked, order, axis=0).reshape(n * x.shape[0], *x.shape[1:])


def scatter_sum_rows(x, axis):
    n = lax.axis_size(axis)
    me = lax.axis_index(axis)
    chunks = x.reshape(n, x.shape[0] // n, *x.shape[1:])
    acc = jnp.take(chunks, me, axis=0)
    for s in range(1, n):
        send = jnp.take(chunks, (me + s) % n, axis=0)
        acc = acc + lax.ppermute(send, axis, [(i, (i + s) % n) for i in range(n)])
    return acc


def scatter_sum_rows_paired(x, axis):
    n = lax.axis_size(axis)
    m = n // 2
    me = lax.axis_index(axis)
    core = me % 2
    chip = me // 2
    chunks = x.reshape(m, 2, x.shape[0] // n, *x.shape[1:])
    keep = jnp.take(chunks, core, axis=1)
    send = jnp.take(chunks, 1 - core, axis=1)
    part = keep + lax.ppermute(send, axis, [(i, i ^ 1) for i in range(n)])
    acc = jnp.take(part, chip, axis=0)
    for s in range(1, m):
        send = jnp.take(part, (chip + s) % m, axis=0)
        perm = [(i, ((i // 2 + s) % m) * 2 + i % 2) for i in range(n)]
        acc = acc + lax.ppermute(send, axis, perm)
    return acc


def gather_pieces(x, axis):
    n = lax.axis_size(axis)
    pieces = [x]
    for s in range(1, n):
        pieces.append(lax.ppermute(x, axis, [(i, (i + s) % n) for i in range(n)]))
    return jnp.stack(pieces)


def projection_kernel(x_ref, wqk_ref, wvz_ref, wba_ref, *outs):
    x = x_ref[...]
    section = outs[0].shape[0]
    offset = 0
    for w_ref in (wqk_ref, wvz_ref, wba_ref):
        width = w_ref.shape[1]
        y = jnp.dot(x, w_ref[...], preferred_element_type=jnp.float32)
        for i, o_ref in enumerate(outs):
            o_ref[:, offset : offset + width] = y[i * section : (i + 1) * section]
        offset += width


def projection(x, w_qk, w_vz, w_ba, sections):
    rows = x.shape[0] // sections
    cols = w_qk.shape[1] + w_vz.shape[1] + w_ba.shape[1]
    return pl.pallas_call(
        projection_kernel,
        out_shape=[jax.ShapeDtypeStruct((rows, cols), jnp.float32)] * sections,
        cost_estimate=pl.CostEstimate(
            flops=2 * x.shape[0] * x.shape[1] * cols,
            bytes_accessed=2 * x.shape[1] * cols + 2 * x.size + 4 * x.shape[0] * cols,
            transcendentals=0,
        ),
    )(x, w_qk, w_vz, w_ba)


def recurrence_kernel(decay_ref, beta_ref, qt_ref, kt_ref, v_ref, s_ref, s_out, o_ref, *, heads, steps, ratio):
    r = pl.program_id(0)
    key_heads = heads // ratio
    for kh in range(key_heads):
        group = [kh * ratio + j for j in range(ratio)]
        states = [s_ref[0, h] for h in group]
        for t in range(steps):
            ck = t * key_heads + kh
            key_col = kt_ref[0, :, ck : ck + 1]
            query_col = qt_ref[0, :, ck : ck + 1]
            for j, h in enumerate(group):
                c = t * heads + h
                state = states[j] * decay_ref[r, c]
                recalled = jnp.sum(key_col * state, axis=0, keepdims=True)
                correction = (v_ref[0, c : c + 1, :] - recalled) * beta_ref[r, c]
                state = state + key_col * correction
                o_ref[0, c : c + 1, :] = jnp.sum(query_col * state, axis=0, keepdims=True)
                states[j] = state
        for j, h in enumerate(group):
            s_out[0, h] = states[j]


def recurrence(decay, beta, qt, kt, values, memory_state):
    rows, heads = memory_state.shape[0], memory_state.shape[1]
    cols = decay.shape[1]
    steps = cols // heads
    key_cols = kt.shape[2]
    kern = functools.partial(recurrence_kernel, heads=heads, steps=steps, ratio=cols // key_cols)
    return pl.pallas_call(
        kern,
        grid=(rows,),
        in_specs=[
            pl.BlockSpec(memory_space=pltpu.SMEM),
            pl.BlockSpec(memory_space=pltpu.SMEM),
            pl.BlockSpec((1, DK, key_cols), lambda r: (r, 0, 0)),
            pl.BlockSpec((1, DK, key_cols), lambda r: (r, 0, 0)),
            pl.BlockSpec((1, cols, DV), lambda r: (r, 0, 0)),
            pl.BlockSpec((1, heads, DK, DV), lambda r: (r, 0, 0, 0)),
        ],
        out_specs=[
            pl.BlockSpec((1, heads, DK, DV), lambda r: (r, 0, 0, 0)),
            pl.BlockSpec((1, cols, DV), lambda r: (r, 0, 0)),
        ],
        out_shape=[
            jax.ShapeDtypeStruct(memory_state.shape, jnp.float32),
            jax.ShapeDtypeStruct((rows, cols, DV), jnp.float32),
        ],
        cost_estimate=pl.CostEstimate(
            flops=8 * rows * cols * DK * DV,
            bytes_accessed=2 * memory_state.size * 4,
            transcendentals=0,
        ),
    )(decay, beta, qt, kt, values, memory_state)


def shards(
    activations,
    w_qk,
    w_vz,
    w_ba,
    conv_qk,
    conv_v,
    a_log,
    dt_bias,
    norm_gain,
    w_out,
    conv_state_qk,
    conv_state_v,
    memory_state,
):
    head_ratio = HV // HK
    step_count = activations.shape[1]
    rows_mem = memory_state.shape[0]
    heads = memory_state.shape[1]
    width_qk = w_qk.shape[1]
    width_vz = w_vz.shape[1]

    pieces = gather_pieces(activations, "head")
    n_head, rows_head = pieces.shape[0], pieces.shape[1]
    flat_pieces = pieces.reshape(-1, pieces.shape[-1])
    me_head = lax.axis_index("head")
    n_dp = lax.axis_size("dp")
    chips = n_dp // 2
    me_dp = lax.axis_index("dp")
    core, chip = me_dp % 2, me_dp // 2
    local_rows = jnp.arange(rows_mem)
    steps = jnp.arange(step_count)
    index_blocks = []
    for which in (1 - core, core):
        for s in range(chips):
            block = ((chip + s) % chips) * 2 + which
            rows = block * rows_mem + local_rows
            source = (me_head - rows // rows_head) % n_head
            flat = (source * rows_head + rows % rows_head)[:, None] * step_count + steps[None, :]
            index_blocks.append(flat.reshape(-1))
    flat_rows = jnp.take(flat_pieces, jnp.concatenate(index_blocks), axis=0)
    outs = projection(flat_rows, w_qk, w_vz, w_ba, 2 * chips)
    pair = [(i, i ^ 1) for i in range(n_dp)]
    part = [keep + lax.ppermute(send, "dp", pair) for send, keep in zip(outs[:chips], outs[chips:])]
    summed = part[0]
    for s in range(1, chips):
        perm = [(i, ((i // 2 + s) % chips) * 2 + i % 2) for i in range(n_dp)]
        summed = summed + lax.ppermute(part[s], "dp", perm)
    summed_qk = summed[:, :width_qk]
    summed_vz = summed[:, width_qk : width_qk + width_vz]
    summed_ba = summed[:, width_qk + width_vz :]
    qk_proj = summed_qk.astype(jnp.bfloat16).reshape(rows_mem, step_count, width_qk)
    vz_proj = summed_vz.astype(jnp.bfloat16).reshape(rows_mem, step_count, width_vz)
    ba_proj = summed_ba.astype(jnp.bfloat16).reshape(rows_mem, step_count, -1)

    split_vz = vz_proj.reshape(rows_mem, step_count, heads, 2, DV)
    values_now = split_vz[:, :, :, 0, :].reshape(rows_mem, step_count, heads * DV)
    gate_z = split_vz[:, :, :, 1, :].astype(jnp.float32)

    qk_conv = conv_steps(conv_state_qk, qk_proj, conv_qk).reshape(rows_mem, step_count, -1, 2, DK)
    v_conv = conv_steps(conv_state_v, values_now, conv_v).reshape(rows_mem, step_count * heads, DV)
    queries = normalize(qk_conv[:, :, :, 0, :]) * DK ** (-0.5)
    key_vec = normalize(qk_conv[:, :, :, 1, :])
    key_heads = queries.shape[2]
    assert key_heads * head_ratio == heads
    qt = queries.transpose(0, 3, 1, 2).reshape(rows_mem, DK, step_count * key_heads)
    kt = key_vec.transpose(0, 3, 1, 2).reshape(rows_mem, DK, step_count * key_heads)

    split_ba = ba_proj.reshape(rows_mem, step_count, heads, 2).astype(jnp.float32)
    beta_gate = jax.nn.sigmoid(split_ba[..., 0])
    log_decay = -jnp.exp(a_log)[None, None, :] * jax.nn.softplus(split_ba[..., 1] + dt_bias[None, None, :])
    decay = jnp.exp(log_decay).reshape(rows_mem, step_count * heads)
    beta_gate = beta_gate.reshape(rows_mem, step_count * heads)

    new_state, readout = recurrence(decay, beta_gate, qt, kt, v_conv, memory_state)
    readout = readout.reshape(rows_mem, step_count, heads, DV)

    scale = lax.rsqrt(jnp.mean(readout * readout, axis=-1, keepdims=True) + 1e-06)
    normed = readout * scale * norm_gain[None, None, None, :] * jax.nn.silu(gate_z)
    normed = normed.reshape(rows_mem, step_count, heads * DV).astype(jnp.bfloat16)

    all_normed = gather_rows(normed, "dp")
    partials = jnp.dot(
        all_normed.reshape(-1, all_normed.shape[-1]), w_out, preferred_element_type=jnp.float32
    )
    layer_out = scatter_sum_rows(partials, "head")
    layer_out = layer_out.astype(jnp.bfloat16).reshape(-1, step_count, w_out.shape[1])
    return (layer_out, new_state)


def solution(mesh):
    in_specs = (
        P(("groups", "head"), None, "dp"),
        P("dp", "head"),
        P("dp", "head"),
        P("dp", "head"),
        P(None, "head"),
        P(None, "head"),
        P("head"),
        P("head"),
        P(),
        P("head", "dp"),
        P(("groups", "dp"), None, "head"),
        P(("groups", "dp"), None, "head"),
        P(("groups", "dp"), "head", None, None),
    )
    out_specs = (P(("groups", "head"), None, "dp"), P(("groups", "dp"), "head", None, None))
    return jax.shard_map(shards, mesh=mesh, in_specs=in_specs, out_specs=out_specs, check_vma=False)
```

```python
import functools

import jax
import jax.numpy as jnp
from jax import lax
from jax.experimental import pallas as pl
from jax.experimental.pallas import tpu as pltpu
from jax.sharding import PartitionSpec as P

HK = 16
HV = 32
DK = 128
DV = 128


def normalize(vectors):
    return vectors * lax.rsqrt(jnp.sum(vectors * vectors, axis=-1, keepdims=True) + 1e-06)


def conv_steps(state, proj, taps):
    seq = jnp.concatenate([state, proj], axis=1).astype(jnp.float32)
    taps = taps.astype(jnp.float32)
    kernel = taps.shape[0]
    steps = proj.shape[1]
    mixed = sum(seq[:, k : k + steps, :] * taps[k][None, None, :] for k in range(kernel))
    return jax.nn.silu(mixed)


def gather_rows(x, axis):
    n = lax.axis_size(axis)
    me = lax.axis_index(axis)
    pieces = [x]
    for s in range(1, n):
        pieces.append(lax.ppermute(x, axis, [(i, (i + s) % n) for i in range(n)]))
    stacked = jnp.stack(pieces)
    order = (me - jnp.arange(n)) % n
    return jnp.take(stacked, order, axis=0).reshape(n * x.shape[0], *x.shape[1:])


def scatter_sum_rows(x, axis):
    n = lax.axis_size(axis)
    me = lax.axis_index(axis)
    chunks = x.reshape(n, x.shape[0] // n, *x.shape[1:])
    acc = jnp.take(chunks, me, axis=0)
    for s in range(1, n):
        send = jnp.take(chunks, (me + s) % n, axis=0)
        acc = acc + lax.ppermute(send, axis, [(i, (i + s) % n) for i in range(n)])
    return acc


def scatter_sum_rows_paired(x, axis):
    n = lax.axis_size(axis)
    m = n // 2
    me = lax.axis_index(axis)
    core = me % 2
    chip = me // 2
    chunks = x.reshape(m, 2, x.shape[0] // n, *x.shape[1:])
    keep = jnp.take(chunks, core, axis=1)
    send = jnp.take(chunks, 1 - core, axis=1)
    part = keep + lax.ppermute(send, axis, [(i, i ^ 1) for i in range(n)])
    acc = jnp.take(part, chip, axis=0)
    for s in range(1, m):
        send = jnp.take(part, (chip + s) % m, axis=0)
        perm = [(i, ((i // 2 + s) % m) * 2 + i % 2) for i in range(n)]
        acc = acc + lax.ppermute(send, axis, perm)
    return acc


def gather_pieces(x, axis):
    n = lax.axis_size(axis)
    pieces = [x]
    for s in range(1, n):
        pieces.append(lax.ppermute(x, axis, [(i, (i + s) % n) for i in range(n)]))
    return jnp.stack(pieces)


def projection_kernel(x_ref, wqk_ref, wvz_ref, wba_ref, *outs):
    x = x_ref[...]
    section = outs[0].shape[0]
    offset = 0
    for w_ref in (wqk_ref, wvz_ref, wba_ref):
        width = w_ref.shape[1]
        y = jnp.dot(x, w_ref[...], preferred_element_type=jnp.float32)
        for i, o_ref in enumerate(outs):
            o_ref[:, offset : offset + width] = y[i * section : (i + 1) * section]
        offset += width


def projection(x, w_qk, w_vz, w_ba, sections):
    rows = x.shape[0] // sections
    cols = w_qk.shape[1] + w_vz.shape[1] + w_ba.shape[1]
    return pl.pallas_call(
        projection_kernel,
        out_shape=[jax.ShapeDtypeStruct((rows, cols), jnp.float32)] * sections,
        cost_estimate=pl.CostEstimate(
            flops=2 * x.shape[0] * x.shape[1] * cols,
            bytes_accessed=2 * x.shape[1] * cols + 2 * x.size + 4 * x.shape[0] * cols,
            transcendentals=0,
        ),
    )(x, w_qk, w_vz, w_ba)


def recurrence_kernel(gates_ref, qt_ref, kt_ref, v_ref, s_ref, s_out, o_ref, *, heads, steps, ratio):
    r = pl.program_id(0)
    key_heads = heads // ratio
    cols = heads * steps
    for kh in range(key_heads):
        group = [kh * ratio + j for j in range(ratio)]
        states = [s_ref[0, h] for h in group]
        for t in range(steps):
            ck = t * key_heads + kh
            key_col = kt_ref[0, :, ck : ck + 1]
            query_col = qt_ref[0, :, ck : ck + 1]
            for j, h in enumerate(group):
                c = t * heads + h
                lanes = slice(h * DV, (h + 1) * DV)
                state = states[j] * gates_ref[r, cols + c]
                recalled = jnp.sum(key_col * state, axis=0, keepdims=True)
                correction = (v_ref[0, t : t + 1, lanes] - recalled) * gates_ref[r, c]
                state = state + key_col * correction
                o_ref[0, t : t + 1, lanes] = jnp.sum(query_col * state, axis=0, keepdims=True)
                states[j] = state
        for j, h in enumerate(group):
            s_out[0, h] = states[j]


def recurrence(gates, qt, kt, values, memory_state):
    rows, heads = memory_state.shape[0], memory_state.shape[1]
    steps = values.shape[1]
    key_cols = kt.shape[2]
    ratio = heads * steps // key_cols
    kern = functools.partial(recurrence_kernel, heads=heads, steps=steps, ratio=ratio)
    return pl.pallas_call(
        kern,
        grid=(rows,),
        in_specs=[
            pl.BlockSpec(memory_space=pltpu.SMEM),
            pl.BlockSpec((1, DK, key_cols), lambda r: (r, 0, 0)),
            pl.BlockSpec((1, DK, key_cols), lambda r: (r, 0, 0)),
            pl.BlockSpec((1, steps, heads * DV), lambda r: (r, 0, 0)),
            pl.BlockSpec((1, heads, DK, DV), lambda r: (r, 0, 0, 0)),
        ],
        out_specs=[
            pl.BlockSpec((1, heads, DK, DV), lambda r: (r, 0, 0, 0)),
            pl.BlockSpec((1, steps, heads * DV), lambda r: (r, 0, 0)),
        ],
        out_shape=[
            jax.ShapeDtypeStruct(memory_state.shape, jnp.float32),
            jax.ShapeDtypeStruct((rows, steps, heads * DV), jnp.float32),
        ],
        cost_estimate=pl.CostEstimate(
            flops=8 * rows * heads * steps * DK * DV,
            bytes_accessed=2 * memory_state.size * 4,
            transcendentals=0,
        ),
    )(gates, qt, kt, values, memory_state)


def shards(
    activations,
    w_qk,
    w_vz,
    w_ba,
    conv_qk,
    conv_v,
    a_log,
    dt_bias,
    norm_gain,
    w_out,
    conv_state_qk,
    conv_state_v,
    memory_state,
):
    head_ratio = HV // HK
    step_count = activations.shape[1]
    rows_mem = memory_state.shape[0]
    heads = memory_state.shape[1]
    width_qk = w_qk.shape[1]
    width_vz = w_vz.shape[1]

    pieces = gather_pieces(activations, "head")
    n_head, rows_head = pieces.shape[0], pieces.shape[1]
    flat_pieces = pieces.reshape(-1, pieces.shape[-1])
    me_head = lax.axis_index("head")
    n_dp = lax.axis_size("dp")
    chips = n_dp // 2
    me_dp = lax.axis_index("dp")
    core, chip = me_dp % 2, me_dp // 2
    local_rows = jnp.arange(rows_mem)
    steps = jnp.arange(step_count)
    index_blocks = []
    for which in (1 - core, core):
        for s in range(chips):
            block = ((chip + s) % chips) * 2 + which
            rows = block * rows_mem + local_rows
            source = (me_head - rows // rows_head) % n_head
            flat = (source * rows_head + rows % rows_head)[:, None] * step_count + steps[None, :]
            index_blocks.append(flat.reshape(-1))
    flat_rows = jnp.take(flat_pieces, jnp.concatenate(index_blocks), axis=0)
    outs = projection(flat_rows, w_qk, w_vz, w_ba, 2 * chips)
    pair = [(i, i ^ 1) for i in range(n_dp)]
    part = [keep + lax.ppermute(send, "dp", pair) for send, keep in zip(outs[:chips], outs[chips:])]
    summed = part[0]
    for s in range(1, chips):
        perm = [(i, ((i // 2 + s) % chips) * 2 + i % 2) for i in range(n_dp)]
        summed = summed + lax.ppermute(part[s], "dp", perm)
    summed_qk = summed[:, :width_qk]
    summed_vz = summed[:, width_qk : width_qk + width_vz]
    summed_ba = summed[:, width_qk + width_vz :]
    qk_proj = summed_qk.astype(jnp.bfloat16).reshape(rows_mem, step_count, width_qk)
    vz_proj = summed_vz.astype(jnp.bfloat16).reshape(rows_mem, step_count, width_vz)
    ba_proj = summed_ba.astype(jnp.bfloat16).reshape(rows_mem, step_count, -1)

    split_vz = vz_proj.reshape(rows_mem, step_count, heads, 2, DV)
    values_now = split_vz[:, :, :, 0, :].reshape(rows_mem, step_count, heads * DV)
    gate_z = split_vz[:, :, :, 1, :].astype(jnp.float32)

    qk_conv = conv_steps(conv_state_qk, qk_proj, conv_qk).reshape(rows_mem, step_count, -1, 2, DK)
    v_conv = conv_steps(conv_state_v, values_now, conv_v)
    queries = normalize(qk_conv[:, :, :, 0, :]) * DK ** (-0.5)
    key_vec = normalize(qk_conv[:, :, :, 1, :])
    key_heads = queries.shape[2]
    assert key_heads * head_ratio == heads
    qt = queries.transpose(0, 3, 1, 2).reshape(rows_mem, DK, step_count * key_heads)
    kt = key_vec.transpose(0, 3, 1, 2).reshape(rows_mem, DK, step_count * key_heads)

    split_ba = ba_proj.reshape(rows_mem, step_count, heads, 2).astype(jnp.float32)
    beta_gate = jax.nn.sigmoid(split_ba[..., 0])
    log_decay = -jnp.exp(a_log)[None, None, :] * jax.nn.softplus(split_ba[..., 1] + dt_bias[None, None, :])
    gates = jnp.concatenate(
        [beta_gate.reshape(rows_mem, -1), jnp.exp(log_decay).reshape(rows_mem, -1)], axis=1
    )

    new_state, readout = recurrence(gates, qt, kt, v_conv, memory_state)
    readout = readout.reshape(rows_mem, step_count, heads, DV)

    scale = lax.rsqrt(jnp.mean(readout * readout, axis=-1, keepdims=True) + 1e-06)
    normed = readout * scale * norm_gain[None, None, None, :] * jax.nn.silu(gate_z)
    normed = normed.reshape(rows_mem, step_count, heads * DV).astype(jnp.bfloat16)

    all_normed = gather_rows(normed, "dp")
    partials = jnp.dot(
        all_normed.reshape(-1, all_normed.shape[-1]), w_out, preferred_element_type=jnp.float32
    )
    layer_out = scatter_sum_rows(partials, "head")
    layer_out = layer_out.astype(jnp.bfloat16).reshape(-1, step_count, w_out.shape[1])
    return (layer_out, new_state)


def solution(mesh):
    in_specs = (
        P(("groups", "head"), None, "dp"),
        P("dp", "head"),
        P("dp", "head"),
        P("dp", "head"),
        P(None, "head"),
        P(None, "head"),
        P("head"),
        P("head"),
        P(),
        P("head", "dp"),
        P(("groups", "dp"), None, "head"),
        P(("groups", "dp"), None, "head"),
        P(("groups", "dp"), "head", None, None),
    )
    out_specs = (P(("groups", "head"), None, "dp"), P(("groups", "dp"), "head", None, None))
    return jax.shard_map(shards, mesh=mesh, in_specs=in_specs, out_specs=out_specs, check_vma=False)
```

```python
import functools

import jax
import jax.numpy as jnp
from jax import lax
from jax.experimental import pallas as pl
from jax.experimental.pallas import tpu as pltpu
from jax.sharding import PartitionSpec as P

HK = 16
HV = 32
DK = 128
DV = 128


def normalize(vectors):
    return vectors * lax.rsqrt(jnp.sum(vectors * vectors, axis=-1, keepdims=True) + 1e-06)


def conv_steps(state, proj, taps):
    seq = jnp.concatenate([state, proj], axis=1).astype(jnp.float32)
    taps = taps.astype(jnp.float32)
    kernel = taps.shape[0]
    steps = proj.shape[1]
    mixed = sum(seq[:, k : k + steps, :] * taps[k][None, None, :] for k in range(kernel))
    return jax.nn.silu(mixed)


def gather_rows(x, axis):
    n = lax.axis_size(axis)
    me = lax.axis_index(axis)
    pieces = [x]
    for s in range(1, n):
        pieces.append(lax.ppermute(x, axis, [(i, (i + s) % n) for i in range(n)]))
    stacked = jnp.stack(pieces)
    order = (me - jnp.arange(n)) % n
    return jnp.take(stacked, order, axis=0).reshape(n * x.shape[0], *x.shape[1:])


def scatter_sum_rows(x, axis):
    n = lax.axis_size(axis)
    me = lax.axis_index(axis)
    chunks = x.reshape(n, x.shape[0] // n, *x.shape[1:])
    acc = jnp.take(chunks, me, axis=0)
    for s in range(1, n):
        send = jnp.take(chunks, (me + s) % n, axis=0)
        acc = acc + lax.ppermute(send, axis, [(i, (i + s) % n) for i in range(n)])
    return acc


def scatter_sum_rows_paired(x, axis):
    n = lax.axis_size(axis)
    m = n // 2
    me = lax.axis_index(axis)
    core = me % 2
    chip = me // 2
    chunks = x.reshape(m, 2, x.shape[0] // n, *x.shape[1:])
    keep = jnp.take(chunks, core, axis=1)
    send = jnp.take(chunks, 1 - core, axis=1)
    part = keep + lax.ppermute(send, axis, [(i, i ^ 1) for i in range(n)])
    acc = jnp.take(part, chip, axis=0)
    for s in range(1, m):
        send = jnp.take(part, (chip + s) % m, axis=0)
        perm = [(i, ((i // 2 + s) % m) * 2 + i % 2) for i in range(n)]
        acc = acc + lax.ppermute(send, axis, perm)
    return acc


def gather_pieces(x, axis):
    n = lax.axis_size(axis)
    pieces = [x]
    for s in range(1, n):
        pieces.append(lax.ppermute(x, axis, [(i, (i + s) % n) for i in range(n)]))
    return jnp.stack(pieces)


def projection_kernel(x_ref, wqk_ref, wvz_ref, wba_ref, *outs):
    x = x_ref[...]
    section = outs[0].shape[0]
    offset = 0
    for w_ref in (wqk_ref, wvz_ref, wba_ref):
        width = w_ref.shape[1]
        y = jnp.dot(x, w_ref[...], preferred_element_type=jnp.float32)
        for i, o_ref in enumerate(outs):
            o_ref[:, offset : offset + width] = y[i * section : (i + 1) * section]
        offset += width


def projection(x, w_qk, w_vz, w_ba, sections):
    rows = x.shape[0] // sections
    cols = w_qk.shape[1] + w_vz.shape[1] + w_ba.shape[1]
    return pl.pallas_call(
        projection_kernel,
        out_shape=[jax.ShapeDtypeStruct((rows, cols), jnp.float32)] * sections,
        cost_estimate=pl.CostEstimate(
            flops=2 * x.shape[0] * x.shape[1] * cols,
            bytes_accessed=2 * x.shape[1] * cols + 2 * x.size + 4 * x.shape[0] * cols,
            transcendentals=0,
        ),
    )(x, w_qk, w_vz, w_ba)


def recurrence_kernel(gates_ref, qt_ref, kt_ref, v_ref, s_ref, s_out, o_ref, *, heads, steps, ratio):
    r = pl.program_id(0)
    key_heads = heads // ratio
    cols = heads * steps
    for kh in range(key_heads):
        group = [kh * ratio + j for j in range(ratio)]
        states = [s_ref[0, h] for h in group]
        for t in range(steps):
            ck = t * key_heads + kh
            key_col = kt_ref[0, :, ck : ck + 1]
            query_col = qt_ref[0, :, ck : ck + 1]
            for j, h in enumerate(group):
                c = t * heads + h
                lanes = slice(h * DV, (h + 1) * DV)
                state = states[j] * gates_ref[r, cols + c]
                recalled = jnp.sum(key_col * state, axis=0, keepdims=True)
                correction = (v_ref[0, t : t + 1, lanes] - recalled) * gates_ref[r, c]
                state = state + key_col * correction
                o_ref[0, t : t + 1, lanes] = jnp.sum(query_col * state, axis=0, keepdims=True)
                states[j] = state
        for j, h in enumerate(group):
            s_out[0, h] = states[j]


def recurrence(gates, qt, kt, values, memory_state):
    rows, heads = memory_state.shape[0], memory_state.shape[1]
    steps = values.shape[1]
    key_cols = kt.shape[2]
    ratio = heads * steps // key_cols
    kern = functools.partial(recurrence_kernel, heads=heads, steps=steps, ratio=ratio)
    return pl.pallas_call(
        kern,
        grid=(rows,),
        in_specs=[
            pl.BlockSpec(memory_space=pltpu.SMEM),
            pl.BlockSpec((1, DK, key_cols), lambda r: (r, 0, 0)),
            pl.BlockSpec((1, DK, key_cols), lambda r: (r, 0, 0)),
            pl.BlockSpec((1, steps, heads * DV), lambda r: (r, 0, 0)),
            pl.BlockSpec((1, heads, DK, DV), lambda r: (r, 0, 0, 0)),
        ],
        out_specs=[
            pl.BlockSpec((1, heads, DK, DV), lambda r: (r, 0, 0, 0)),
            pl.BlockSpec((1, steps, heads * DV), lambda r: (r, 0, 0)),
        ],
        out_shape=[
            jax.ShapeDtypeStruct(memory_state.shape, jnp.float32),
            jax.ShapeDtypeStruct((rows, steps, heads * DV), jnp.float32),
        ],
        cost_estimate=pl.CostEstimate(
            flops=8 * rows * heads * steps * DK * DV,
            bytes_accessed=2 * memory_state.size * 4,
            transcendentals=0,
        ),
    )(gates, qt, kt, values, memory_state)


def shards(
    activations,
    w_qk,
    w_vz,
    w_ba,
    conv_qk,
    conv_v,
    a_log,
    dt_bias,
    norm_gain,
    w_out,
    conv_state_qk,
    conv_state_v,
    memory_state,
):
    head_ratio = HV // HK
    step_count = activations.shape[1]
    rows_mem = memory_state.shape[0]
    heads = memory_state.shape[1]
    width_qk = w_qk.shape[1]
    width_vz = w_vz.shape[1]

    pieces = gather_pieces(activations, "head")
    n_head, rows_head = pieces.shape[0], pieces.shape[1]
    flat_pieces = pieces.reshape(-1, pieces.shape[-1])
    me_head = lax.axis_index("head")
    n_dp = lax.axis_size("dp")
    chips = n_dp // 2
    me_dp = lax.axis_index("dp")
    core, chip = me_dp % 2, me_dp // 2
    local_rows = jnp.arange(rows_mem)
    steps = jnp.arange(step_count)
    index_blocks = []
    for which in (1 - core, core):
        for s in range(chips):
            block = ((chip + s) % chips) * 2 + which
            rows = block * rows_mem + local_rows
            source = (me_head - rows // rows_head) % n_head
            flat = (source * rows_head + rows % rows_head)[:, None] * step_count + steps[None, :]
            index_blocks.append(flat.reshape(-1))
    flat_rows = jnp.take(flat_pieces, jnp.concatenate(index_blocks), axis=0)
    outs = projection(flat_rows, w_qk, w_vz, w_ba, 2 * chips)
    pair = [(i, i ^ 1) for i in range(n_dp)]
    part = [keep + lax.ppermute(send, "dp", pair) for send, keep in zip(outs[:chips], outs[chips:])]
    summed_qk = part[0][:, :width_qk]
    summed_rest = part[0][:, width_qk:]
    for s in range(1, chips):
        perm = [(i, ((i // 2 + s) % chips) * 2 + i % 2) for i in range(n_dp)]
        summed_qk = summed_qk + lax.ppermute(part[s][:, :width_qk], "dp", perm)
        summed_rest = summed_rest + lax.ppermute(part[s][:, width_qk:], "dp", perm)
    summed_vz = summed_rest[:, :width_vz]
    summed_ba = summed_rest[:, width_vz:]
    qk_proj = summed_qk.astype(jnp.bfloat16).reshape(rows_mem, step_count, width_qk)
    vz_proj = summed_vz.astype(jnp.bfloat16).reshape(rows_mem, step_count, width_vz)
    ba_proj = summed_ba.astype(jnp.bfloat16).reshape(rows_mem, step_count, -1)

    split_vz = vz_proj.reshape(rows_mem, step_count, heads, 2, DV)
    values_now = split_vz[:, :, :, 0, :].reshape(rows_mem, step_count, heads * DV)
    gate_z = split_vz[:, :, :, 1, :].astype(jnp.float32)

    qk_conv = conv_steps(conv_state_qk, qk_proj, conv_qk).reshape(rows_mem, step_count, -1, 2, DK)
    v_conv = conv_steps(conv_state_v, values_now, conv_v)
    queries = normalize(qk_conv[:, :, :, 0, :]) * DK ** (-0.5)
    key_vec = normalize(qk_conv[:, :, :, 1, :])
    key_heads = queries.shape[2]
    assert key_heads * head_ratio == heads
    qt = queries.transpose(0, 3, 1, 2).reshape(rows_mem, DK, step_count * key_heads)
    kt = key_vec.transpose(0, 3, 1, 2).reshape(rows_mem, DK, step_count * key_heads)

    split_ba = ba_proj.reshape(rows_mem, step_count, heads, 2).astype(jnp.float32)
    beta_gate = jax.nn.sigmoid(split_ba[..., 0])
    log_decay = -jnp.exp(a_log)[None, None, :] * jax.nn.softplus(split_ba[..., 1] + dt_bias[None, None, :])
    gates = jnp.concatenate(
        [beta_gate.reshape(rows_mem, -1), jnp.exp(log_decay).reshape(rows_mem, -1)], axis=1
    )

    new_state, readout = recurrence(gates, qt, kt, v_conv, memory_state)
    readout = readout.reshape(rows_mem, step_count, heads, DV)

    scale = lax.rsqrt(jnp.mean(readout * readout, axis=-1, keepdims=True) + 1e-06)
    normed = readout * scale * norm_gain[None, None, None, :] * jax.nn.silu(gate_z)
    normed = normed.reshape(rows_mem, step_count, heads * DV).astype(jnp.bfloat16)

    all_normed = gather_rows(normed, "dp")
    partials = jnp.dot(
        all_normed.reshape(-1, all_normed.shape[-1]), w_out, preferred_element_type=jnp.float32
    )
    layer_out = scatter_sum_rows(partials, "head")
    layer_out = layer_out.astype(jnp.bfloat16).reshape(-1, step_count, w_out.shape[1])
    return (layer_out, new_state)


def solution(mesh):
    in_specs = (
        P(("groups", "head"), None, "dp"),
        P("dp", "head"),
        P("dp", "head"),
        P("dp", "head"),
        P(None, "head"),
        P(None, "head"),
        P("head"),
        P("head"),
        P(),
        P("head", "dp"),
        P(("groups", "dp"), None, "head"),
        P(("groups", "dp"), None, "head"),
        P(("groups", "dp"), "head", None, None),
    )
    out_specs = (P(("groups", "head"), None, "dp"), P(("groups", "dp"), "head", None, None))
    return jax.shard_map(shards, mesh=mesh, in_specs=in_specs, out_specs=out_specs, check_vma=False)
```

```python
import functools

import jax
import jax.numpy as jnp
from jax import lax
from jax.experimental import pallas as pl
from jax.experimental.pallas import tpu as pltpu
from jax.sharding import PartitionSpec as P

HK = 16
HV = 32
DK = 128
DV = 128


def normalize(vectors):
    return vectors * lax.rsqrt(jnp.sum(vectors * vectors, axis=-1, keepdims=True) + 1e-06)


def conv_steps(state, proj, taps):
    seq = jnp.concatenate([state, proj], axis=1).astype(jnp.float32)
    taps = taps.astype(jnp.float32)
    kernel = taps.shape[0]
    steps = proj.shape[1]
    mixed = sum(seq[:, k : k + steps, :] * taps[k][None, None, :] for k in range(kernel))
    return jax.nn.silu(mixed)


def gather_rows(x, axis):
    n = lax.axis_size(axis)
    me = lax.axis_index(axis)
    pieces = [x]
    for s in range(1, n):
        pieces.append(lax.ppermute(x, axis, [(i, (i + s) % n) for i in range(n)]))
    stacked = jnp.stack(pieces)
    order = (me - jnp.arange(n)) % n
    return jnp.take(stacked, order, axis=0, mode="clip").reshape(n * x.shape[0], *x.shape[1:])


def scatter_sum_rows(x, axis):
    n = lax.axis_size(axis)
    me = lax.axis_index(axis)
    chunks = x.reshape(n, x.shape[0] // n, *x.shape[1:])
    acc = jnp.take(chunks, me, axis=0)
    for s in range(1, n):
        send = jnp.take(chunks, (me + s) % n, axis=0)
        acc = acc + lax.ppermute(send, axis, [(i, (i + s) % n) for i in range(n)])
    return acc


def scatter_sum_rows_paired(x, axis):
    n = lax.axis_size(axis)
    m = n // 2
    me = lax.axis_index(axis)
    core = me % 2
    chip = me // 2
    chunks = x.reshape(m, 2, x.shape[0] // n, *x.shape[1:])
    keep = jnp.take(chunks, core, axis=1)
    send = jnp.take(chunks, 1 - core, axis=1)
    part = keep + lax.ppermute(send, axis, [(i, i ^ 1) for i in range(n)])
    acc = jnp.take(part, chip, axis=0)
    for s in range(1, m):
        send = jnp.take(part, (chip + s) % m, axis=0)
        perm = [(i, ((i // 2 + s) % m) * 2 + i % 2) for i in range(n)]
        acc = acc + lax.ppermute(send, axis, perm)
    return acc


def gather_pieces(x, axis):
    n = lax.axis_size(axis)
    pieces = [x]
    for s in range(1, n):
        pieces.append(lax.ppermute(x, axis, [(i, (i + s) % n) for i in range(n)]))
    return jnp.stack(pieces)


def projection_kernel(x_ref, wqk_ref, wvz_ref, wba_t_ref, *outs):
    x = x_ref[...]
    section = outs[0].shape[0]
    offset = 0
    for w_ref, transposed in ((wqk_ref, False), (wvz_ref, False), (wba_t_ref, True)):
        width = w_ref.shape[0 if transposed else 1]
        contract = 1 if transposed else 0
        y = lax.dot_general(
            x, w_ref[...], (((1,), (contract,)), ((), ())), preferred_element_type=jnp.float32
        )
        for i, o_ref in enumerate(outs):
            o_ref[:, offset : offset + width] = y[i * section : (i + 1) * section]
        offset += width


def projection(x, w_qk, w_vz, w_ba, sections):
    rows = x.shape[0] // sections
    cols = w_qk.shape[1] + w_vz.shape[1] + w_ba.shape[1]
    return pl.pallas_call(
        projection_kernel,
        out_shape=[jax.ShapeDtypeStruct((rows, cols), jnp.float32)] * sections,
        cost_estimate=pl.CostEstimate(
            flops=2 * x.shape[0] * x.shape[1] * cols,
            bytes_accessed=2 * x.shape[1] * cols + 2 * x.size + 4 * x.shape[0] * cols,
            transcendentals=0,
        ),
    )(x, w_qk, w_vz, w_ba.T)


def recurrence_kernel(gates_ref, qt_ref, kt_ref, v_ref, s_ref, s_out, o_ref, *, heads, steps, ratio):
    r = pl.program_id(0)
    key_heads = heads // ratio
    cols = heads * steps
    for kh in range(key_heads):
        group = [kh * ratio + j for j in range(ratio)]
        states = [s_ref[0, h] for h in group]
        for t in range(steps):
            ck = t * key_heads + kh
            key_col = kt_ref[0, :, ck : ck + 1]
            query_col = qt_ref[0, :, ck : ck + 1]
            for j, h in enumerate(group):
                c = t * heads + h
                lanes = slice(h * DV, (h + 1) * DV)
                state = states[j] * gates_ref[r, cols + c]
                recalled = jnp.sum(key_col * state, axis=0, keepdims=True)
                correction = (v_ref[0, t : t + 1, lanes] - recalled) * gates_ref[r, c]
                state = state + key_col * correction
                o_ref[0, t : t + 1, lanes] = jnp.sum(query_col * state, axis=0, keepdims=True)
                states[j] = state
        for j, h in enumerate(group):
            s_out[0, h] = states[j]


def recurrence(gates, qt, kt, values, memory_state):
    rows, heads = memory_state.shape[0], memory_state.shape[1]
    steps = values.shape[1]
    key_cols = kt.shape[2]
    ratio = heads * steps // key_cols
    kern = functools.partial(recurrence_kernel, heads=heads, steps=steps, ratio=ratio)
    return pl.pallas_call(
        kern,
        grid=(rows,),
        in_specs=[
            pl.BlockSpec(memory_space=pltpu.SMEM),
            pl.BlockSpec((1, DK, key_cols), lambda r: (r, 0, 0)),
            pl.BlockSpec((1, DK, key_cols), lambda r: (r, 0, 0)),
            pl.BlockSpec((1, steps, heads * DV), lambda r: (r, 0, 0)),
            pl.BlockSpec((1, heads, DK, DV), lambda r: (r, 0, 0, 0)),
        ],
        out_specs=[
            pl.BlockSpec((1, heads, DK, DV), lambda r: (r, 0, 0, 0)),
            pl.BlockSpec((1, steps, heads * DV), lambda r: (r, 0, 0)),
        ],
        out_shape=[
            jax.ShapeDtypeStruct(memory_state.shape, jnp.float32),
            jax.ShapeDtypeStruct((rows, steps, heads * DV), jnp.float32),
        ],
        cost_estimate=pl.CostEstimate(
            flops=8 * rows * heads * steps * DK * DV,
            bytes_accessed=2 * memory_state.size * 4,
            transcendentals=0,
        ),
    )(gates, qt, kt, values, memory_state)


def shards(
    activations,
    w_qk,
    w_vz,
    w_ba,
    conv_qk,
    conv_v,
    a_log,
    dt_bias,
    norm_gain,
    w_out,
    conv_state_qk,
    conv_state_v,
    memory_state,
):
    head_ratio = HV // HK
    step_count = activations.shape[1]
    rows_mem = memory_state.shape[0]
    heads = memory_state.shape[1]
    width_qk = w_qk.shape[1]
    width_vz = w_vz.shape[1]

    pieces = gather_pieces(activations, "head")
    n_head, rows_head = pieces.shape[0], pieces.shape[1]
    me_head = lax.axis_index("head")
    n_dp = lax.axis_size("dp")
    chips = n_dp // 2
    me_dp = lax.axis_index("dp")
    core, chip = me_dp % 2, me_dp // 2
    assert rows_head % rows_mem == 0
    sections = []
    for which in (1 - core, core):
        for s in range(chips):
            block = ((chip + s) % chips) * 2 + which
            first = block * rows_mem
            source = (me_head - first // rows_head) % n_head
            offset = first % rows_head
            picked = pieces[0]
            for shift in range(1, n_head):
                picked = jnp.where(source == shift, pieces[shift], picked)
            picked = lax.dynamic_slice_in_dim(picked, offset, rows_mem, axis=0)
            sections.append(picked.reshape(rows_mem * step_count, -1))
    flat_rows = jnp.concatenate(sections, axis=0)
    outs = projection(flat_rows, w_qk, w_vz, w_ba, 2 * chips)
    pair = [(i, i ^ 1) for i in range(n_dp)]
    part = [keep + lax.ppermute(send, "dp", pair) for send, keep in zip(outs[:chips], outs[chips:])]
    summed_qk = part[0][:, :width_qk]
    summed_rest = part[0][:, width_qk:]
    for s in range(1, chips):
        perm = [(i, ((i // 2 + s) % chips) * 2 + i % 2) for i in range(n_dp)]
        summed_qk = summed_qk + lax.ppermute(part[s][:, :width_qk], "dp", perm)
        summed_rest = summed_rest + lax.ppermute(part[s][:, width_qk:], "dp", perm)
    summed_vz = summed_rest[:, :width_vz]
    summed_ba = summed_rest[:, width_vz:]
    qk_proj = summed_qk.astype(jnp.bfloat16).reshape(rows_mem, step_count, width_qk)
    vz_proj = summed_vz.astype(jnp.bfloat16).reshape(rows_mem, step_count, width_vz)
    ba_proj = summed_ba.astype(jnp.bfloat16).reshape(rows_mem, step_count, -1)

    split_vz = vz_proj.reshape(rows_mem, step_count, heads, 2, DV)
    values_now = split_vz[:, :, :, 0, :].reshape(rows_mem, step_count, heads * DV)
    gate_z = split_vz[:, :, :, 1, :].astype(jnp.float32)

    qk_conv = conv_steps(conv_state_qk, qk_proj, conv_qk).reshape(rows_mem, step_count, -1, 2, DK)
    v_conv = conv_steps(conv_state_v, values_now, conv_v)
    queries = normalize(qk_conv[:, :, :, 0, :]) * DK ** (-0.5)
    key_vec = normalize(qk_conv[:, :, :, 1, :])
    key_heads = queries.shape[2]
    assert key_heads * head_ratio == heads
    qt = queries.transpose(0, 3, 1, 2).reshape(rows_mem, DK, step_count * key_heads)
    kt = key_vec.transpose(0, 3, 1, 2).reshape(rows_mem, DK, step_count * key_heads)

    split_ba = ba_proj.reshape(rows_mem, step_count, heads, 2).astype(jnp.float32)
    beta_gate = jax.nn.sigmoid(split_ba[..., 0])
    log_decay = -jnp.exp(a_log)[None, None, :] * jax.nn.softplus(split_ba[..., 1] + dt_bias[None, None, :])
    gates = jnp.concatenate(
        [beta_gate.reshape(rows_mem, -1), jnp.exp(log_decay).reshape(rows_mem, -1)], axis=1
    )

    new_state, readout = recurrence(gates, qt, kt, v_conv, memory_state)
    readout = readout.reshape(rows_mem, step_count, heads, DV)

    scale = lax.rsqrt(jnp.mean(readout * readout, axis=-1, keepdims=True) + 1e-06)
    normed = readout * scale * norm_gain[None, None, None, :] * jax.nn.silu(gate_z)
    normed = normed.reshape(rows_mem, step_count, heads * DV).astype(jnp.bfloat16)

    all_normed = gather_rows(normed, "dp")
    partials = jnp.dot(
        all_normed.reshape(-1, all_normed.shape[-1]), w_out, preferred_element_type=jnp.float32
    )
    layer_out = scatter_sum_rows(partials, "head")
    layer_out = layer_out.astype(jnp.bfloat16).reshape(-1, step_count, w_out.shape[1])
    return (layer_out, new_state)


def solution(mesh):
    in_specs = (
        P(("groups", "head"), None, "dp"),
        P("dp", "head"),
        P("dp", "head"),
        P("dp", "head"),
        P(None, "head"),
        P(None, "head"),
        P("head"),
        P("head"),
        P(),
        P("head", "dp"),
        P(("groups", "dp"), None, "head"),
        P(("groups", "dp"), None, "head"),
        P(("groups", "dp"), "head", None, None),
    )
    out_specs = (P(("groups", "head"), None, "dp"), P(("groups", "dp"), "head", None, None))
    return jax.shard_map(shards, mesh=mesh, in_specs=in_specs, out_specs=out_specs, check_vma=False)
```

```python
import functools

import jax
import jax.numpy as jnp
from jax import lax
from jax.experimental import pallas as pl
from jax.experimental.pallas import tpu as pltpu
from jax.sharding import PartitionSpec as P

HK = 16
HV = 32
DK = 128
DV = 128


def normalize(vectors):
    return vectors * lax.rsqrt(jnp.sum(vectors * vectors, axis=-1, keepdims=True) + 1e-06)


def conv_steps(state, proj, taps):
    seq = jnp.concatenate([state, proj], axis=1).astype(jnp.float32)
    taps = taps.astype(jnp.float32)
    kernel = taps.shape[0]
    steps = proj.shape[1]
    mixed = sum(seq[:, k : k + steps, :] * taps[k][None, None, :] for k in range(kernel))
    return jax.nn.silu(mixed)


def gather_rows(x, axis):
    n = lax.axis_size(axis)
    me = lax.axis_index(axis)
    pieces = [x]
    for s in range(1, n):
        pieces.append(lax.ppermute(x, axis, [(i, (i + s) % n) for i in range(n)]))
    stacked = jnp.stack(pieces)
    order = (me - jnp.arange(n)) % n
    return jnp.take(stacked, order, axis=0, mode="clip").reshape(n * x.shape[0], *x.shape[1:])


def scatter_sum_rows(x, axis):
    n = lax.axis_size(axis)
    me = lax.axis_index(axis)
    chunks = x.reshape(n, x.shape[0] // n, *x.shape[1:])
    acc = jnp.take(chunks, me, axis=0)
    for s in range(1, n):
        send = jnp.take(chunks, (me + s) % n, axis=0)
        acc = acc + lax.ppermute(send, axis, [(i, (i + s) % n) for i in range(n)])
    return acc


def scatter_sum_rows_paired(x, axis):
    n = lax.axis_size(axis)
    m = n // 2
    me = lax.axis_index(axis)
    core = me % 2
    chip = me // 2
    chunks = x.reshape(m, 2, x.shape[0] // n, *x.shape[1:])
    keep = jnp.take(chunks, core, axis=1)
    send = jnp.take(chunks, 1 - core, axis=1)
    part = keep + lax.ppermute(send, axis, [(i, i ^ 1) for i in range(n)])
    acc = jnp.take(part, chip, axis=0)
    for s in range(1, m):
        send = jnp.take(part, (chip + s) % m, axis=0)
        perm = [(i, ((i // 2 + s) % m) * 2 + i % 2) for i in range(n)]
        acc = acc + lax.ppermute(send, axis, perm)
    return acc


def gather_pieces(x, axis):
    n = lax.axis_size(axis)
    pieces = [x]
    for s in range(1, n):
        pieces.append(lax.ppermute(x, axis, [(i, (i + s) % n) for i in range(n)]))
    return jnp.stack(pieces)


def weight_chunks(width):
    step = 512 if width % 512 == 0 else width
    return [(c, step) for c in range(0, width, step)]


def projection_kernel(x_ref, wqk_hbm, wvz_hbm, wba_t_hbm, *rest):
    outs = rest[:-4]
    qk_buf, vz_buf, ba_buf, sems = rest[-4:]
    section = outs[0].shape[0]
    width_qk, width_vz = qk_buf.shape[1], vz_buf.shape[1]
    copies = []
    for src, buf, offset in ((wqk_hbm, qk_buf, 0), (wvz_hbm, vz_buf, width_qk)):
        for c, step in weight_chunks(buf.shape[1]):
            copy = pltpu.make_async_copy(
                src.at[:, pl.ds(c, step)], buf.at[:, pl.ds(c, step)], sems.at[len(copies)]
            )
            copy.start()
            copies.append((copy, buf, c, step, offset + c))
    ba_copy = pltpu.make_async_copy(wba_t_hbm, ba_buf, sems.at[len(copies)])
    ba_copy.start()
    x = x_ref[...]
    for copy, buf, c, step, column in copies:
        copy.wait()
        y = jnp.dot(x, buf[:, c : c + step], preferred_element_type=jnp.float32)
        for i, o_ref in enumerate(outs):
            o_ref[:, column : column + step] = y[i * section : (i + 1) * section]
    ba_copy.wait()
    y = lax.dot_general(x, ba_buf[...], (((1,), (1,)), ((), ())), preferred_element_type=jnp.float32)
    column = width_qk + width_vz
    for i, o_ref in enumerate(outs):
        o_ref[:, column : column + ba_buf.shape[0]] = y[i * section : (i + 1) * section]


def projection(x, w_qk, w_vz, w_ba, sections):
    rows = x.shape[0] // sections
    cols = w_qk.shape[1] + w_vz.shape[1] + w_ba.shape[1]
    n_copies = len(weight_chunks(w_qk.shape[1])) + len(weight_chunks(w_vz.shape[1])) + 1
    return pl.pallas_call(
        projection_kernel,
        in_specs=[
            pl.BlockSpec(memory_space=pltpu.VMEM),
            pl.BlockSpec(memory_space=pl.ANY),
            pl.BlockSpec(memory_space=pl.ANY),
            pl.BlockSpec(memory_space=pl.ANY),
        ],
        out_specs=[pl.BlockSpec(memory_space=pltpu.VMEM)] * sections,
        out_shape=[jax.ShapeDtypeStruct((rows, cols), jnp.float32)] * sections,
        scratch_shapes=[
            pltpu.VMEM(w_qk.shape, w_qk.dtype),
            pltpu.VMEM(w_vz.shape, w_vz.dtype),
            pltpu.VMEM((w_ba.shape[1], w_ba.shape[0]), w_ba.dtype),
            pltpu.SemaphoreType.DMA((n_copies,)),
        ],
        cost_estimate=pl.CostEstimate(
            flops=2 * x.shape[0] * x.shape[1] * cols,
            bytes_accessed=2 * x.shape[1] * cols + 2 * x.size + 4 * x.shape[0] * cols,
            transcendentals=0,
        ),
    )(x, w_qk, w_vz, w_ba.T)


def recurrence_kernel(gates_ref, qt_ref, kt_ref, v_ref, s_ref, s_out, o_ref, *, heads, steps, ratio):
    r = pl.program_id(0)
    key_heads = heads // ratio
    cols = heads * steps
    for kh in range(key_heads):
        group = [kh * ratio + j for j in range(ratio)]
        states = [s_ref[0, h] for h in group]
        for t in range(steps):
            ck = t * key_heads + kh
            key_col = kt_ref[0, :, ck : ck + 1]
            query_col = qt_ref[0, :, ck : ck + 1]
            for j, h in enumerate(group):
                c = t * heads + h
                lanes = slice(h * DV, (h + 1) * DV)
                state = states[j] * gates_ref[r, cols + c]
                recalled = jnp.sum(key_col * state, axis=0, keepdims=True)
                correction = (v_ref[0, t : t + 1, lanes] - recalled) * gates_ref[r, c]
                state = state + key_col * correction
                o_ref[0, t : t + 1, lanes] = jnp.sum(query_col * state, axis=0, keepdims=True)
                states[j] = state
        for j, h in enumerate(group):
            s_out[0, h] = states[j]


def recurrence(gates, qt, kt, values, memory_state):
    rows, heads = memory_state.shape[0], memory_state.shape[1]
    steps = values.shape[1]
    key_cols = kt.shape[2]
    ratio = heads * steps // key_cols
    kern = functools.partial(recurrence_kernel, heads=heads, steps=steps, ratio=ratio)
    return pl.pallas_call(
        kern,
        grid=(rows,),
        in_specs=[
            pl.BlockSpec(memory_space=pltpu.SMEM),
            pl.BlockSpec((1, DK, key_cols), lambda r: (r, 0, 0)),
            pl.BlockSpec((1, DK, key_cols), lambda r: (r, 0, 0)),
            pl.BlockSpec((1, steps, heads * DV), lambda r: (r, 0, 0)),
            pl.BlockSpec((1, heads, DK, DV), lambda r: (r, 0, 0, 0)),
        ],
        out_specs=[
            pl.BlockSpec((1, heads, DK, DV), lambda r: (r, 0, 0, 0)),
            pl.BlockSpec((1, steps, heads * DV), lambda r: (r, 0, 0)),
        ],
        out_shape=[
            jax.ShapeDtypeStruct(memory_state.shape, jnp.float32),
            jax.ShapeDtypeStruct((rows, steps, heads * DV), jnp.float32),
        ],
        cost_estimate=pl.CostEstimate(
            flops=8 * rows * heads * steps * DK * DV,
            bytes_accessed=2 * memory_state.size * 4,
            transcendentals=0,
        ),
    )(gates, qt, kt, values, memory_state)


def shards(
    activations,
    w_qk,
    w_vz,
    w_ba,
    conv_qk,
    conv_v,
    a_log,
    dt_bias,
    norm_gain,
    w_out,
    conv_state_qk,
    conv_state_v,
    memory_state,
):
    head_ratio = HV // HK
    step_count = activations.shape[1]
    rows_mem = memory_state.shape[0]
    heads = memory_state.shape[1]
    width_qk = w_qk.shape[1]
    width_vz = w_vz.shape[1]

    pieces = gather_pieces(activations, "head")
    n_head, rows_head = pieces.shape[0], pieces.shape[1]
    me_head = lax.axis_index("head")
    n_dp = lax.axis_size("dp")
    chips = n_dp // 2
    me_dp = lax.axis_index("dp")
    core, chip = me_dp % 2, me_dp // 2
    assert rows_head % rows_mem == 0
    sections = []
    for which in (1 - core, core):
        for s in range(chips):
            block = ((chip + s) % chips) * 2 + which
            first = block * rows_mem
            source = (me_head - first // rows_head) % n_head
            offset = first % rows_head
            picked = pieces[0]
            for shift in range(1, n_head):
                picked = jnp.where(source == shift, pieces[shift], picked)
            picked = lax.dynamic_slice_in_dim(picked, offset, rows_mem, axis=0)
            sections.append(picked.reshape(rows_mem * step_count, -1))
    flat_rows = jnp.concatenate(sections, axis=0)
    outs = projection(flat_rows, w_qk, w_vz, w_ba, 2 * chips)
    pair = [(i, i ^ 1) for i in range(n_dp)]
    part = [keep + lax.ppermute(send, "dp", pair) for send, keep in zip(outs[:chips], outs[chips:])]
    summed_qk = part[0][:, :width_qk]
    summed_rest = part[0][:, width_qk:]
    for s in range(1, chips):
        perm = [(i, ((i // 2 + s) % chips) * 2 + i % 2) for i in range(n_dp)]
        summed_qk = summed_qk + lax.ppermute(part[s][:, :width_qk], "dp", perm)
        summed_rest = summed_rest + lax.ppermute(part[s][:, width_qk:], "dp", perm)
    summed_vz = summed_rest[:, :width_vz]
    summed_ba = summed_rest[:, width_vz:]
    qk_proj = summed_qk.astype(jnp.bfloat16).reshape(rows_mem, step_count, width_qk)
    vz_proj = summed_vz.astype(jnp.bfloat16).reshape(rows_mem, step_count, width_vz)
    ba_proj = summed_ba.astype(jnp.bfloat16).reshape(rows_mem, step_count, -1)

    split_vz = vz_proj.reshape(rows_mem, step_count, heads, 2, DV)
    values_now = split_vz[:, :, :, 0, :].reshape(rows_mem, step_count, heads * DV)
    gate_z = split_vz[:, :, :, 1, :].astype(jnp.float32)

    qk_conv = conv_steps(conv_state_qk, qk_proj, conv_qk).reshape(rows_mem, step_count, -1, 2, DK)
    v_conv = conv_steps(conv_state_v, values_now, conv_v)
    queries = normalize(qk_conv[:, :, :, 0, :]) * DK ** (-0.5)
    key_vec = normalize(qk_conv[:, :, :, 1, :])
    key_heads = queries.shape[2]
    assert key_heads * head_ratio == heads
    qt = queries.transpose(0, 3, 1, 2).reshape(rows_mem, DK, step_count * key_heads)
    kt = key_vec.transpose(0, 3, 1, 2).reshape(rows_mem, DK, step_count * key_heads)

    split_ba = ba_proj.reshape(rows_mem, step_count, heads, 2).astype(jnp.float32)
    beta_gate = jax.nn.sigmoid(split_ba[..., 0])
    log_decay = -jnp.exp(a_log)[None, None, :] * jax.nn.softplus(split_ba[..., 1] + dt_bias[None, None, :])
    gates = jnp.concatenate(
        [beta_gate.reshape(rows_mem, -1), jnp.exp(log_decay).reshape(rows_mem, -1)], axis=1
    )

    new_state, readout = recurrence(gates, qt, kt, v_conv, memory_state)
    readout = readout.reshape(rows_mem, step_count, heads, DV)

    scale = lax.rsqrt(jnp.mean(readout * readout, axis=-1, keepdims=True) + 1e-06)
    normed = readout * scale * norm_gain[None, None, None, :] * jax.nn.silu(gate_z)
    normed = normed.reshape(rows_mem, step_count, heads * DV).astype(jnp.bfloat16)

    all_normed = gather_rows(normed, "dp")
    partials = jnp.dot(
        all_normed.reshape(-1, all_normed.shape[-1]), w_out, preferred_element_type=jnp.float32
    )
    layer_out = scatter_sum_rows(partials, "head")
    layer_out = layer_out.astype(jnp.bfloat16).reshape(-1, step_count, w_out.shape[1])
    return (layer_out, new_state)


def solution(mesh):
    in_specs = (
        P(("groups", "head"), None, "dp"),
        P("dp", "head"),
        P("dp", "head"),
        P("dp", "head"),
        P(None, "head"),
        P(None, "head"),
        P("head"),
        P("head"),
        P(),
        P("head", "dp"),
        P(("groups", "dp"), None, "head"),
        P(("groups", "dp"), None, "head"),
        P(("groups", "dp"), "head", None, None),
    )
    out_specs = (P(("groups", "head"), None, "dp"), P(("groups", "dp"), "head", None, None))
    return jax.shard_map(shards, mesh=mesh, in_specs=in_specs, out_specs=out_specs, check_vma=False)
```

```python
import functools

import jax
import jax.numpy as jnp
from jax import lax
from jax.experimental import pallas as pl
from jax.experimental.pallas import tpu as pltpu
from jax.sharding import PartitionSpec as P

HK = 16
HV = 32
DK = 128
DV = 128


def normalize(vectors):
    return vectors * lax.rsqrt(jnp.sum(vectors * vectors, axis=-1, keepdims=True) + 1e-06)


def conv_steps(state, proj, taps):
    seq = jnp.concatenate([state, proj], axis=1).astype(jnp.float32)
    taps = taps.astype(jnp.float32)
    kernel = taps.shape[0]
    steps = proj.shape[1]
    mixed = sum(seq[:, k : k + steps, :] * taps[k][None, None, :] for k in range(kernel))
    return jax.nn.silu(mixed)


def gather_rows(x, axis):
    n = lax.axis_size(axis)
    me = lax.axis_index(axis)
    pieces = [x]
    for s in range(1, n):
        pieces.append(lax.ppermute(x, axis, [(i, (i + s) % n) for i in range(n)]))
    stacked = jnp.stack(pieces)
    order = (me - jnp.arange(n)) % n
    return jnp.take(stacked, order, axis=0, mode="clip").reshape(n * x.shape[0], *x.shape[1:])


def scatter_sum_rows(x, axis):
    n = lax.axis_size(axis)
    me = lax.axis_index(axis)
    chunks = x.reshape(n, x.shape[0] // n, *x.shape[1:])
    acc = jnp.take(chunks, me, axis=0)
    for s in range(1, n):
        send = jnp.take(chunks, (me + s) % n, axis=0)
        acc = acc + lax.ppermute(send, axis, [(i, (i + s) % n) for i in range(n)])
    return acc


def scatter_sum_rows_paired(x, axis):
    n = lax.axis_size(axis)
    m = n // 2
    me = lax.axis_index(axis)
    core = me % 2
    chip = me // 2
    chunks = x.reshape(m, 2, x.shape[0] // n, *x.shape[1:])
    keep = jnp.take(chunks, core, axis=1)
    send = jnp.take(chunks, 1 - core, axis=1)
    part = keep + lax.ppermute(send, axis, [(i, i ^ 1) for i in range(n)])
    acc = jnp.take(part, chip, axis=0)
    for s in range(1, m):
        send = jnp.take(part, (chip + s) % m, axis=0)
        perm = [(i, ((i // 2 + s) % m) * 2 + i % 2) for i in range(n)]
        acc = acc + lax.ppermute(send, axis, perm)
    return acc


def gather_pieces(x, axis):
    n = lax.axis_size(axis)
    pieces = [x]
    for s in range(1, n):
        pieces.append(lax.ppermute(x, axis, [(i, (i + s) % n) for i in range(n)]))
    return jnp.stack(pieces)


def projection_kernel(x_ref, wqk_ref, wvz_ref, wba_t_ref, *outs):
    x = x_ref[...]
    section = outs[0].shape[0]
    offset = 0
    for w_ref, transposed in ((wqk_ref, False), (wvz_ref, False), (wba_t_ref, True)):
        width = w_ref.shape[0 if transposed else 1]
        contract = 1 if transposed else 0
        y = lax.dot_general(
            x, w_ref[...], (((1,), (contract,)), ((), ())), preferred_element_type=jnp.float32
        )
        for i, o_ref in enumerate(outs):
            o_ref[:, offset : offset + width] = y[i * section : (i + 1) * section]
        offset += width


def projection(x, w_qk, w_vz, w_ba, sections):
    rows = x.shape[0] // sections
    cols = w_qk.shape[1] + w_vz.shape[1] + w_ba.shape[1]
    return pl.pallas_call(
        projection_kernel,
        out_shape=[jax.ShapeDtypeStruct((rows, cols), jnp.float32)] * sections,
        cost_estimate=pl.CostEstimate(
            flops=2 * x.shape[0] * x.shape[1] * cols,
            bytes_accessed=2 * x.shape[1] * cols + 2 * x.size + 4 * x.shape[0] * cols,
            transcendentals=0,
        ),
    )(x, w_qk, w_vz, w_ba.T)


def recurrence_kernel(gates_ref, gain_ref, qt_ref, kt_ref, v_ref, z_ref, s_ref, s_out, o_ref, *, heads, steps, ratio):
    r = pl.program_id(0)
    key_heads = heads // ratio
    cols = heads * steps
    for kh in range(key_heads):
        group = [kh * ratio + j for j in range(ratio)]
        states = [s_ref[0, h] for h in group]
        for t in range(steps):
            ck = t * key_heads + kh
            key_col = kt_ref[0, :, ck : ck + 1]
            query_col = qt_ref[0, :, ck : ck + 1]
            for j, h in enumerate(group):
                c = t * heads + h
                lanes = slice(h * DV, (h + 1) * DV)
                state = states[j] * gates_ref[r, cols + c]
                recalled = jnp.sum(key_col * state, axis=0, keepdims=True)
                correction = (v_ref[0, t : t + 1, lanes] - recalled) * gates_ref[r, c]
                state = state + key_col * correction
                readout = jnp.sum(query_col * state, axis=0, keepdims=True)
                scale = lax.rsqrt(jnp.mean(readout * readout, axis=-1, keepdims=True) + 1e-06)
                gate = z_ref[0, t : t + 1, lanes]
                o_ref[0, t : t + 1, lanes] = readout * scale * gain_ref[...] * (gate * jax.nn.sigmoid(gate))
                states[j] = state
        for j, h in enumerate(group):
            s_out[0, h] = states[j]


def recurrence(gates, norm_gain, qt, kt, values, gate_z, memory_state):
    rows, heads = memory_state.shape[0], memory_state.shape[1]
    steps = values.shape[1]
    key_cols = kt.shape[2]
    ratio = heads * steps // key_cols
    kern = functools.partial(recurrence_kernel, heads=heads, steps=steps, ratio=ratio)
    return pl.pallas_call(
        kern,
        grid=(rows,),
        in_specs=[
            pl.BlockSpec(memory_space=pltpu.SMEM),
            pl.BlockSpec((1, DV), lambda r: (0, 0)),
            pl.BlockSpec((1, DK, key_cols), lambda r: (r, 0, 0)),
            pl.BlockSpec((1, DK, key_cols), lambda r: (r, 0, 0)),
            pl.BlockSpec((1, steps, heads * DV), lambda r: (r, 0, 0)),
            pl.BlockSpec((1, steps, heads * DV), lambda r: (r, 0, 0)),
            pl.BlockSpec((1, heads, DK, DV), lambda r: (r, 0, 0, 0)),
        ],
        out_specs=[
            pl.BlockSpec((1, heads, DK, DV), lambda r: (r, 0, 0, 0)),
            pl.BlockSpec((1, steps, heads * DV), lambda r: (r, 0, 0)),
        ],
        out_shape=[
            jax.ShapeDtypeStruct(memory_state.shape, jnp.float32),
            jax.ShapeDtypeStruct((rows, steps, heads * DV), jnp.float32),
        ],
        cost_estimate=pl.CostEstimate(
            flops=8 * rows * heads * steps * DK * DV,
            bytes_accessed=2 * memory_state.size * 4,
            transcendentals=0,
        ),
    )(gates, norm_gain.reshape(1, DV), qt, kt, values, gate_z, memory_state)


def shards(
    activations,
    w_qk,
    w_vz,
    w_ba,
    conv_qk,
    conv_v,
    a_log,
    dt_bias,
    norm_gain,
    w_out,
    conv_state_qk,
    conv_state_v,
    memory_state,
):
    head_ratio = HV // HK
    step_count = activations.shape[1]
    rows_mem = memory_state.shape[0]
    heads = memory_state.shape[1]
    width_qk = w_qk.shape[1]
    width_vz = w_vz.shape[1]

    pieces = gather_pieces(activations, "head")
    n_head, rows_head = pieces.shape[0], pieces.shape[1]
    me_head = lax.axis_index("head")
    n_dp = lax.axis_size("dp")
    chips = n_dp // 2
    me_dp = lax.axis_index("dp")
    core, chip = me_dp % 2, me_dp // 2
    assert rows_head % rows_mem == 0
    sections = []
    for which in (1 - core, core):
        for s in range(chips):
            block = ((chip + s) % chips) * 2 + which
            first = block * rows_mem
            source = (me_head - first // rows_head) % n_head
            offset = first % rows_head
            picked = pieces[0]
            for shift in range(1, n_head):
                picked = jnp.where(source == shift, pieces[shift], picked)
            picked = lax.dynamic_slice_in_dim(picked, offset, rows_mem, axis=0)
            sections.append(picked.reshape(rows_mem * step_count, -1))
    flat_rows = jnp.concatenate(sections, axis=0)
    outs = projection(flat_rows, w_qk, w_vz, w_ba, 2 * chips)
    pair = [(i, i ^ 1) for i in range(n_dp)]
    part = [keep + lax.ppermute(send, "dp", pair) for send, keep in zip(outs[:chips], outs[chips:])]
    summed_qk = part[0][:, :width_qk]
    summed_rest = part[0][:, width_qk:]
    for s in range(1, chips):
        perm = [(i, ((i // 2 + s) % chips) * 2 + i % 2) for i in range(n_dp)]
        summed_qk = summed_qk + lax.ppermute(part[s][:, :width_qk], "dp", perm)
        summed_rest = summed_rest + lax.ppermute(part[s][:, width_qk:], "dp", perm)
    summed_vz = summed_rest[:, :width_vz]
    summed_ba = summed_rest[:, width_vz:]
    qk_proj = summed_qk.astype(jnp.bfloat16).reshape(rows_mem, step_count, width_qk)
    vz_proj = summed_vz.astype(jnp.bfloat16).reshape(rows_mem, step_count, width_vz)
    ba_proj = summed_ba.astype(jnp.bfloat16).reshape(rows_mem, step_count, -1)

    split_vz = vz_proj.reshape(rows_mem, step_count, heads, 2, DV)
    values_now = split_vz[:, :, :, 0, :].reshape(rows_mem, step_count, heads * DV)
    gate_z = split_vz[:, :, :, 1, :].astype(jnp.float32)

    qk_conv = conv_steps(conv_state_qk, qk_proj, conv_qk).reshape(rows_mem, step_count, -1, 2, DK)
    v_conv = conv_steps(conv_state_v, values_now, conv_v)
    queries = normalize(qk_conv[:, :, :, 0, :]) * DK ** (-0.5)
    key_vec = normalize(qk_conv[:, :, :, 1, :])
    key_heads = queries.shape[2]
    assert key_heads * head_ratio == heads
    qt = queries.transpose(0, 3, 1, 2).reshape(rows_mem, DK, step_count * key_heads)
    kt = key_vec.transpose(0, 3, 1, 2).reshape(rows_mem, DK, step_count * key_heads)

    split_ba = ba_proj.reshape(rows_mem, step_count, heads, 2).astype(jnp.float32)
    beta_gate = jax.nn.sigmoid(split_ba[..., 0])
    log_decay = -jnp.exp(a_log)[None, None, :] * jax.nn.softplus(split_ba[..., 1] + dt_bias[None, None, :])
    gates = jnp.concatenate(
        [beta_gate.reshape(rows_mem, -1), jnp.exp(log_decay).reshape(rows_mem, -1)], axis=1
    )

    new_state, normed = recurrence(
        gates, norm_gain, qt, kt, v_conv, gate_z.reshape(rows_mem, step_count, heads * DV), memory_state
    )
    normed = normed.astype(jnp.bfloat16)

    all_normed = gather_rows(normed, "dp")
    partials = jnp.dot(
        all_normed.reshape(-1, all_normed.shape[-1]), w_out, preferred_element_type=jnp.float32
    )
    layer_out = scatter_sum_rows(partials, "head")
    layer_out = layer_out.astype(jnp.bfloat16).reshape(-1, step_count, w_out.shape[1])
    return (layer_out, new_state)


def solution(mesh):
    in_specs = (
        P(("groups", "head"), None, "dp"),
        P("dp", "head"),
        P("dp", "head"),
        P("dp", "head"),
        P(None, "head"),
        P(None, "head"),
        P("head"),
        P("head"),
        P(),
        P("head", "dp"),
        P(("groups", "dp"), None, "head"),
        P(("groups", "dp"), None, "head"),
        P(("groups", "dp"), "head", None, None),
    )
    out_specs = (P(("groups", "head"), None, "dp"), P(("groups", "dp"), "head", None, None))
    return jax.shard_map(shards, mesh=mesh, in_specs=in_specs, out_specs=out_specs, check_vma=False)
```

```python
import functools

import jax
import jax.numpy as jnp
from jax import lax
from jax.experimental import pallas as pl
from jax.experimental.pallas import tpu as pltpu
from jax.sharding import PartitionSpec as P

HK = 16
HV = 32
DK = 128
DV = 128


def normalize(vectors):
    return vectors * lax.rsqrt(jnp.sum(vectors * vectors, axis=-1, keepdims=True) + 1e-06)


def conv_steps(state, proj, taps):
    seq = jnp.concatenate([state, proj], axis=1).astype(jnp.float32)
    taps = taps.astype(jnp.float32)
    kernel = taps.shape[0]
    steps = proj.shape[1]
    mixed = sum(seq[:, k : k + steps, :] * taps[k][None, None, :] for k in range(kernel))
    return jax.nn.silu(mixed)


def gather_rows(x, axis):
    n = lax.axis_size(axis)
    me = lax.axis_index(axis)
    pieces = [x]
    for s in range(1, n):
        pieces.append(lax.ppermute(x, axis, [(i, (i + s) % n) for i in range(n)]))
    stacked = jnp.stack(pieces)
    order = (me - jnp.arange(n)) % n
    return jnp.take(stacked, order, axis=0, mode="clip").reshape(n * x.shape[0], *x.shape[1:])


def scatter_sum_rows(x, axis):
    n = lax.axis_size(axis)
    me = lax.axis_index(axis)
    chunks = x.reshape(n, x.shape[0] // n, *x.shape[1:])
    acc = jnp.take(chunks, me, axis=0)
    for s in range(1, n):
        send = jnp.take(chunks, (me + s) % n, axis=0)
        acc = acc + lax.ppermute(send, axis, [(i, (i + s) % n) for i in range(n)])
    return acc


def scatter_sum_rows_paired(x, axis):
    n = lax.axis_size(axis)
    m = n // 2
    me = lax.axis_index(axis)
    core = me % 2
    chip = me // 2
    chunks = x.reshape(m, 2, x.shape[0] // n, *x.shape[1:])
    keep = jnp.take(chunks, core, axis=1)
    send = jnp.take(chunks, 1 - core, axis=1)
    part = keep + lax.ppermute(send, axis, [(i, i ^ 1) for i in range(n)])
    acc = jnp.take(part, chip, axis=0)
    for s in range(1, m):
        send = jnp.take(part, (chip + s) % m, axis=0)
        perm = [(i, ((i // 2 + s) % m) * 2 + i % 2) for i in range(n)]
        acc = acc + lax.ppermute(send, axis, perm)
    return acc


def gather_pieces(x, axis):
    n = lax.axis_size(axis)
    pieces = [x]
    for s in range(1, n):
        pieces.append(lax.ppermute(x, axis, [(i, (i + s) % n) for i in range(n)]))
    return jnp.stack(pieces)


def projection_kernel(x_ref, wqk_ref, wvz_ref, wba_t_ref, *outs):
    x = x_ref[...]
    section = outs[0].shape[0]
    offset = 0
    for w_ref, transposed in ((wqk_ref, False), (wvz_ref, False), (wba_t_ref, True)):
        width = w_ref.shape[0 if transposed else 1]
        contract = 1 if transposed else 0
        y = lax.dot_general(
            x, w_ref[...], (((1,), (contract,)), ((), ())), preferred_element_type=jnp.float32
        )
        for i, o_ref in enumerate(outs):
            o_ref[:, offset : offset + width] = y[i * section : (i + 1) * section]
        offset += width


def projection(x, w_qk, w_vz, w_ba, sections):
    rows = x.shape[0] // sections
    cols = w_qk.shape[1] + w_vz.shape[1] + w_ba.shape[1]
    return pl.pallas_call(
        projection_kernel,
        out_shape=[jax.ShapeDtypeStruct((rows, cols), jnp.float32)] * sections,
        cost_estimate=pl.CostEstimate(
            flops=2 * x.shape[0] * x.shape[1] * cols,
            bytes_accessed=2 * x.shape[1] * cols + 2 * x.size + 4 * x.shape[0] * cols,
            transcendentals=0,
        ),
    )(x, w_qk, w_vz, w_ba.T)


def recurrence_kernel(gates_ref, qt_ref, kt_ref, v_ref, s_ref, s_out, o_ref, *, heads, steps, ratio):
    r = pl.program_id(0)
    key_heads = heads // ratio
    cols = heads * steps
    for kh in range(key_heads):
        group = [kh * ratio + j for j in range(ratio)]
        states = [s_ref[0, h] for h in group]
        for t in range(steps):
            ck = t * key_heads + kh
            key_col = kt_ref[0, :, ck : ck + 1]
            query_col = qt_ref[0, :, ck : ck + 1]
            for j, h in enumerate(group):
                c = t * heads + h
                lanes = slice(h * DV, (h + 1) * DV)
                state = states[j] * gates_ref[r, cols + c]
                recalled = jnp.sum(key_col * state, axis=0, keepdims=True)
                correction = (v_ref[0, t : t + 1, lanes] - recalled) * gates_ref[r, c]
                state = state + key_col * correction
                o_ref[0, t, h : h + 1, :] = jnp.sum(query_col * state, axis=0, keepdims=True)
                states[j] = state
        for j, h in enumerate(group):
            s_out[0, h] = states[j]


def recurrence(gates, qt, kt, values, memory_state):
    rows, heads = memory_state.shape[0], memory_state.shape[1]
    steps = values.shape[1]
    key_cols = kt.shape[2]
    ratio = heads * steps // key_cols
    kern = functools.partial(recurrence_kernel, heads=heads, steps=steps, ratio=ratio)
    return pl.pallas_call(
        kern,
        grid=(rows,),
        in_specs=[
            pl.BlockSpec(memory_space=pltpu.SMEM),
            pl.BlockSpec((1, DK, key_cols), lambda r: (r, 0, 0)),
            pl.BlockSpec((1, DK, key_cols), lambda r: (r, 0, 0)),
            pl.BlockSpec((1, steps, heads * DV), lambda r: (r, 0, 0)),
            pl.BlockSpec((1, heads, DK, DV), lambda r: (r, 0, 0, 0)),
        ],
        out_specs=[
            pl.BlockSpec((1, heads, DK, DV), lambda r: (r, 0, 0, 0)),
            pl.BlockSpec((1, steps, heads, DV), lambda r: (r, 0, 0, 0)),
        ],
        out_shape=[
            jax.ShapeDtypeStruct(memory_state.shape, jnp.float32),
            jax.ShapeDtypeStruct((rows, steps, heads, DV), jnp.float32),
        ],
        cost_estimate=pl.CostEstimate(
            flops=8 * rows * heads * steps * DK * DV,
            bytes_accessed=2 * memory_state.size * 4,
            transcendentals=0,
        ),
    )(gates, qt, kt, values, memory_state)


def shards(
    activations,
    w_qk,
    w_vz,
    w_ba,
    conv_qk,
    conv_v,
    a_log,
    dt_bias,
    norm_gain,
    w_out,
    conv_state_qk,
    conv_state_v,
    memory_state,
):
    head_ratio = HV // HK
    step_count = activations.shape[1]
    rows_mem = memory_state.shape[0]
    heads = memory_state.shape[1]
    width_qk = w_qk.shape[1]
    width_vz = w_vz.shape[1]

    pieces = gather_pieces(activations, "head")
    n_head, rows_head = pieces.shape[0], pieces.shape[1]
    me_head = lax.axis_index("head")
    n_dp = lax.axis_size("dp")
    chips = n_dp // 2
    me_dp = lax.axis_index("dp")
    core, chip = me_dp % 2, me_dp // 2
    assert rows_head % rows_mem == 0
    sections = []
    for which in (1 - core, core):
        for s in range(chips):
            block = ((chip + s) % chips) * 2 + which
            first = block * rows_mem
            source = (me_head - first // rows_head) % n_head
            offset = first % rows_head
            picked = pieces[0]
            for shift in range(1, n_head):
                picked = jnp.where(source == shift, pieces[shift], picked)
            picked = lax.dynamic_slice_in_dim(picked, offset, rows_mem, axis=0)
            sections.append(picked.reshape(rows_mem * step_count, -1))
    flat_rows = jnp.concatenate(sections, axis=0)
    outs = projection(flat_rows, w_qk, w_vz, w_ba, 2 * chips)
    pair = [(i, i ^ 1) for i in range(n_dp)]
    part = [keep + lax.ppermute(send, "dp", pair) for send, keep in zip(outs[:chips], outs[chips:])]
    summed_qk = part[0][:, :width_qk]
    summed_rest = part[0][:, width_qk:]
    for s in range(1, chips):
        perm = [(i, ((i // 2 + s) % chips) * 2 + i % 2) for i in range(n_dp)]
        summed_qk = summed_qk + lax.ppermute(part[s][:, :width_qk], "dp", perm)
        summed_rest = summed_rest + lax.ppermute(part[s][:, width_qk:], "dp", perm)
    summed_vz = summed_rest[:, :width_vz]
    summed_ba = summed_rest[:, width_vz:]
    qk_proj = summed_qk.astype(jnp.bfloat16).reshape(rows_mem, step_count, width_qk)
    vz_proj = summed_vz.astype(jnp.bfloat16).reshape(rows_mem, step_count, width_vz)
    ba_proj = summed_ba.astype(jnp.bfloat16).reshape(rows_mem, step_count, -1)

    split_vz = vz_proj.reshape(rows_mem, step_count, heads, 2, DV)
    values_now = split_vz[:, :, :, 0, :].reshape(rows_mem, step_count, heads * DV)
    gate_z = split_vz[:, :, :, 1, :].astype(jnp.float32)

    qk_conv = conv_steps(conv_state_qk, qk_proj, conv_qk).reshape(rows_mem, step_count, -1, 2, DK)
    v_conv = conv_steps(conv_state_v, values_now, conv_v)
    queries = normalize(qk_conv[:, :, :, 0, :]) * DK ** (-0.5)
    key_vec = normalize(qk_conv[:, :, :, 1, :])
    key_heads = queries.shape[2]
    assert key_heads * head_ratio == heads
    qt = queries.transpose(0, 3, 1, 2).reshape(rows_mem, DK, step_count * key_heads)
    kt = key_vec.transpose(0, 3, 1, 2).reshape(rows_mem, DK, step_count * key_heads)

    split_ba = ba_proj.reshape(rows_mem, step_count, heads, 2).astype(jnp.float32)
    beta_gate = jax.nn.sigmoid(split_ba[..., 0])
    log_decay = -jnp.exp(a_log)[None, None, :] * jax.nn.softplus(split_ba[..., 1] + dt_bias[None, None, :])
    gates = jnp.concatenate(
        [beta_gate.reshape(rows_mem, -1), jnp.exp(log_decay).reshape(rows_mem, -1)], axis=1
    )

    new_state, readout = recurrence(gates, qt, kt, v_conv, memory_state)

    scale = lax.rsqrt(jnp.mean(readout * readout, axis=-1, keepdims=True) + 1e-06)
    normed = readout * scale * norm_gain[None, None, None, :] * jax.nn.silu(gate_z)
    normed = normed.astype(jnp.bfloat16)

    all_normed = gather_rows(normed, "dp")
    partials = jnp.einsum(
        "rthd,hde->rte",
        all_normed,
        w_out.reshape(heads, DV, -1),
        preferred_element_type=jnp.float32,
    ).reshape(-1, w_out.shape[1])
    layer_out = scatter_sum_rows(partials, "head")
    layer_out = layer_out.astype(jnp.bfloat16).reshape(-1, step_count, w_out.shape[1])
    return (layer_out, new_state)


def solution(mesh):
    in_specs = (
        P(("groups", "head"), None, "dp"),
        P("dp", "head"),
        P("dp", "head"),
        P("dp", "head"),
        P(None, "head"),
        P(None, "head"),
        P("head"),
        P("head"),
        P(),
        P("head", "dp"),
        P(("groups", "dp"), None, "head"),
        P(("groups", "dp"), None, "head"),
        P(("groups", "dp"), "head", None, None),
    )
    out_specs = (P(("groups", "head"), None, "dp"), P(("groups", "dp"), "head", None, None))
    return jax.shard_map(shards, mesh=mesh, in_specs=in_specs, out_specs=out_specs, check_vma=False)
```

```python
import functools

import jax
import jax.numpy as jnp
from jax import lax
from jax.experimental import pallas as pl
from jax.experimental.pallas import tpu as pltpu
from jax.sharding import PartitionSpec as P

HK = 16
HV = 32
DK = 128
DV = 128


def normalize(vectors):
    return vectors * lax.rsqrt(jnp.sum(vectors * vectors, axis=-1, keepdims=True) + 1e-06)


def conv_steps(state, proj, taps):
    seq = jnp.concatenate([state, proj], axis=1).astype(jnp.float32)
    taps = taps.astype(jnp.float32)
    kernel = taps.shape[0]
    steps = proj.shape[1]
    mixed = sum(seq[:, k : k + steps, :] * taps[k][None, None, :] for k in range(kernel))
    return jax.nn.silu(mixed)


def gather_rows(x, axis):
    n = lax.axis_size(axis)
    me = lax.axis_index(axis)
    pieces = [x]
    for s in range(1, n):
        pieces.append(lax.ppermute(x, axis, [(i, (i + s) % n) for i in range(n)]))
    stacked = jnp.stack(pieces)
    order = (me - jnp.arange(n)) % n
    return jnp.take(stacked, order, axis=0, mode="clip").reshape(n * x.shape[0], *x.shape[1:])


def scatter_sum_rows(x, axis):
    n = lax.axis_size(axis)
    me = lax.axis_index(axis)
    chunks = x.reshape(n, x.shape[0] // n, *x.shape[1:])
    acc = jnp.take(chunks, me, axis=0)
    for s in range(1, n):
        send = jnp.take(chunks, (me + s) % n, axis=0)
        acc = acc + lax.ppermute(send, axis, [(i, (i + s) % n) for i in range(n)])
    return acc


def scatter_sum_rows_paired(x, axis):
    n = lax.axis_size(axis)
    m = n // 2
    me = lax.axis_index(axis)
    core = me % 2
    chip = me // 2
    chunks = x.reshape(m, 2, x.shape[0] // n, *x.shape[1:])
    keep = jnp.take(chunks, core, axis=1)
    send = jnp.take(chunks, 1 - core, axis=1)
    part = keep + lax.ppermute(send, axis, [(i, i ^ 1) for i in range(n)])
    acc = jnp.take(part, chip, axis=0)
    for s in range(1, m):
        send = jnp.take(part, (chip + s) % m, axis=0)
        perm = [(i, ((i // 2 + s) % m) * 2 + i % 2) for i in range(n)]
        acc = acc + lax.ppermute(send, axis, perm)
    return acc


def gather_pieces(x, axis):
    n = lax.axis_size(axis)
    pieces = [x]
    for s in range(1, n):
        pieces.append(lax.ppermute(x, axis, [(i, (i + s) % n) for i in range(n)]))
    return jnp.stack(pieces)


def projection_kernel(x_ref, wqk_ref, wvz_ref, wba_t_ref, *outs):
    k = pl.program_id(0)
    x = x_ref[...]
    section = outs[0].shape[0]
    offset = 0
    for w_ref, transposed in ((wqk_ref, False), (wvz_ref, False), (wba_t_ref, True)):
        width = w_ref.shape[0 if transposed else 1]
        contract = 1 if transposed else 0
        y = lax.dot_general(
            x, w_ref[...], (((1,), (contract,)), ((), ())), preferred_element_type=jnp.float32
        )
        for i, o_ref in enumerate(outs):
            part = y[i * section : (i + 1) * section]

            @pl.when(k == 0)
            def _():
                o_ref[:, offset : offset + width] = part

            @pl.when(k > 0)
            def _():
                o_ref[:, offset : offset + width] += part

        offset += width


def projection(x, w_qk, w_vz, w_ba, sections):
    rows = x.shape[0] // sections
    cols = w_qk.shape[1] + w_vz.shape[1] + w_ba.shape[1]
    features = x.shape[1]
    block = 256 if features % 256 == 0 else features
    return pl.pallas_call(
        projection_kernel,
        grid=(features // block,),
        in_specs=[
            pl.BlockSpec((x.shape[0], block), lambda k: (0, k)),
            pl.BlockSpec((block, w_qk.shape[1]), lambda k: (k, 0)),
            pl.BlockSpec((block, w_vz.shape[1]), lambda k: (k, 0)),
            pl.BlockSpec((w_ba.shape[1], block), lambda k: (0, k)),
        ],
        out_specs=[pl.BlockSpec((rows, cols), lambda k: (0, 0))] * sections,
        out_shape=[jax.ShapeDtypeStruct((rows, cols), jnp.float32)] * sections,
        cost_estimate=pl.CostEstimate(
            flops=2 * x.shape[0] * x.shape[1] * cols,
            bytes_accessed=2 * x.shape[1] * cols + 2 * x.size + 4 * x.shape[0] * cols,
            transcendentals=0,
        ),
    )(x, w_qk, w_vz, w_ba.T)


def recurrence_kernel(gates_ref, qt_ref, kt_ref, v_ref, s_ref, s_out, o_ref, *, heads, steps, ratio):
    r = pl.program_id(0)
    key_heads = heads // ratio
    cols = heads * steps
    for kh in range(key_heads):
        group = [kh * ratio + j for j in range(ratio)]
        states = [s_ref[0, h] for h in group]
        for t in range(steps):
            ck = t * key_heads + kh
            key_col = kt_ref[0, :, ck : ck + 1]
            query_col = qt_ref[0, :, ck : ck + 1]
            for j, h in enumerate(group):
                c = t * heads + h
                lanes = slice(h * DV, (h + 1) * DV)
                state = states[j] * gates_ref[r, cols + c]
                recalled = jnp.sum(key_col * state, axis=0, keepdims=True)
                correction = (v_ref[0, t : t + 1, lanes] - recalled) * gates_ref[r, c]
                state = state + key_col * correction
                o_ref[0, t, h : h + 1, :] = jnp.sum(query_col * state, axis=0, keepdims=True)
                states[j] = state
        for j, h in enumerate(group):
            s_out[0, h] = states[j]


def recurrence(gates, qt, kt, values, memory_state):
    rows, heads = memory_state.shape[0], memory_state.shape[1]
    steps = values.shape[1]
    key_cols = kt.shape[2]
    ratio = heads * steps // key_cols
    kern = functools.partial(recurrence_kernel, heads=heads, steps=steps, ratio=ratio)
    return pl.pallas_call(
        kern,
        grid=(rows,),
        in_specs=[
            pl.BlockSpec(memory_space=pltpu.SMEM),
            pl.BlockSpec((1, DK, key_cols), lambda r: (r, 0, 0)),
            pl.BlockSpec((1, DK, key_cols), lambda r: (r, 0, 0)),
            pl.BlockSpec((1, steps, heads * DV), lambda r: (r, 0, 0)),
            pl.BlockSpec((1, heads, DK, DV), lambda r: (r, 0, 0, 0)),
        ],
        out_specs=[
            pl.BlockSpec((1, heads, DK, DV), lambda r: (r, 0, 0, 0)),
            pl.BlockSpec((1, steps, heads, DV), lambda r: (r, 0, 0, 0)),
        ],
        out_shape=[
            jax.ShapeDtypeStruct(memory_state.shape, jnp.float32),
            jax.ShapeDtypeStruct((rows, steps, heads, DV), jnp.float32),
        ],
        cost_estimate=pl.CostEstimate(
            flops=8 * rows * heads * steps * DK * DV,
            bytes_accessed=2 * memory_state.size * 4,
            transcendentals=0,
        ),
    )(gates, qt, kt, values, memory_state)


def shards(
    activations,
    w_qk,
    w_vz,
    w_ba,
    conv_qk,
    conv_v,
    a_log,
    dt_bias,
    norm_gain,
    w_out,
    conv_state_qk,
    conv_state_v,
    memory_state,
):
    head_ratio = HV // HK
    step_count = activations.shape[1]
    rows_mem = memory_state.shape[0]
    heads = memory_state.shape[1]
    width_qk = w_qk.shape[1]
    width_vz = w_vz.shape[1]

    pieces = gather_pieces(activations, "head")
    n_head, rows_head = pieces.shape[0], pieces.shape[1]
    me_head = lax.axis_index("head")
    n_dp = lax.axis_size("dp")
    chips = n_dp // 2
    me_dp = lax.axis_index("dp")
    core, chip = me_dp % 2, me_dp // 2
    assert rows_head % rows_mem == 0
    sections = []
    for which in (1 - core, core):
        for s in range(chips):
            block = ((chip + s) % chips) * 2 + which
            first = block * rows_mem
            source = (me_head - first // rows_head) % n_head
            offset = first % rows_head
            picked = pieces[0]
            for shift in range(1, n_head):
                picked = jnp.where(source == shift, pieces[shift], picked)
            picked = lax.dynamic_slice_in_dim(picked, offset, rows_mem, axis=0)
            sections.append(picked.reshape(rows_mem * step_count, -1))
    flat_rows = jnp.concatenate(sections, axis=0)
    outs = projection(flat_rows, w_qk, w_vz, w_ba, 2 * chips)
    pair = [(i, i ^ 1) for i in range(n_dp)]
    part = [keep + lax.ppermute(send, "dp", pair) for send, keep in zip(outs[:chips], outs[chips:])]
    summed_qk = part[0][:, :width_qk]
    summed_rest = part[0][:, width_qk:]
    for s in range(1, chips):
        perm = [(i, ((i // 2 + s) % chips) * 2 + i % 2) for i in range(n_dp)]
        summed_qk = summed_qk + lax.ppermute(part[s][:, :width_qk], "dp", perm)
        summed_rest = summed_rest + lax.ppermute(part[s][:, width_qk:], "dp", perm)
    summed_vz = summed_rest[:, :width_vz]
    summed_ba = summed_rest[:, width_vz:]
    qk_proj = summed_qk.astype(jnp.bfloat16).reshape(rows_mem, step_count, width_qk)
    vz_proj = summed_vz.astype(jnp.bfloat16).reshape(rows_mem, step_count, width_vz)
    ba_proj = summed_ba.astype(jnp.bfloat16).reshape(rows_mem, step_count, -1)

    split_vz = vz_proj.reshape(rows_mem, step_count, heads, 2, DV)
    values_now = split_vz[:, :, :, 0, :].reshape(rows_mem, step_count, heads * DV)
    gate_z = split_vz[:, :, :, 1, :].astype(jnp.float32)

    qk_conv = conv_steps(conv_state_qk, qk_proj, conv_qk).reshape(rows_mem, step_count, -1, 2, DK)
    v_conv = conv_steps(conv_state_v, values_now, conv_v)
    queries = normalize(qk_conv[:, :, :, 0, :]) * DK ** (-0.5)
    key_vec = normalize(qk_conv[:, :, :, 1, :])
    key_heads = queries.shape[2]
    assert key_heads * head_ratio == heads
    qt = queries.transpose(0, 3, 1, 2).reshape(rows_mem, DK, step_count * key_heads)
    kt = key_vec.transpose(0, 3, 1, 2).reshape(rows_mem, DK, step_count * key_heads)

    split_ba = ba_proj.reshape(rows_mem, step_count, heads, 2).astype(jnp.float32)
    beta_gate = jax.nn.sigmoid(split_ba[..., 0])
    log_decay = -jnp.exp(a_log)[None, None, :] * jax.nn.softplus(split_ba[..., 1] + dt_bias[None, None, :])
    gates = jnp.concatenate(
        [beta_gate.reshape(rows_mem, -1), jnp.exp(log_decay).reshape(rows_mem, -1)], axis=1
    )

    new_state, readout = recurrence(gates, qt, kt, v_conv, memory_state)

    scale = lax.rsqrt(jnp.mean(readout * readout, axis=-1, keepdims=True) + 1e-06)
    normed = readout * scale * norm_gain[None, None, None, :] * jax.nn.silu(gate_z)
    normed = normed.astype(jnp.bfloat16)

    all_normed = gather_rows(normed, "dp")
    partials = jnp.einsum(
        "rthd,hde->rte",
        all_normed,
        w_out.reshape(heads, DV, -1),
        preferred_element_type=jnp.float32,
    ).reshape(-1, w_out.shape[1])
    layer_out = scatter_sum_rows(partials, "head")
    layer_out = layer_out.astype(jnp.bfloat16).reshape(-1, step_count, w_out.shape[1])
    return (layer_out, new_state)


def solution(mesh):
    in_specs = (
        P(("groups", "head"), None, "dp"),
        P("dp", "head"),
        P("dp", "head"),
        P("dp", "head"),
        P(None, "head"),
        P(None, "head"),
        P("head"),
        P("head"),
        P(),
        P("head", "dp"),
        P(("groups", "dp"), None, "head"),
        P(("groups", "dp"), None, "head"),
        P(("groups", "dp"), "head", None, None),
    )
    out_specs = (P(("groups", "head"), None, "dp"), P(("groups", "dp"), "head", None, None))
    return jax.shard_map(shards, mesh=mesh, in_specs=in_specs, out_specs=out_specs, check_vma=False)
```

```python
import functools

import jax
import jax.numpy as jnp
from jax import lax
from jax.experimental import pallas as pl
from jax.experimental.pallas import tpu as pltpu
from jax.sharding import PartitionSpec as P

HK = 16
HV = 32
DK = 128
DV = 128


def normalize(vectors):
    return vectors * lax.rsqrt(jnp.sum(vectors * vectors, axis=-1, keepdims=True) + 1e-06)


def conv_steps(state, proj, taps):
    seq = jnp.concatenate([state, proj], axis=1).astype(jnp.float32)
    taps = taps.astype(jnp.float32)
    kernel = taps.shape[0]
    steps = proj.shape[1]
    mixed = sum(seq[:, k : k + steps, :] * taps[k][None, None, :] for k in range(kernel))
    return jax.nn.silu(mixed)


def gather_rows(x, axis):
    n = lax.axis_size(axis)
    me = lax.axis_index(axis)
    pieces = [x]
    for s in range(1, n):
        pieces.append(lax.ppermute(x, axis, [(i, (i + s) % n) for i in range(n)]))
    stacked = jnp.stack(pieces)
    order = (me - jnp.arange(n)) % n
    return jnp.take(stacked, order, axis=0, mode="clip").reshape(n * x.shape[0], *x.shape[1:])


def scatter_sum_rows(x, axis):
    n = lax.axis_size(axis)
    me = lax.axis_index(axis)
    chunks = x.reshape(n, x.shape[0] // n, *x.shape[1:])
    acc = jnp.take(chunks, me, axis=0)
    for s in range(1, n):
        send = jnp.take(chunks, (me + s) % n, axis=0)
        acc = acc + lax.ppermute(send, axis, [(i, (i + s) % n) for i in range(n)])
    return acc


def scatter_sum_rows_paired(x, axis):
    n = lax.axis_size(axis)
    m = n // 2
    me = lax.axis_index(axis)
    core = me % 2
    chip = me // 2
    chunks = x.reshape(m, 2, x.shape[0] // n, *x.shape[1:])
    keep = jnp.take(chunks, core, axis=1)
    send = jnp.take(chunks, 1 - core, axis=1)
    part = keep + lax.ppermute(send, axis, [(i, i ^ 1) for i in range(n)])
    acc = jnp.take(part, chip, axis=0)
    for s in range(1, m):
        send = jnp.take(part, (chip + s) % m, axis=0)
        perm = [(i, ((i // 2 + s) % m) * 2 + i % 2) for i in range(n)]
        acc = acc + lax.ppermute(send, axis, perm)
    return acc


def gather_pieces(x, axis):
    n = lax.axis_size(axis)
    pieces = [x]
    for s in range(1, n):
        pieces.append(lax.ppermute(x, axis, [(i, (i + s) % n) for i in range(n)]))
    return jnp.stack(pieces)


def projection_kernel(x_ref, wqk_ref, wvz_ref, wba_t_ref, *outs):
    x = x_ref[...]
    section = outs[0].shape[0]
    width_qk, width_ba = wqk_ref.shape[1], wba_t_ref.shape[0]
    padded_ba = -(-width_ba // 128) * 128
    placed = ((wqk_ref, False, 0), (wba_t_ref, True, width_qk), (wvz_ref, False, width_qk + padded_ba))
    for w_ref, transposed, offset in placed:
        width = w_ref.shape[0 if transposed else 1]
        contract = 1 if transposed else 0
        y = lax.dot_general(
            x, w_ref[...], (((1,), (contract,)), ((), ())), preferred_element_type=jnp.float32
        )
        for i, o_ref in enumerate(outs):
            o_ref[:, offset : offset + width] = y[i * section : (i + 1) * section]
    for o_ref in outs:
        o_ref[:, width_qk + width_ba : width_qk + padded_ba] = jnp.zeros(
            (section, padded_ba - width_ba), jnp.float32
        )


def projection(x, w_qk, w_vz, w_ba, sections):
    rows = x.shape[0] // sections
    padded_ba = -(-w_ba.shape[1] // 128) * 128
    cols = w_qk.shape[1] + padded_ba + w_vz.shape[1]
    return pl.pallas_call(
        projection_kernel,
        out_shape=[jax.ShapeDtypeStruct((rows, cols), jnp.float32)] * sections,
        cost_estimate=pl.CostEstimate(
            flops=2 * x.shape[0] * x.shape[1] * cols,
            bytes_accessed=2 * x.shape[1] * cols + 2 * x.size + 4 * x.shape[0] * cols,
            transcendentals=0,
        ),
    )(x, w_qk, w_vz, w_ba.T)


def recurrence_kernel(gates_ref, qt_ref, kt_ref, v_ref, s_ref, s_out, o_ref, *, heads, steps, ratio):
    r = pl.program_id(0)
    key_heads = heads // ratio
    cols = heads * steps
    for kh in range(key_heads):
        group = [kh * ratio + j for j in range(ratio)]
        states = [s_ref[0, h] for h in group]
        for t in range(steps):
            ck = t * key_heads + kh
            key_col = kt_ref[0, :, ck : ck + 1]
            query_col = qt_ref[0, :, ck : ck + 1]
            for j, h in enumerate(group):
                c = t * heads + h
                lanes = slice(h * DV, (h + 1) * DV)
                state = states[j] * gates_ref[r, cols + c]
                recalled = jnp.sum(key_col * state, axis=0, keepdims=True)
                correction = (v_ref[0, t : t + 1, lanes] - recalled) * gates_ref[r, c]
                state = state + key_col * correction
                o_ref[0, t, h : h + 1, :] = jnp.sum(query_col * state, axis=0, keepdims=True)
                states[j] = state
        for j, h in enumerate(group):
            s_out[0, h] = states[j]


def recurrence(gates, qt, kt, values, memory_state):
    rows, heads = memory_state.shape[0], memory_state.shape[1]
    steps = values.shape[1]
    key_cols = kt.shape[2]
    ratio = heads * steps // key_cols
    kern = functools.partial(recurrence_kernel, heads=heads, steps=steps, ratio=ratio)
    return pl.pallas_call(
        kern,
        grid=(rows,),
        in_specs=[
            pl.BlockSpec(memory_space=pltpu.SMEM),
            pl.BlockSpec((1, DK, key_cols), lambda r: (r, 0, 0)),
            pl.BlockSpec((1, DK, key_cols), lambda r: (r, 0, 0)),
            pl.BlockSpec((1, steps, heads * DV), lambda r: (r, 0, 0)),
            pl.BlockSpec((1, heads, DK, DV), lambda r: (r, 0, 0, 0)),
        ],
        out_specs=[
            pl.BlockSpec((1, heads, DK, DV), lambda r: (r, 0, 0, 0)),
            pl.BlockSpec((1, steps, heads, DV), lambda r: (r, 0, 0, 0)),
        ],
        out_shape=[
            jax.ShapeDtypeStruct(memory_state.shape, jnp.float32),
            jax.ShapeDtypeStruct((rows, steps, heads, DV), jnp.float32),
        ],
        cost_estimate=pl.CostEstimate(
            flops=8 * rows * heads * steps * DK * DV,
            bytes_accessed=2 * memory_state.size * 4,
            transcendentals=0,
        ),
    )(gates, qt, kt, values, memory_state)


def shards(
    activations,
    w_qk,
    w_vz,
    w_ba,
    conv_qk,
    conv_v,
    a_log,
    dt_bias,
    norm_gain,
    w_out,
    conv_state_qk,
    conv_state_v,
    memory_state,
):
    head_ratio = HV // HK
    step_count = activations.shape[1]
    rows_mem = memory_state.shape[0]
    heads = memory_state.shape[1]
    width_qk = w_qk.shape[1]
    width_vz = w_vz.shape[1]

    pieces = gather_pieces(activations, "head")
    n_head, rows_head = pieces.shape[0], pieces.shape[1]
    me_head = lax.axis_index("head")
    n_dp = lax.axis_size("dp")
    chips = n_dp // 2
    me_dp = lax.axis_index("dp")
    core, chip = me_dp % 2, me_dp // 2
    assert rows_head % rows_mem == 0
    sections = []
    for which in (1 - core, core):
        for s in range(chips):
            block = ((chip + s) % chips) * 2 + which
            first = block * rows_mem
            source = (me_head - first // rows_head) % n_head
            offset = first % rows_head
            picked = pieces[0]
            for shift in range(1, n_head):
                picked = jnp.where(source == shift, pieces[shift], picked)
            picked = lax.dynamic_slice_in_dim(picked, offset, rows_mem, axis=0)
            sections.append(picked.reshape(rows_mem * step_count, -1))
    flat_rows = jnp.concatenate(sections, axis=0)
    outs = projection(flat_rows, w_qk, w_vz, w_ba, 2 * chips)
    pair = [(i, i ^ 1) for i in range(n_dp)]
    part = [keep + lax.ppermute(send, "dp", pair) for send, keep in zip(outs[:chips], outs[chips:])]
    width_ba = w_ba.shape[1]
    split = width_qk + (-(-width_ba // 128) * 128)
    summed_first = part[0][:, :split]
    summed_vz = part[0][:, split:]
    for s in range(1, chips):
        perm = [(i, ((i // 2 + s) % chips) * 2 + i % 2) for i in range(n_dp)]
        summed_first = summed_first + lax.ppermute(part[s][:, :split], "dp", perm)
        summed_vz = summed_vz + lax.ppermute(part[s][:, split:], "dp", perm)
    summed_qk = summed_first[:, :width_qk]
    summed_ba = summed_first[:, width_qk : width_qk + width_ba]
    qk_proj = summed_qk.astype(jnp.bfloat16).reshape(rows_mem, step_count, width_qk)
    vz_proj = summed_vz.astype(jnp.bfloat16).reshape(rows_mem, step_count, width_vz)
    ba_proj = summed_ba.astype(jnp.bfloat16).reshape(rows_mem, step_count, -1)

    split_vz = vz_proj.reshape(rows_mem, step_count, heads, 2, DV)
    values_now = split_vz[:, :, :, 0, :].reshape(rows_mem, step_count, heads * DV)
    gate_z = split_vz[:, :, :, 1, :].astype(jnp.float32)

    qk_conv = conv_steps(conv_state_qk, qk_proj, conv_qk).reshape(rows_mem, step_count, -1, 2, DK)
    v_conv = conv_steps(conv_state_v, values_now, conv_v)
    queries = normalize(qk_conv[:, :, :, 0, :]) * DK ** (-0.5)
    key_vec = normalize(qk_conv[:, :, :, 1, :])
    key_heads = queries.shape[2]
    assert key_heads * head_ratio == heads
    qt = queries.transpose(0, 3, 1, 2).reshape(rows_mem, DK, step_count * key_heads)
    kt = key_vec.transpose(0, 3, 1, 2).reshape(rows_mem, DK, step_count * key_heads)

    split_ba = ba_proj.reshape(rows_mem, step_count, heads, 2).astype(jnp.float32)
    beta_gate = jax.nn.sigmoid(split_ba[..., 0])
    log_decay = -jnp.exp(a_log)[None, None, :] * jax.nn.softplus(split_ba[..., 1] + dt_bias[None, None, :])
    gates = jnp.concatenate(
        [beta_gate.reshape(rows_mem, -1), jnp.exp(log_decay).reshape(rows_mem, -1)], axis=1
    )

    new_state, readout = recurrence(gates, qt, kt, v_conv, memory_state)

    scale = lax.rsqrt(jnp.mean(readout * readout, axis=-1, keepdims=True) + 1e-06)
    normed = readout * scale * norm_gain[None, None, None, :] * jax.nn.silu(gate_z)
    normed = normed.astype(jnp.bfloat16)

    all_normed = gather_rows(normed, "dp")
    partials = jnp.einsum(
        "rthd,hde->rte",
        all_normed,
        w_out.reshape(heads, DV, -1),
        preferred_element_type=jnp.float32,
    ).reshape(-1, w_out.shape[1])
    layer_out = scatter_sum_rows(partials, "head")
    layer_out = layer_out.astype(jnp.bfloat16).reshape(-1, step_count, w_out.shape[1])
    return (layer_out, new_state)


def solution(mesh):
    in_specs = (
        P(("groups", "head"), None, "dp"),
        P("dp", "head"),
        P("dp", "head"),
        P("dp", "head"),
        P(None, "head"),
        P(None, "head"),
        P("head"),
        P("head"),
        P(),
        P("head", "dp"),
        P(("groups", "dp"), None, "head"),
        P(("groups", "dp"), None, "head"),
        P(("groups", "dp"), "head", None, None),
    )
    out_specs = (P(("groups", "head"), None, "dp"), P(("groups", "dp"), "head", None, None))
    return jax.shard_map(shards, mesh=mesh, in_specs=in_specs, out_specs=out_specs, check_vma=False)
```

```python
import functools

import jax
import jax.numpy as jnp
from jax import lax
from jax.experimental import pallas as pl
from jax.experimental.pallas import tpu as pltpu
from jax.sharding import PartitionSpec as P

HK = 16
HV = 32
DK = 128
DV = 128


def normalize(vectors):
    return vectors * lax.rsqrt(jnp.sum(vectors * vectors, axis=-1, keepdims=True) + 1e-06)


def conv_steps(state, proj, taps):
    seq = jnp.concatenate([state, proj], axis=1).astype(jnp.float32)
    taps = taps.astype(jnp.float32)
    kernel = taps.shape[0]
    steps = proj.shape[1]
    mixed = sum(seq[:, k : k + steps, :] * taps[k][None, None, :] for k in range(kernel))
    return jax.nn.silu(mixed)


def gather_rows(x, axis):
    n = lax.axis_size(axis)
    me = lax.axis_index(axis)
    pieces = [x]
    for s in range(1, n):
        pieces.append(lax.ppermute(x, axis, [(i, (i + s) % n) for i in range(n)]))
    stacked = jnp.stack(pieces)
    order = (me - jnp.arange(n)) % n
    return jnp.take(stacked, order, axis=0, mode="clip").reshape(n * x.shape[0], *x.shape[1:])


def scatter_sum_rows(x, axis):
    n = lax.axis_size(axis)
    me = lax.axis_index(axis)
    chunks = x.reshape(n, x.shape[0] // n, *x.shape[1:])
    acc = jnp.take(chunks, me, axis=0)
    for s in range(1, n):
        send = jnp.take(chunks, (me + s) % n, axis=0)
        acc = acc + lax.ppermute(send, axis, [(i, (i + s) % n) for i in range(n)])
    return acc


def scatter_sum_rows_paired(x, axis):
    n = lax.axis_size(axis)
    m = n // 2
    me = lax.axis_index(axis)
    core = me % 2
    chip = me // 2
    chunks = x.reshape(m, 2, x.shape[0] // n, *x.shape[1:])
    keep = jnp.take(chunks, core, axis=1)
    send = jnp.take(chunks, 1 - core, axis=1)
    part = keep + lax.ppermute(send, axis, [(i, i ^ 1) for i in range(n)])
    acc = jnp.take(part, chip, axis=0)
    for s in range(1, m):
        send = jnp.take(part, (chip + s) % m, axis=0)
        perm = [(i, ((i // 2 + s) % m) * 2 + i % 2) for i in range(n)]
        acc = acc + lax.ppermute(send, axis, perm)
    return acc


def gather_pieces(x, axis):
    n = lax.axis_size(axis)
    pieces = [x]
    for s in range(1, n):
        pieces.append(lax.ppermute(x, axis, [(i, (i + s) % n) for i in range(n)]))
    return jnp.stack(pieces)


def projection_kernel(x_ref, wqk_ref, wvz_ref, wba_t_ref, *outs):
    x = x_ref[...]
    section = outs[0].shape[0]
    width_qk, width_ba = wqk_ref.shape[1], wba_t_ref.shape[0]
    padded_ba = -(-width_ba // 128) * 128
    placed = ((wqk_ref, False, 0), (wba_t_ref, True, width_qk), (wvz_ref, False, width_qk + padded_ba))
    for w_ref, transposed, offset in placed:
        width = w_ref.shape[0 if transposed else 1]
        contract = 1 if transposed else 0
        y = lax.dot_general(
            x, w_ref[...], (((1,), (contract,)), ((), ())), preferred_element_type=jnp.float32
        )
        if w_ref is wvz_ref:
            half = width // 2
            for h in range(width // (2 * DV)):
                for i, o_ref in enumerate(outs):
                    rows = y[i * section : (i + 1) * section]
                    o_ref[:, offset + h * DV : offset + (h + 1) * DV] = rows[:, 2 * h * DV : (2 * h + 1) * DV]
                    o_ref[:, offset + half + h * DV : offset + half + (h + 1) * DV] = rows[
                        :, (2 * h + 1) * DV : (2 * h + 2) * DV
                    ]
            continue
        for i, o_ref in enumerate(outs):
            o_ref[:, offset : offset + width] = y[i * section : (i + 1) * section]
    for o_ref in outs:
        o_ref[:, width_qk + width_ba : width_qk + padded_ba] = jnp.zeros(
            (section, padded_ba - width_ba), jnp.float32
        )


def projection(x, w_qk, w_vz, w_ba, sections):
    rows = x.shape[0] // sections
    padded_ba = -(-w_ba.shape[1] // 128) * 128
    cols = w_qk.shape[1] + padded_ba + w_vz.shape[1]
    return pl.pallas_call(
        projection_kernel,
        out_shape=[jax.ShapeDtypeStruct((rows, cols), jnp.float32)] * sections,
        cost_estimate=pl.CostEstimate(
            flops=2 * x.shape[0] * x.shape[1] * cols,
            bytes_accessed=2 * x.shape[1] * cols + 2 * x.size + 4 * x.shape[0] * cols,
            transcendentals=0,
        ),
    )(x, w_qk, w_vz, w_ba.T)


def recurrence_kernel(gates_ref, qt_ref, kt_ref, v_ref, s_ref, s_out, o_ref, *, heads, steps, ratio):
    r = pl.program_id(0)
    key_heads = heads // ratio
    cols = heads * steps
    for kh in range(key_heads):
        group = [kh * ratio + j for j in range(ratio)]
        states = [s_ref[0, h] for h in group]
        for t in range(steps):
            ck = t * key_heads + kh
            key_col = kt_ref[0, :, ck : ck + 1]
            query_col = qt_ref[0, :, ck : ck + 1]
            for j, h in enumerate(group):
                c = t * heads + h
                lanes = slice(h * DV, (h + 1) * DV)
                state = states[j] * gates_ref[r, cols + c]
                recalled = jnp.sum(key_col * state, axis=0, keepdims=True)
                correction = (v_ref[0, t : t + 1, lanes] - recalled) * gates_ref[r, c]
                state = state + key_col * correction
                o_ref[0, t, h : h + 1, :] = jnp.sum(query_col * state, axis=0, keepdims=True)
                states[j] = state
        for j, h in enumerate(group):
            s_out[0, h] = states[j]


def recurrence(gates, qt, kt, values, memory_state):
    rows, heads = memory_state.shape[0], memory_state.shape[1]
    steps = values.shape[1]
    key_cols = kt.shape[2]
    ratio = heads * steps // key_cols
    kern = functools.partial(recurrence_kernel, heads=heads, steps=steps, ratio=ratio)
    return pl.pallas_call(
        kern,
        grid=(rows,),
        in_specs=[
            pl.BlockSpec(memory_space=pltpu.SMEM),
            pl.BlockSpec((1, DK, key_cols), lambda r: (r, 0, 0)),
            pl.BlockSpec((1, DK, key_cols), lambda r: (r, 0, 0)),
            pl.BlockSpec((1, steps, heads * DV), lambda r: (r, 0, 0)),
            pl.BlockSpec((1, heads, DK, DV), lambda r: (r, 0, 0, 0)),
        ],
        out_specs=[
            pl.BlockSpec((1, heads, DK, DV), lambda r: (r, 0, 0, 0)),
            pl.BlockSpec((1, steps, heads, DV), lambda r: (r, 0, 0, 0)),
        ],
        out_shape=[
            jax.ShapeDtypeStruct(memory_state.shape, jnp.float32),
            jax.ShapeDtypeStruct((rows, steps, heads, DV), jnp.float32),
        ],
        cost_estimate=pl.CostEstimate(
            flops=8 * rows * heads * steps * DK * DV,
            bytes_accessed=2 * memory_state.size * 4,
            transcendentals=0,
        ),
    )(gates, qt, kt, values, memory_state)


def shards(
    activations,
    w_qk,
    w_vz,
    w_ba,
    conv_qk,
    conv_v,
    a_log,
    dt_bias,
    norm_gain,
    w_out,
    conv_state_qk,
    conv_state_v,
    memory_state,
):
    head_ratio = HV // HK
    step_count = activations.shape[1]
    rows_mem = memory_state.shape[0]
    heads = memory_state.shape[1]
    width_qk = w_qk.shape[1]
    width_vz = w_vz.shape[1]

    pieces = gather_pieces(activations, "head")
    n_head, rows_head = pieces.shape[0], pieces.shape[1]
    me_head = lax.axis_index("head")
    n_dp = lax.axis_size("dp")
    chips = n_dp // 2
    me_dp = lax.axis_index("dp")
    core, chip = me_dp % 2, me_dp // 2
    assert rows_head % rows_mem == 0
    sections = []
    for which in (1 - core, core):
        for s in range(chips):
            block = ((chip + s) % chips) * 2 + which
            first = block * rows_mem
            source = (me_head - first // rows_head) % n_head
            offset = first % rows_head
            picked = pieces[0]
            for shift in range(1, n_head):
                picked = jnp.where(source == shift, pieces[shift], picked)
            picked = lax.dynamic_slice_in_dim(picked, offset, rows_mem, axis=0)
            sections.append(picked.reshape(rows_mem * step_count, -1))
    flat_rows = jnp.concatenate(sections, axis=0)
    outs = projection(flat_rows, w_qk, w_vz, w_ba, 2 * chips)
    pair = [(i, i ^ 1) for i in range(n_dp)]
    part = [keep + lax.ppermute(send, "dp", pair) for send, keep in zip(outs[:chips], outs[chips:])]
    width_ba = w_ba.shape[1]
    split = width_qk + (-(-width_ba // 128) * 128)
    bounds = [(0, split), (split, split + width_vz)]
    summed = [part[0][:, lo:hi] for lo, hi in bounds]
    for s in range(1, chips):
        perm = [(i, ((i // 2 + s) % chips) * 2 + i % 2) for i in range(n_dp)]
        summed = [acc + lax.ppermute(part[s][:, lo:hi], "dp", perm) for acc, (lo, hi) in zip(summed, bounds)]
    summed_first, summed_vz = summed
    summed_v = summed_vz[:, : width_vz // 2]
    summed_z = summed_vz[:, width_vz // 2 :]
    summed_qk = summed_first[:, :width_qk]
    summed_ba = summed_first[:, width_qk : width_qk + width_ba]
    qk_proj = summed_qk.astype(jnp.bfloat16).reshape(rows_mem, step_count, width_qk)
    ba_proj = summed_ba.astype(jnp.bfloat16).reshape(rows_mem, step_count, -1)
    values_now = summed_v.astype(jnp.bfloat16).reshape(rows_mem, step_count, heads * DV)
    gate_z = summed_z.astype(jnp.bfloat16).astype(jnp.float32).reshape(rows_mem, step_count, heads, DV)

    qk_conv = conv_steps(conv_state_qk, qk_proj, conv_qk).reshape(rows_mem, step_count, -1, 2, DK)
    v_conv = conv_steps(conv_state_v, values_now, conv_v)
    queries = normalize(qk_conv[:, :, :, 0, :]) * DK ** (-0.5)
    key_vec = normalize(qk_conv[:, :, :, 1, :])
    key_heads = queries.shape[2]
    assert key_heads * head_ratio == heads
    qt = queries.transpose(0, 3, 1, 2).reshape(rows_mem, DK, step_count * key_heads)
    kt = key_vec.transpose(0, 3, 1, 2).reshape(rows_mem, DK, step_count * key_heads)

    split_ba = ba_proj.reshape(rows_mem, step_count, heads, 2).astype(jnp.float32)
    beta_gate = jax.nn.sigmoid(split_ba[..., 0])
    log_decay = -jnp.exp(a_log)[None, None, :] * jax.nn.softplus(split_ba[..., 1] + dt_bias[None, None, :])
    gates = jnp.concatenate(
        [beta_gate.reshape(rows_mem, -1), jnp.exp(log_decay).reshape(rows_mem, -1)], axis=1
    )

    new_state, readout = recurrence(gates, qt, kt, v_conv, memory_state)

    scale = lax.rsqrt(jnp.mean(readout * readout, axis=-1, keepdims=True) + 1e-06)
    normed = readout * scale * norm_gain[None, None, None, :] * jax.nn.silu(gate_z)
    normed = normed.astype(jnp.bfloat16)

    all_normed = gather_rows(normed, "dp")
    partials = jnp.einsum(
        "rthd,hde->rte",
        all_normed,
        w_out.reshape(heads, DV, -1),
        preferred_element_type=jnp.float32,
    ).reshape(-1, w_out.shape[1])
    layer_out = scatter_sum_rows(partials, "head")
    layer_out = layer_out.astype(jnp.bfloat16).reshape(-1, step_count, w_out.shape[1])
    return (layer_out, new_state)


def solution(mesh):
    in_specs = (
        P(("groups", "head"), None, "dp"),
        P("dp", "head"),
        P("dp", "head"),
        P("dp", "head"),
        P(None, "head"),
        P(None, "head"),
        P("head"),
        P("head"),
        P(),
        P("head", "dp"),
        P(("groups", "dp"), None, "head"),
        P(("groups", "dp"), None, "head"),
        P(("groups", "dp"), "head", None, None),
    )
    out_specs = (P(("groups", "head"), None, "dp"), P(("groups", "dp"), "head", None, None))
    return jax.shard_map(shards, mesh=mesh, in_specs=in_specs, out_specs=out_specs, check_vma=False)
```

```python
import functools

import jax
import jax.numpy as jnp
from jax import lax
from jax.experimental import pallas as pl
from jax.experimental.pallas import tpu as pltpu
from jax.sharding import PartitionSpec as P

HK = 16
HV = 32
DK = 128
DV = 128


def normalize(vectors):
    return vectors * lax.rsqrt(jnp.sum(vectors * vectors, axis=-1, keepdims=True) + 1e-06)


def conv_steps(state, proj, taps):
    seq = jnp.concatenate([state, proj], axis=1).astype(jnp.float32)
    taps = taps.astype(jnp.float32)
    kernel = taps.shape[0]
    steps = proj.shape[1]
    mixed = sum(seq[:, k : k + steps, :] * taps[k][None, None, :] for k in range(kernel))
    return jax.nn.silu(mixed)


def gather_rows(x, axis):
    n = lax.axis_size(axis)
    me = lax.axis_index(axis)
    pieces = [x]
    for s in range(1, n):
        pieces.append(lax.ppermute(x, axis, [(i, (i + s) % n) for i in range(n)]))
    stacked = jnp.stack(pieces)
    order = (me - jnp.arange(n)) % n
    return jnp.take(stacked, order, axis=0, mode="clip").reshape(n * x.shape[0], *x.shape[1:])


def scatter_sum_rows(x, axis):
    n = lax.axis_size(axis)
    me = lax.axis_index(axis)
    chunks = x.reshape(n, x.shape[0] // n, *x.shape[1:])
    acc = jnp.take(chunks, me, axis=0)
    for s in range(1, n):
        send = jnp.take(chunks, (me + s) % n, axis=0)
        acc = acc + lax.ppermute(send, axis, [(i, (i + s) % n) for i in range(n)])
    return acc


def scatter_sum_rows_paired(x, axis):
    n = lax.axis_size(axis)
    m = n // 2
    me = lax.axis_index(axis)
    core = me % 2
    chip = me // 2
    chunks = x.reshape(m, 2, x.shape[0] // n, *x.shape[1:])
    keep = jnp.take(chunks, core, axis=1)
    send = jnp.take(chunks, 1 - core, axis=1)
    part = keep + lax.ppermute(send, axis, [(i, i ^ 1) for i in range(n)])
    acc = jnp.take(part, chip, axis=0)
    for s in range(1, m):
        send = jnp.take(part, (chip + s) % m, axis=0)
        perm = [(i, ((i // 2 + s) % m) * 2 + i % 2) for i in range(n)]
        acc = acc + lax.ppermute(send, axis, perm)
    return acc


def gather_pieces(x, axis):
    n = lax.axis_size(axis)
    pieces = [x]
    for s in range(1, n):
        pieces.append(lax.ppermute(x, axis, [(i, (i + s) % n) for i in range(n)]))
    return jnp.stack(pieces)


def projection_kernel(x_ref, wqk_ref, wvz_ref, wba_t_ref, *outs):
    x = x_ref[...]
    section = outs[0].shape[0]
    width_qk, width_ba = wqk_ref.shape[1], wba_t_ref.shape[0]
    padded_ba = -(-width_ba // 128) * 128
    placed = ((wqk_ref, False, 0), (wba_t_ref, True, width_qk), (wvz_ref, False, width_qk + padded_ba))
    for w_ref, transposed, offset in placed:
        width = w_ref.shape[0 if transposed else 1]
        contract = 1 if transposed else 0
        y = lax.dot_general(
            x, w_ref[...], (((1,), (contract,)), ((), ())), preferred_element_type=jnp.float32
        )
        if w_ref is wvz_ref:
            half = width // 2
            for h in range(width // (2 * DV)):
                for i, o_ref in enumerate(outs):
                    rows = y[i * section : (i + 1) * section]
                    o_ref[:, offset + h * DV : offset + (h + 1) * DV] = rows[:, 2 * h * DV : (2 * h + 1) * DV]
                    o_ref[:, offset + half + h * DV : offset + half + (h + 1) * DV] = rows[
                        :, (2 * h + 1) * DV : (2 * h + 2) * DV
                    ]
            continue
        for i, o_ref in enumerate(outs):
            o_ref[:, offset : offset + width] = y[i * section : (i + 1) * section]
    for o_ref in outs:
        o_ref[:, width_qk + width_ba : width_qk + padded_ba] = jnp.zeros(
            (section, padded_ba - width_ba), jnp.float32
        )


def projection(x, w_qk, w_vz, w_ba, sections):
    rows = x.shape[0] // sections
    padded_ba = -(-w_ba.shape[1] // 128) * 128
    cols = w_qk.shape[1] + padded_ba + w_vz.shape[1]
    return pl.pallas_call(
        projection_kernel,
        out_shape=[jax.ShapeDtypeStruct((rows, cols), jnp.float32)] * sections,
        cost_estimate=pl.CostEstimate(
            flops=2 * x.shape[0] * x.shape[1] * cols,
            bytes_accessed=2 * x.shape[1] * cols + 2 * x.size + 4 * x.shape[0] * cols,
            transcendentals=0,
        ),
    )(x, w_qk, w_vz, w_ba.T)


def recurrence_kernel(gates_ref, qt_ref, kt_ref, v_ref, s_ref, s_out, o_ref, *, heads, steps, ratio):
    r = pl.program_id(0)
    key_heads = heads // ratio
    cols = heads * steps
    for kh in range(key_heads):
        group = [kh * ratio + j for j in range(ratio)]
        states = [s_ref[0, h] for h in group]
        for t in range(steps):
            ck = t * key_heads + kh
            key_col = kt_ref[0, :, ck : ck + 1]
            query_col = qt_ref[0, :, ck : ck + 1]
            for j, h in enumerate(group):
                c = t * heads + h
                lanes = slice(h * DV, (h + 1) * DV)
                state = states[j] * gates_ref[r, cols + c]
                recalled = jnp.sum(key_col * state, axis=0, keepdims=True)
                correction = (v_ref[0, t : t + 1, lanes] - recalled) * gates_ref[r, c]
                state = state + key_col * correction
                o_ref[0, t, h : h + 1, :] = jnp.sum(query_col * state, axis=0, keepdims=True)
                states[j] = state
        for j, h in enumerate(group):
            s_out[0, h] = states[j]


def recurrence(gates, qt, kt, values, memory_state):
    rows, heads = memory_state.shape[0], memory_state.shape[1]
    steps = values.shape[1]
    key_cols = kt.shape[2]
    ratio = heads * steps // key_cols
    kern = functools.partial(recurrence_kernel, heads=heads, steps=steps, ratio=ratio)
    return pl.pallas_call(
        kern,
        grid=(rows,),
        in_specs=[
            pl.BlockSpec(memory_space=pltpu.SMEM),
            pl.BlockSpec((1, DK, key_cols), lambda r: (r, 0, 0)),
            pl.BlockSpec((1, DK, key_cols), lambda r: (r, 0, 0)),
            pl.BlockSpec((1, steps, heads * DV), lambda r: (r, 0, 0)),
            pl.BlockSpec((1, heads, DK, DV), lambda r: (r, 0, 0, 0)),
        ],
        out_specs=[
            pl.BlockSpec((1, heads, DK, DV), lambda r: (r, 0, 0, 0)),
            pl.BlockSpec((1, steps, heads, DV), lambda r: (r, 0, 0, 0)),
        ],
        out_shape=[
            jax.ShapeDtypeStruct(memory_state.shape, jnp.float32),
            jax.ShapeDtypeStruct((rows, steps, heads, DV), jnp.float32),
        ],
        cost_estimate=pl.CostEstimate(
            flops=8 * rows * heads * steps * DK * DV,
            bytes_accessed=2 * memory_state.size * 4,
            transcendentals=0,
        ),
    )(gates, qt, kt, values, memory_state)


def shards(
    activations,
    w_qk,
    w_vz,
    w_ba,
    conv_qk,
    conv_v,
    a_log,
    dt_bias,
    norm_gain,
    w_out,
    conv_state_qk,
    conv_state_v,
    memory_state,
):
    head_ratio = HV // HK
    step_count = activations.shape[1]
    rows_mem = memory_state.shape[0]
    heads = memory_state.shape[1]
    width_qk = w_qk.shape[1]
    width_vz = w_vz.shape[1]

    pieces = gather_pieces(activations, "head")
    n_head, rows_head = pieces.shape[0], pieces.shape[1]
    me_head = lax.axis_index("head")
    n_dp = lax.axis_size("dp")
    chips = n_dp // 2
    me_dp = lax.axis_index("dp")
    core, chip = me_dp % 2, me_dp // 2
    assert rows_head % rows_mem == 0
    sections = []
    for which in (1 - core, core):
        for s in range(chips):
            block = ((chip + s) % chips) * 2 + which
            first = block * rows_mem
            source = (me_head - first // rows_head) % n_head
            offset = first % rows_head
            picked = pieces[0]
            for shift in range(1, n_head):
                picked = jnp.where(source == shift, pieces[shift], picked)
            picked = lax.dynamic_slice_in_dim(picked, offset, rows_mem, axis=0)
            sections.append(picked.reshape(rows_mem * step_count, -1))
    flat_rows = jnp.concatenate(sections, axis=0)
    outs = projection(flat_rows, w_qk, w_vz, w_ba, 2 * chips)
    width_ba = w_ba.shape[1]
    split = width_qk + (-(-width_ba // 128) * 128)
    bounds = [(0, split), (split, split + width_vz)]
    pair = [(i, i ^ 1) for i in range(n_dp)]
    part = [
        [keep[:, lo:hi] + lax.ppermute(send[:, lo:hi], "dp", pair) for lo, hi in bounds]
        for send, keep in zip(outs[:chips], outs[chips:])
    ]
    summed = list(part[0])
    for s in range(1, chips):
        perm = [(i, ((i // 2 + s) % chips) * 2 + i % 2) for i in range(n_dp)]
        summed = [acc + lax.ppermute(piece, "dp", perm) for acc, piece in zip(summed, part[s])]
    summed_first, summed_vz = summed
    summed_v = summed_vz[:, : width_vz // 2]
    summed_z = summed_vz[:, width_vz // 2 :]
    summed_qk = summed_first[:, :width_qk]
    summed_ba = summed_first[:, width_qk : width_qk + width_ba]
    qk_proj = summed_qk.astype(jnp.bfloat16).reshape(rows_mem, step_count, width_qk)
    ba_proj = summed_ba.astype(jnp.bfloat16).reshape(rows_mem, step_count, -1)
    values_now = summed_v.astype(jnp.bfloat16).reshape(rows_mem, step_count, heads * DV)
    gate_z = summed_z.astype(jnp.bfloat16).astype(jnp.float32).reshape(rows_mem, step_count, heads, DV)

    qk_conv = conv_steps(conv_state_qk, qk_proj, conv_qk).reshape(rows_mem, step_count, -1, 2, DK)
    v_conv = conv_steps(conv_state_v, values_now, conv_v)
    queries = normalize(qk_conv[:, :, :, 0, :]) * DK ** (-0.5)
    key_vec = normalize(qk_conv[:, :, :, 1, :])
    key_heads = queries.shape[2]
    assert key_heads * head_ratio == heads
    qt = queries.transpose(0, 3, 1, 2).reshape(rows_mem, DK, step_count * key_heads)
    kt = key_vec.transpose(0, 3, 1, 2).reshape(rows_mem, DK, step_count * key_heads)

    split_ba = ba_proj.reshape(rows_mem, step_count, heads, 2).astype(jnp.float32)
    beta_gate = jax.nn.sigmoid(split_ba[..., 0])
    log_decay = -jnp.exp(a_log)[None, None, :] * jax.nn.softplus(split_ba[..., 1] + dt_bias[None, None, :])
    gates = jnp.concatenate(
        [beta_gate.reshape(rows_mem, -1), jnp.exp(log_decay).reshape(rows_mem, -1)], axis=1
    )

    new_state, readout = recurrence(gates, qt, kt, v_conv, memory_state)

    scale = lax.rsqrt(jnp.mean(readout * readout, axis=-1, keepdims=True) + 1e-06)
    normed = readout * scale * norm_gain[None, None, None, :] * jax.nn.silu(gate_z)
    normed = normed.astype(jnp.bfloat16)

    all_normed = gather_rows(normed, "dp")
    partials = jnp.einsum(
        "rthd,hde->rte",
        all_normed,
        w_out.reshape(heads, DV, -1),
        preferred_element_type=jnp.float32,
    ).reshape(-1, w_out.shape[1])
    layer_out = scatter_sum_rows(partials, "head")
    layer_out = layer_out.astype(jnp.bfloat16).reshape(-1, step_count, w_out.shape[1])
    return (layer_out, new_state)


def solution(mesh):
    in_specs = (
        P(("groups", "head"), None, "dp"),
        P("dp", "head"),
        P("dp", "head"),
        P("dp", "head"),
        P(None, "head"),
        P(None, "head"),
        P("head"),
        P("head"),
        P(),
        P("head", "dp"),
        P(("groups", "dp"), None, "head"),
        P(("groups", "dp"), None, "head"),
        P(("groups", "dp"), "head", None, None),
    )
    out_specs = (P(("groups", "head"), None, "dp"), P(("groups", "dp"), "head", None, None))
    return jax.shard_map(shards, mesh=mesh, in_specs=in_specs, out_specs=out_specs, check_vma=False)
```

```python
import functools

import jax
import jax.numpy as jnp
from jax import lax
from jax.experimental import pallas as pl
from jax.experimental.pallas import tpu as pltpu
from jax.sharding import PartitionSpec as P

HK = 16
HV = 32
DK = 128
DV = 128


def normalize(vectors):
    return vectors * lax.rsqrt(jnp.sum(vectors * vectors, axis=-1, keepdims=True) + 1e-06)


def conv_steps(state, proj, taps):
    seq = jnp.concatenate([state, proj], axis=1).astype(jnp.float32)
    taps = taps.astype(jnp.float32)
    kernel = taps.shape[0]
    steps = proj.shape[1]
    mixed = sum(seq[:, k : k + steps, :] * taps[k][None, None, :] for k in range(kernel))
    return jax.nn.silu(mixed)


def gather_rows(x, axis):
    n = lax.axis_size(axis)
    me = lax.axis_index(axis)
    pieces = [x]
    for s in range(1, n):
        pieces.append(lax.ppermute(x, axis, [(i, (i + s) % n) for i in range(n)]))
    stacked = jnp.stack(pieces)
    order = (me - jnp.arange(n)) % n
    return jnp.take(stacked, order, axis=0, mode="clip").reshape(n * x.shape[0], *x.shape[1:])


def scatter_sum_rows(x, axis):
    n = lax.axis_size(axis)
    me = lax.axis_index(axis)
    chunks = x.reshape(n, x.shape[0] // n, *x.shape[1:])
    acc = jnp.take(chunks, me, axis=0)
    for s in range(1, n):
        send = jnp.take(chunks, (me + s) % n, axis=0)
        acc = acc + lax.ppermute(send, axis, [(i, (i + s) % n) for i in range(n)])
    return acc


def scatter_sum_rows_paired(x, axis):
    n = lax.axis_size(axis)
    m = n // 2
    me = lax.axis_index(axis)
    core = me % 2
    chip = me // 2
    chunks = x.reshape(m, 2, x.shape[0] // n, *x.shape[1:])
    keep = jnp.take(chunks, core, axis=1)
    send = jnp.take(chunks, 1 - core, axis=1)
    part = keep + lax.ppermute(send, axis, [(i, i ^ 1) for i in range(n)])
    acc = jnp.take(part, chip, axis=0)
    for s in range(1, m):
        send = jnp.take(part, (chip + s) % m, axis=0)
        perm = [(i, ((i // 2 + s) % m) * 2 + i % 2) for i in range(n)]
        acc = acc + lax.ppermute(send, axis, perm)
    return acc


def gather_pieces(x, axis):
    n = lax.axis_size(axis)
    pieces = [x]
    for s in range(1, n):
        pieces.append(lax.ppermute(x, axis, [(i, (i + s) % n) for i in range(n)]))
    return jnp.stack(pieces)


def projection_kernel(x_ref, wqk_ref, wvz_ref, wba_t_ref, *outs):
    x = x_ref[...]
    section = outs[0].shape[0]
    width_qk, width_ba = wqk_ref.shape[1], wba_t_ref.shape[0]
    padded_ba = -(-width_ba // 128) * 128
    placed = ((wqk_ref, False, 0), (wba_t_ref, True, width_qk), (wvz_ref, False, width_qk + padded_ba))
    for w_ref, transposed, offset in placed:
        width = w_ref.shape[0 if transposed else 1]
        contract = 1 if transposed else 0
        y = lax.dot_general(
            x, w_ref[...], (((1,), (contract,)), ((), ())), preferred_element_type=jnp.float32
        )
        if w_ref is wvz_ref:
            half = width // 2
            for h in range(width // (2 * DV)):
                for i, o_ref in enumerate(outs):
                    rows = y[i * section : (i + 1) * section]
                    o_ref[:, offset + h * DV : offset + (h + 1) * DV] = rows[:, 2 * h * DV : (2 * h + 1) * DV]
                    o_ref[:, offset + half + h * DV : offset + half + (h + 1) * DV] = rows[
                        :, (2 * h + 1) * DV : (2 * h + 2) * DV
                    ]
            continue
        for i, o_ref in enumerate(outs):
            o_ref[:, offset : offset + width] = y[i * section : (i + 1) * section]
    for o_ref in outs:
        o_ref[:, width_qk + width_ba : width_qk + padded_ba] = jnp.zeros(
            (section, padded_ba - width_ba), jnp.float32
        )


def projection(x, w_qk, w_vz, w_ba, sections):
    rows = x.shape[0] // sections
    padded_ba = -(-w_ba.shape[1] // 128) * 128
    cols = w_qk.shape[1] + padded_ba + w_vz.shape[1]
    return pl.pallas_call(
        projection_kernel,
        out_shape=[jax.ShapeDtypeStruct((rows, cols), jnp.float32)] * sections,
        cost_estimate=pl.CostEstimate(
            flops=2 * x.shape[0] * x.shape[1] * cols,
            bytes_accessed=2 * x.shape[1] * cols + 2 * x.size + 4 * x.shape[0] * cols,
            transcendentals=0,
        ),
    )(x, w_qk, w_vz, w_ba.T)


def recurrence_kernel(gates_ref, qt_ref, kt_ref, v_ref, s_ref, s_out, o_ref, *, heads, steps, ratio, block):
    key_heads = heads // ratio
    cols = heads * steps
    for b in range(block):
        recurrence_row(gates_ref, qt_ref, kt_ref, v_ref, s_ref, s_out, o_ref, b, heads, steps, ratio)


def recurrence_row(gates_ref, qt_ref, kt_ref, v_ref, s_ref, s_out, o_ref, b, heads, steps, ratio):
    r = pl.program_id(0) * s_ref.shape[0] + b
    key_heads = heads // ratio
    cols = heads * steps
    for kh in range(key_heads):
        group = [kh * ratio + j for j in range(ratio)]
        states = [s_ref[b, h] for h in group]
        for t in range(steps):
            ck = t * key_heads + kh
            key_col = kt_ref[b, :, ck : ck + 1]
            query_col = qt_ref[b, :, ck : ck + 1]
            for j, h in enumerate(group):
                c = t * heads + h
                lanes = slice(h * DV, (h + 1) * DV)
                state = states[j] * gates_ref[r, cols + c]
                recalled = jnp.sum(key_col * state, axis=0, keepdims=True)
                correction = (v_ref[b, t : t + 1, lanes] - recalled) * gates_ref[r, c]
                state = state + key_col * correction
                o_ref[b, t, h : h + 1, :] = jnp.sum(query_col * state, axis=0, keepdims=True)
                states[j] = state
        for j, h in enumerate(group):
            s_out[b, h] = states[j]


def recurrence(gates, qt, kt, values, memory_state):
    rows, heads = memory_state.shape[0], memory_state.shape[1]
    steps = values.shape[1]
    key_cols = kt.shape[2]
    ratio = heads * steps // key_cols
    block = 2 if rows % 2 == 0 else 1
    kern = functools.partial(recurrence_kernel, heads=heads, steps=steps, ratio=ratio, block=block)
    return pl.pallas_call(
        kern,
        grid=(rows // block,),
        in_specs=[
            pl.BlockSpec(memory_space=pltpu.SMEM),
            pl.BlockSpec((block, DK, key_cols), lambda r: (r, 0, 0)),
            pl.BlockSpec((block, DK, key_cols), lambda r: (r, 0, 0)),
            pl.BlockSpec((block, steps, heads * DV), lambda r: (r, 0, 0)),
            pl.BlockSpec((block, heads, DK, DV), lambda r: (r, 0, 0, 0)),
        ],
        out_specs=[
            pl.BlockSpec((block, heads, DK, DV), lambda r: (r, 0, 0, 0)),
            pl.BlockSpec((block, steps, heads, DV), lambda r: (r, 0, 0, 0)),
        ],
        out_shape=[
            jax.ShapeDtypeStruct(memory_state.shape, jnp.float32),
            jax.ShapeDtypeStruct((rows, steps, heads, DV), jnp.float32),
        ],
        cost_estimate=pl.CostEstimate(
            flops=8 * rows * heads * steps * DK * DV,
            bytes_accessed=2 * memory_state.size * 4,
            transcendentals=0,
        ),
    )(gates, qt, kt, values, memory_state)


def shards(
    activations,
    w_qk,
    w_vz,
    w_ba,
    conv_qk,
    conv_v,
    a_log,
    dt_bias,
    norm_gain,
    w_out,
    conv_state_qk,
    conv_state_v,
    memory_state,
):
    head_ratio = HV // HK
    step_count = activations.shape[1]
    rows_mem = memory_state.shape[0]
    heads = memory_state.shape[1]
    width_qk = w_qk.shape[1]
    width_vz = w_vz.shape[1]

    pieces = gather_pieces(activations, "head")
    n_head, rows_head = pieces.shape[0], pieces.shape[1]
    me_head = lax.axis_index("head")
    n_dp = lax.axis_size("dp")
    chips = n_dp // 2
    me_dp = lax.axis_index("dp")
    core, chip = me_dp % 2, me_dp // 2
    assert rows_head % rows_mem == 0
    sections = []
    for which in (1 - core, core):
        for s in range(chips):
            block = ((chip + s) % chips) * 2 + which
            first = block * rows_mem
            source = (me_head - first // rows_head) % n_head
            offset = first % rows_head
            picked = pieces[0]
            for shift in range(1, n_head):
                picked = jnp.where(source == shift, pieces[shift], picked)
            picked = lax.dynamic_slice_in_dim(picked, offset, rows_mem, axis=0)
            sections.append(picked.reshape(rows_mem * step_count, -1))
    flat_rows = jnp.concatenate(sections, axis=0)
    outs = projection(flat_rows, w_qk, w_vz, w_ba, 2 * chips)
    pair = [(i, i ^ 1) for i in range(n_dp)]
    part = [keep + lax.ppermute(send, "dp", pair) for send, keep in zip(outs[:chips], outs[chips:])]
    width_ba = w_ba.shape[1]
    split = width_qk + (-(-width_ba // 128) * 128)
    bounds = [(0, split), (split, split + width_vz)]
    summed = [part[0][:, lo:hi] for lo, hi in bounds]
    for s in range(1, chips):
        perm = [(i, ((i // 2 + s) % chips) * 2 + i % 2) for i in range(n_dp)]
        summed = [acc + lax.ppermute(part[s][:, lo:hi], "dp", perm) for acc, (lo, hi) in zip(summed, bounds)]
    summed_first, summed_vz = summed
    summed_v = summed_vz[:, : width_vz // 2]
    summed_z = summed_vz[:, width_vz // 2 :]
    summed_qk = summed_first[:, :width_qk]
    summed_ba = summed_first[:, width_qk : width_qk + width_ba]
    qk_proj = summed_qk.astype(jnp.bfloat16).reshape(rows_mem, step_count, width_qk)
    ba_proj = summed_ba.astype(jnp.bfloat16).reshape(rows_mem, step_count, -1)
    values_now = summed_v.astype(jnp.bfloat16).reshape(rows_mem, step_count, heads * DV)
    gate_z = summed_z.astype(jnp.bfloat16).astype(jnp.float32).reshape(rows_mem, step_count, heads, DV)

    qk_conv = conv_steps(conv_state_qk, qk_proj, conv_qk).reshape(rows_mem, step_count, -1, 2, DK)
    v_conv = conv_steps(conv_state_v, values_now, conv_v)
    queries = normalize(qk_conv[:, :, :, 0, :]) * DK ** (-0.5)
    key_vec = normalize(qk_conv[:, :, :, 1, :])
    key_heads = queries.shape[2]
    assert key_heads * head_ratio == heads
    qt = queries.transpose(0, 3, 1, 2).reshape(rows_mem, DK, step_count * key_heads)
    kt = key_vec.transpose(0, 3, 1, 2).reshape(rows_mem, DK, step_count * key_heads)

    split_ba = ba_proj.reshape(rows_mem, step_count, heads, 2).astype(jnp.float32)
    beta_gate = jax.nn.sigmoid(split_ba[..., 0])
    log_decay = -jnp.exp(a_log)[None, None, :] * jax.nn.softplus(split_ba[..., 1] + dt_bias[None, None, :])
    gates = jnp.concatenate(
        [beta_gate.reshape(rows_mem, -1), jnp.exp(log_decay).reshape(rows_mem, -1)], axis=1
    )

    new_state, readout = recurrence(gates, qt, kt, v_conv, memory_state)

    scale = lax.rsqrt(jnp.mean(readout * readout, axis=-1, keepdims=True) + 1e-06)
    normed = readout * scale * norm_gain[None, None, None, :] * jax.nn.silu(gate_z)
    normed = normed.astype(jnp.bfloat16)

    all_normed = gather_rows(normed, "dp")
    partials = jnp.einsum(
        "rthd,hde->rte",
        all_normed,
        w_out.reshape(heads, DV, -1),
        preferred_element_type=jnp.float32,
    ).reshape(-1, w_out.shape[1])
    layer_out = scatter_sum_rows(partials, "head")
    layer_out = layer_out.astype(jnp.bfloat16).reshape(-1, step_count, w_out.shape[1])
    return (layer_out, new_state)


def solution(mesh):
    in_specs = (
        P(("groups", "head"), None, "dp"),
        P("dp", "head"),
        P("dp", "head"),
        P("dp", "head"),
        P(None, "head"),
        P(None, "head"),
        P("head"),
        P("head"),
        P(),
        P("head", "dp"),
        P(("groups", "dp"), None, "head"),
        P(("groups", "dp"), None, "head"),
        P(("groups", "dp"), "head", None, None),
    )
    out_specs = (P(("groups", "head"), None, "dp"), P(("groups", "dp"), "head", None, None))
    return jax.shard_map(shards, mesh=mesh, in_specs=in_specs, out_specs=out_specs, check_vma=False)
```

```python
import functools

import jax
import jax.numpy as jnp
from jax import lax
from jax.experimental import pallas as pl
from jax.experimental.pallas import tpu as pltpu
from jax.sharding import PartitionSpec as P

HK = 16
HV = 32
DK = 128
DV = 128


def normalize(vectors):
    return vectors * lax.rsqrt(jnp.sum(vectors * vectors, axis=-1, keepdims=True) + 1e-06)


def conv_steps(state, proj, taps):
    seq = jnp.concatenate([state, proj], axis=1).astype(jnp.float32)
    taps = taps.astype(jnp.float32)
    kernel = taps.shape[0]
    steps = proj.shape[1]
    mixed = sum(seq[:, k : k + steps, :] * taps[k][None, None, :] for k in range(kernel))
    return jax.nn.silu(mixed)


def gather_rows(x, axis):
    n = lax.axis_size(axis)
    me = lax.axis_index(axis)
    pieces = [x]
    for s in range(1, n):
        pieces.append(lax.ppermute(x, axis, [(i, (i + s) % n) for i in range(n)]))
    stacked = jnp.stack(pieces)
    order = (me - jnp.arange(n)) % n
    return jnp.take(stacked, order, axis=0, mode="clip").reshape(n * x.shape[0], *x.shape[1:])


def scatter_sum_rows(x, axis):
    n = lax.axis_size(axis)
    me = lax.axis_index(axis)
    chunks = x.reshape(n, x.shape[0] // n, *x.shape[1:])
    acc = jnp.take(chunks, me, axis=0)
    for s in range(1, n):
        send = jnp.take(chunks, (me + s) % n, axis=0)
        acc = acc + lax.ppermute(send, axis, [(i, (i + s) % n) for i in range(n)])
    return acc


def scatter_sum_rows_paired(x, axis):
    n = lax.axis_size(axis)
    m = n // 2
    me = lax.axis_index(axis)
    core = me % 2
    chip = me // 2
    chunks = x.reshape(m, 2, x.shape[0] // n, *x.shape[1:])
    keep = jnp.take(chunks, core, axis=1)
    send = jnp.take(chunks, 1 - core, axis=1)
    part = keep + lax.ppermute(send, axis, [(i, i ^ 1) for i in range(n)])
    acc = jnp.take(part, chip, axis=0)
    for s in range(1, m):
        send = jnp.take(part, (chip + s) % m, axis=0)
        perm = [(i, ((i // 2 + s) % m) * 2 + i % 2) for i in range(n)]
        acc = acc + lax.ppermute(send, axis, perm)
    return acc


def gather_pieces(x, axis):
    n = lax.axis_size(axis)
    pieces = [x]
    for s in range(1, n):
        pieces.append(lax.ppermute(x, axis, [(i, (i + s) % n) for i in range(n)]))
    return jnp.stack(pieces)


def projection_kernel(x_ref, wqk_ref, wvz_ref, wba_t_ref, *outs):
    x = x_ref[...]
    section = outs[0].shape[0]
    width_qk, width_ba = wqk_ref.shape[1], wba_t_ref.shape[0]
    padded_ba = -(-width_ba // 128) * 128
    placed = ((wqk_ref, False, 0), (wba_t_ref, True, width_qk), (wvz_ref, False, width_qk + padded_ba))
    for w_ref, transposed, offset in placed:
        width = w_ref.shape[0 if transposed else 1]
        contract = 1 if transposed else 0
        y = lax.dot_general(
            x, w_ref[...], (((1,), (contract,)), ((), ())), preferred_element_type=jnp.float32
        )
        if w_ref is wvz_ref:
            half = width // 2
            for h in range(width // (2 * DV)):
                for i, o_ref in enumerate(outs):
                    rows = y[i * section : (i + 1) * section]
                    o_ref[:, offset + h * DV : offset + (h + 1) * DV] = rows[:, 2 * h * DV : (2 * h + 1) * DV]
                    o_ref[:, offset + half + h * DV : offset + half + (h + 1) * DV] = rows[
                        :, (2 * h + 1) * DV : (2 * h + 2) * DV
                    ]
            continue
        for i, o_ref in enumerate(outs):
            o_ref[:, offset : offset + width] = y[i * section : (i + 1) * section]
    for o_ref in outs:
        o_ref[:, width_qk + width_ba : width_qk + padded_ba] = jnp.zeros(
            (section, padded_ba - width_ba), jnp.float32
        )


def projection(x, w_qk, w_vz, w_ba, sections):
    rows = x.shape[0] // sections
    padded_ba = -(-w_ba.shape[1] // 128) * 128
    cols = w_qk.shape[1] + padded_ba + w_vz.shape[1]
    return pl.pallas_call(
        projection_kernel,
        out_shape=[jax.ShapeDtypeStruct((rows, cols), jnp.float32)] * sections,
        cost_estimate=pl.CostEstimate(
            flops=2 * x.shape[0] * x.shape[1] * cols,
            bytes_accessed=2 * x.shape[1] * cols + 2 * x.size + 4 * x.shape[0] * cols,
            transcendentals=0,
        ),
    )(x, w_qk, w_vz, w_ba.T)


def recurrence_kernel(gates_ref, qt_ref, kt_ref, v_ref, s_ref, s_out, o_ref, *, heads, steps, ratio, block):
    key_heads = heads // ratio
    cols = heads * steps
    for b in range(block):
        recurrence_row(gates_ref, qt_ref, kt_ref, v_ref, s_ref, s_out, o_ref, b, heads, steps, ratio)


def recurrence_row(gates_ref, qt_ref, kt_ref, v_ref, s_ref, s_out, o_ref, b, heads, steps, ratio):
    r = pl.program_id(0) * s_ref.shape[0] + b
    key_heads = heads // ratio
    cols = heads * steps
    for kh in range(key_heads):
        group = [kh * ratio + j for j in range(ratio)]
        states = [s_ref[b, h] for h in group]
        for t in range(steps):
            ck = t * key_heads + kh
            key_col = kt_ref[b, :, ck : ck + 1]
            query_col = qt_ref[b, :, ck : ck + 1]
            for j, h in enumerate(group):
                c = t * heads + h
                lanes = slice(h * DV, (h + 1) * DV)
                state = states[j] * gates_ref[r, cols + c]
                recalled = jnp.sum(key_col * state, axis=0, keepdims=True)
                correction = (v_ref[b, t : t + 1, lanes] - recalled) * gates_ref[r, c]
                state = state + key_col * correction
                o_ref[b, t, h : h + 1, :] = jnp.sum(query_col * state, axis=0, keepdims=True)
                states[j] = state
        for j, h in enumerate(group):
            s_out[b, h] = states[j]


def recurrence(gates, qt, kt, values, memory_state):
    rows, heads = memory_state.shape[0], memory_state.shape[1]
    steps = values.shape[1]
    key_cols = kt.shape[2]
    ratio = heads * steps // key_cols
    block = 4 if rows % 4 == 0 else 1
    kern = functools.partial(recurrence_kernel, heads=heads, steps=steps, ratio=ratio, block=block)
    return pl.pallas_call(
        kern,
        grid=(rows // block,),
        in_specs=[
            pl.BlockSpec(memory_space=pltpu.SMEM),
            pl.BlockSpec((block, DK, key_cols), lambda r: (r, 0, 0)),
            pl.BlockSpec((block, DK, key_cols), lambda r: (r, 0, 0)),
            pl.BlockSpec((block, steps, heads * DV), lambda r: (r, 0, 0)),
            pl.BlockSpec((block, heads, DK, DV), lambda r: (r, 0, 0, 0)),
        ],
        out_specs=[
            pl.BlockSpec((block, heads, DK, DV), lambda r: (r, 0, 0, 0)),
            pl.BlockSpec((block, steps, heads, DV), lambda r: (r, 0, 0, 0)),
        ],
        out_shape=[
            jax.ShapeDtypeStruct(memory_state.shape, jnp.float32),
            jax.ShapeDtypeStruct((rows, steps, heads, DV), jnp.float32),
        ],
        cost_estimate=pl.CostEstimate(
            flops=8 * rows * heads * steps * DK * DV,
            bytes_accessed=2 * memory_state.size * 4,
            transcendentals=0,
        ),
    )(gates, qt, kt, values, memory_state)


def shards(
    activations,
    w_qk,
    w_vz,
    w_ba,
    conv_qk,
    conv_v,
    a_log,
    dt_bias,
    norm_gain,
    w_out,
    conv_state_qk,
    conv_state_v,
    memory_state,
):
    head_ratio = HV // HK
    step_count = activations.shape[1]
    rows_mem = memory_state.shape[0]
    heads = memory_state.shape[1]
    width_qk = w_qk.shape[1]
    width_vz = w_vz.shape[1]

    pieces = gather_pieces(activations, "head")
    n_head, rows_head = pieces.shape[0], pieces.shape[1]
    me_head = lax.axis_index("head")
    n_dp = lax.axis_size("dp")
    chips = n_dp // 2
    me_dp = lax.axis_index("dp")
    core, chip = me_dp % 2, me_dp // 2
    assert rows_head % rows_mem == 0
    sections = []
    for which in (1 - core, core):
        for s in range(chips):
            block = ((chip + s) % chips) * 2 + which
            first = block * rows_mem
            source = (me_head - first // rows_head) % n_head
            offset = first % rows_head
            picked = pieces[0]
            for shift in range(1, n_head):
                picked = jnp.where(source == shift, pieces[shift], picked)
            picked = lax.dynamic_slice_in_dim(picked, offset, rows_mem, axis=0)
            sections.append(picked.reshape(rows_mem * step_count, -1))
    flat_rows = jnp.concatenate(sections, axis=0)
    outs = projection(flat_rows, w_qk, w_vz, w_ba, 2 * chips)
    pair = [(i, i ^ 1) for i in range(n_dp)]
    part = [keep + lax.ppermute(send, "dp", pair) for send, keep in zip(outs[:chips], outs[chips:])]
    width_ba = w_ba.shape[1]
    split = width_qk + (-(-width_ba // 128) * 128)
    bounds = [(0, split), (split, split + width_vz)]
    summed = [part[0][:, lo:hi] for lo, hi in bounds]
    for s in range(1, chips):
        perm = [(i, ((i // 2 + s) % chips) * 2 + i % 2) for i in range(n_dp)]
        summed = [acc + lax.ppermute(part[s][:, lo:hi], "dp", perm) for acc, (lo, hi) in zip(summed, bounds)]
    summed_first, summed_vz = summed
    summed_v = summed_vz[:, : width_vz // 2]
    summed_z = summed_vz[:, width_vz // 2 :]
    summed_qk = summed_first[:, :width_qk]
    summed_ba = summed_first[:, width_qk : width_qk + width_ba]
    qk_proj = summed_qk.astype(jnp.bfloat16).reshape(rows_mem, step_count, width_qk)
    ba_proj = summed_ba.astype(jnp.bfloat16).reshape(rows_mem, step_count, -1)
    values_now = summed_v.astype(jnp.bfloat16).reshape(rows_mem, step_count, heads * DV)
    gate_z = summed_z.astype(jnp.bfloat16).astype(jnp.float32).reshape(rows_mem, step_count, heads, DV)

    qk_conv = conv_steps(conv_state_qk, qk_proj, conv_qk).reshape(rows_mem, step_count, -1, 2, DK)
    v_conv = conv_steps(conv_state_v, values_now, conv_v)
    queries = normalize(qk_conv[:, :, :, 0, :]) * DK ** (-0.5)
    key_vec = normalize(qk_conv[:, :, :, 1, :])
    key_heads = queries.shape[2]
    assert key_heads * head_ratio == heads
    qt = queries.transpose(0, 3, 1, 2).reshape(rows_mem, DK, step_count * key_heads)
    kt = key_vec.transpose(0, 3, 1, 2).reshape(rows_mem, DK, step_count * key_heads)

    split_ba = ba_proj.reshape(rows_mem, step_count, heads, 2).astype(jnp.float32)
    beta_gate = jax.nn.sigmoid(split_ba[..., 0])
    log_decay = -jnp.exp(a_log)[None, None, :] * jax.nn.softplus(split_ba[..., 1] + dt_bias[None, None, :])
    gates = jnp.concatenate(
        [beta_gate.reshape(rows_mem, -1), jnp.exp(log_decay).reshape(rows_mem, -1)], axis=1
    )

    new_state, readout = recurrence(gates, qt, kt, v_conv, memory_state)

    scale = lax.rsqrt(jnp.mean(readout * readout, axis=-1, keepdims=True) + 1e-06)
    normed = readout * scale * norm_gain[None, None, None, :] * jax.nn.silu(gate_z)
    normed = normed.astype(jnp.bfloat16)

    all_normed = gather_rows(normed, "dp")
    partials = jnp.einsum(
        "rthd,hde->rte",
        all_normed,
        w_out.reshape(heads, DV, -1),
        preferred_element_type=jnp.float32,
    ).reshape(-1, w_out.shape[1])
    layer_out = scatter_sum_rows(partials, "head")
    layer_out = layer_out.astype(jnp.bfloat16).reshape(-1, step_count, w_out.shape[1])
    return (layer_out, new_state)


def solution(mesh):
    in_specs = (
        P(("groups", "head"), None, "dp"),
        P("dp", "head"),
        P("dp", "head"),
        P("dp", "head"),
        P(None, "head"),
        P(None, "head"),
        P("head"),
        P("head"),
        P(),
        P("head", "dp"),
        P(("groups", "dp"), None, "head"),
        P(("groups", "dp"), None, "head"),
        P(("groups", "dp"), "head", None, None),
    )
    out_specs = (P(("groups", "head"), None, "dp"), P(("groups", "dp"), "head", None, None))
    return jax.shard_map(shards, mesh=mesh, in_specs=in_specs, out_specs=out_specs, check_vma=False)
```
